128 devices in a mesh: req: 64 (over z, x, y), mlp: 2 (over core).
Axes of the slice: x: 4, y: 4, z: 4, core: 2. Of those that a mesh axis runs over, the one named last changes fastest.
Arguments:
- resid: bfloat16 [2048, 2048], P('req'), may hold values from -50 to 50
- q_in: bfloat16 [2048, 2048], P('req', 'mlp'), may hold values from -36 to 36
- kv_in: bfloat16 [2048, 2, 512], P('req', None, 'mlp'), may hold values from -36 to 36
- parents: int32 [128, 16], P('req'), may hold values from -1 to 14, as said below
- counts: int32 [128], P('req'), may hold values from 8 to 16, as said below
- accept_leaf: int32 [128], P('req'), may hold values from 0 to 15, as said below
- cache: bfloat16 [4096, 2, 128, 512], P('req', None, None, 'mlp'), may hold values from -6 to 6
- held_table: int32 [128, 48], P('req'), may hold values from 0 to 63, as said below
- held_len: int32 [128], P('req'), may hold values from 1 to 6144, as said below
- prev_owner: int32 [64], P('req'), may hold values from 0 to 63, as said below
- w_out: bfloat16 [2048, 2048], P('mlp'), may hold values from -0.125 to 0.125
- gain_mid: bfloat16 [2048], replicated, may hold values from 0.099609375 to 1.8984375
- w_in: bfloat16 [2, 8192, 2048], P(None, ('req', 'mlp')), may hold values from -0.125 to 0.125
- w_down: bfloat16 [8192, 2048], P(('req', 'mlp')), may hold values from -0.0625 to 0.0625
- gain_next: bfloat16 [2048], replicated, may hold values from 0.099609375 to 1.8984375
- w_next: bfloat16 [2048, 3072], P(None, 'mlp'), may hold values from -0.125 to 0.125
Outputs:
- hidden_out: bfloat16 [2048, 2048], P('req')
- next_qkv: bfloat16 [2048, 3072], P('req', 'mlp')
- accepted_kv: bfloat16 [2048, 2, 512], P('req', None, 'mlp')
The draws below stay inside these ranges and needn't reach their ends.
Inputs may be any that keep to these rules, and one draw needn't show every extreme that they name: parents[r, 0] is -1; for i of 1 or more parents[r, i] lies in 0 to i - 1. Draft tokens 0 to counts[r] - 1 of request r are live; some request has 16. `accept_leaf`: a live draft token of the request. `held_len`: entry 2 d holds the length of request 2 d, entry 2 d + 1 that of request 2 e + 1 where prev_owner[e] = d; some entry is 6144; the pages used by the two caches of one index of req are distinct. `held_table`: rows 2 d and 2 d + 1 belong to index d of req, as in held_len. `prev_owner`: one cycle through all indices of req, so never d itself.
All inputs are finite; a program needn't handle non-finite values.
Results may differ from the reference program's by a relative error of at most 0.014.
Values may be sent and summed in bfloat16 or wider, within the bound.
No kernel may reach another device: no remote copies, remote signals or barrier semaphores. Data moves between devices by JAX's collectives and lax.ppermute only.
A program may use at most 128 MiB of HBM per device.

```python
import jax
import jax.numpy as jnp
from jax import lax

D = 2048
HEADS = 32
KV_HEADS = 8
HEAD_DIM = 64
FF = 8192
DRAFT = 16
PAGE = 128
MAXLEN = 6144
POOL = 64
GROUP = 4
QKV_WIDTH = 3072
MAXPAGES = 48
OWNERS = 64
REQS = 128
TOKENS = 2048


def draw_q_in(key, part):
    shape = (REQS, DRAFT, KV_HEADS, HEADS // KV_HEADS, HEAD_DIM)
    base = jnp.clip(jax.random.normal(jax.random.fold_in(key, 1), shape, jnp.float32), -6.0, 6.0)
    return base.reshape(TOKENS, HEADS * HEAD_DIM).astype(jnp.bfloat16)


def draw_kv_in(key, part):
    shape = (REQS, DRAFT, 2, KV_HEADS, HEAD_DIM)
    base = jnp.clip(jax.random.normal(jax.random.fold_in(key, 2), shape, jnp.float32), -6.0, 6.0)
    return base.reshape(TOKENS, 2, KV_HEADS * HEAD_DIM).astype(jnp.bfloat16)


def draw_resid(key, part):
    row_scale = jnp.exp(jax.random.uniform(jax.random.fold_in(key, 31), (TOKENS, 1), jnp.float32, -1.2, 1.2))
    col_scale = jnp.exp(jax.random.uniform(jax.random.fold_in(key, 32), (1, D), jnp.float32, -1.2, 1.2))
    base = jnp.clip(jax.random.normal(jax.random.fold_in(key, 33), (TOKENS, D), jnp.float32), -4.0, 4.0)
    return (base * row_scale * col_scale).astype(jnp.bfloat16)


def draw_parents(key, part):
    nodes = jnp.arange(DRAFT, dtype=jnp.int32)
    picks = jax.random.randint(jax.random.fold_in(key, 3), (REQS, DRAFT), 0, 1 << 20)
    chosen = picks % jnp.maximum(nodes, 1)[None, :]
    return jnp.where(nodes[None, :] == 0, -1, chosen).astype(jnp.int32)


def draft_plan(key):
    requests = jnp.arange(REQS, dtype=jnp.int32)
    sizes = jax.random.randint(jax.random.fold_in(key, 5), (REQS,), DRAFT // 2, DRAFT + 1)
    widest = jax.random.randint(jax.random.fold_in(key, 6), (), 0, REQS)
    lowest_leaf = (widest + 1) % REQS
    fewest = (widest + 2) % REQS
    sizes = jnp.where(requests == widest, DRAFT, sizes)
    sizes = jnp.where(requests == fewest, DRAFT // 2, sizes)
    picks = jax.random.randint(jax.random.fold_in(key, 7), (REQS,), 0, 1 << 20)
    leaves = picks % sizes
    leaves = jnp.where(requests == widest, DRAFT - 1, leaves)
    leaves = jnp.where(requests == lowest_leaf, 0, leaves)
    return (sizes.astype(jnp.int32), leaves.astype(jnp.int32))


def draw_counts(key, part):
    return draft_plan(key)[0]


def draw_accept_leaf(key, part):
    return draft_plan(key)[1]


def shuffled_pages(key):
    return jax.random.permutation(key, POOL)


def pool_plan(key):
    expo = jax.random.randint(jax.random.fold_in(key, 11), (OWNERS, 2), 2, MAXLEN.bit_length())
    picks = jax.random.randint(jax.random.fold_in(key, 12), (OWNERS, 2), 0, 1 << 24)
    lengths = jnp.minimum(1 + picks % jnp.left_shift(jnp.int32(1), expo), MAXLEN)
    widest = jax.random.randint(jax.random.fold_in(key, 13), (), 0, OWNERS)
    wide_slot = jax.random.randint(jax.random.fold_in(key, 14), (), 0, 2)
    owners_row = jnp.arange(OWNERS, dtype=jnp.int32)[:, None]
    slot_col = jnp.arange(2, dtype=jnp.int32)[None, :]
    lengths = jnp.where((owners_row == widest) & (slot_col == wide_slot), MAXLEN, lengths)
    first = lengths[:, 0]
    first = jnp.where((jnp.arange(OWNERS, dtype=jnp.int32) == widest) & (wide_slot == 1), jnp.minimum(first, POOL * PAGE - MAXLEN), first)
    first_pages = (first + PAGE - 1) // PAGE
    second = jnp.minimum(lengths[:, 1], POOL * PAGE - first_pages * PAGE)
    orders = jax.vmap(shuffled_pages)(jax.random.split(jax.random.fold_in(key, 15), OWNERS)).astype(jnp.int32)
    slots = jnp.arange(MAXPAGES, dtype=jnp.int32)
    table_first = orders[:, slots % POOL]
    table_second = jnp.take_along_axis(orders, (first_pages[:, None] + slots[None, :]) % POOL, axis=1)
    tables = jnp.stack([table_first, table_second], axis=1).reshape(OWNERS * 2, MAXPAGES)
    held = jnp.stack([first, second], axis=1).reshape(OWNERS * 2)
    return (tables.astype(jnp.int32), held.astype(jnp.int32))


def draw_held_table(key, part):
    return pool_plan(key)[0]


def draw_held_len(key, part):
    return pool_plan(key)[1]


def draw_prev_owner(key, part):
    half_way = OWNERS // 2
    values = jnp.arange(OWNERS, dtype=jnp.int32)
    shuffled = jax.random.permutation(jax.random.fold_in(key, 21), OWNERS).astype(jnp.int32)
    shuffled_place = jnp.argsort(shuffled).astype(jnp.int32)
    fixed_rank = jnp.where(values == 0, 0, jnp.where(values == 1, 1, jnp.where(values == 1 + half_way, 2, jnp.where(values == half_way, 3, -1))))
    score = jnp.where(fixed_rank >= 0, fixed_rank, 4 + shuffled_place)
    order = jnp.argsort(score).astype(jnp.int32)
    offset = jax.random.randint(jax.random.fold_in(key, 22), (), 0, OWNERS)
    order = ((order + offset) % OWNERS).astype(jnp.int32)
    place = jnp.argsort(order)
    return order[(place + 1) % OWNERS].astype(jnp.int32)


def block_levels(key, shape, shards, smallest, largest):
    factor_of, own = 1.0, jax.random.fold_in(key, 6)
    for position, blocks in shards:
        heights = jnp.exp(jax.random.uniform(jax.random.fold_in(own, position), (blocks,), jnp.float32, smallest / len(shards), largest / len(shards)))
        factor_of = factor_of * jnp.repeat(heights, shape[position] // blocks).reshape([-1 if axis == position else 1 for axis in range(len(shape))])
    return factor_of


def centred(stream_key, shape, spread, bound, pieces=(), kind=jnp.bfloat16):
    entries = jax.random.normal(stream_key, shape, jnp.float32) * spread
    if len(pieces) > 0:
        entries = block_levels(stream_key, shape, pieces, -0.22, 0.18) * entries
    return jnp.clip(entries, min=-bound, max=bound).astype(kind)


def setup_inputs(seed: int = 0) -> dict:
    streams_of = jax.random.split(jax.random.key(seed), 17)
    return {
        "resid": draw_resid(jax.random.fold_in(streams_of[16], 71), 0),
        "q_in": draw_q_in(jax.random.fold_in(streams_of[16], 71), 0),
        "kv_in": draw_kv_in(jax.random.fold_in(streams_of[16], 71), 0),
        "parents": draw_parents(jax.random.fold_in(streams_of[16], 71), 0),
        "counts": draw_counts(jax.random.fold_in(streams_of[16], 71), 0),
        "accept_leaf": draw_accept_leaf(jax.random.fold_in(streams_of[16], 71), 0),
        "cache": centred(streams_of[6], (OWNERS * POOL, 2, PAGE, KV_HEADS * HEAD_DIM), 1.0, 6.0, ((0, 64), (3, 2))),
        "held_table": draw_held_table(jax.random.fold_in(streams_of[16], 71), 0),
        "held_len": draw_held_len(jax.random.fold_in(streams_of[16], 71), 0),
        "prev_owner": draw_prev_owner(jax.random.fold_in(streams_of[16], 71), 0),
        "w_out": centred(streams_of[10], (HEADS * HEAD_DIM, D), (HEADS * HEAD_DIM) ** -0.5, 0.125, ((0, 2),)),
        "gain_mid": jnp.clip(1.0 + 0.18 * jax.random.normal(streams_of[11], (D,), jnp.float32), 0.099609375, 1.8984375).astype(jnp.bfloat16),
        "w_in": centred(streams_of[12], (2, FF, D), D ** -0.5, 0.125, ((1, 128),)),
        "w_down": centred(streams_of[13], (FF, D), FF ** -0.5, 0.0625, ((0, 128),)),
        "gain_next": jnp.clip(1.0 + 0.18 * jax.random.normal(streams_of[14], (D,), jnp.float32), 0.099609375, 1.8984375).astype(jnp.bfloat16),
        "w_next": centred(streams_of[15], (D, QKV_WIDTH), D ** -0.5, 0.125, ((1, 2),)),
    }


norm_eps = 1e-05
masked_score = -1e+30

def ancestors(parents):
    count_nodes = parents.shape[-1]
    nodes = jnp.arange(count_nodes, dtype=jnp.int32)
    reach = (parents[..., :, None] == nodes).astype(jnp.float32) + jnp.eye(count_nodes, dtype=jnp.float32)
    for step in range(count_nodes.bit_length()):
        reach = jnp.minimum(jnp.einsum('sij,sjk->sik', reach, reach, precision=lax.Precision.HIGHEST), 1.0)
    return reach

def rms_scale(rows, gain):
    values = rows.astype(jnp.float32)
    factor = lax.rsqrt(lax.optimization_barrier(jnp.mean(values * values, axis=-1, keepdims=True)) + norm_eps)
    return (values * factor * gain.astype(jnp.float32)).astype(jnp.bfloat16)

def swiglu_rows(rows, w_in, w_down):
    dims = (((1,), (1,)), ((), ()))
    gate = lax.dot_general(rows, w_in[0], dims, preferred_element_type=jnp.float32)
    up_part = lax.dot_general(rows, w_in[1], dims, preferred_element_type=jnp.float32)
    hidden = (jax.nn.silu(gate) * up_part).astype(jnp.bfloat16)
    return jnp.dot(hidden, w_down, preferred_element_type=jnp.float32)

def compact_path(reach, leaves, rows):
    count_nodes = reach.shape[-1]
    nodes = jnp.arange(count_nodes, dtype=jnp.int32)
    leaf_hot = (nodes[None, :] == leaves[:, None]).astype(jnp.float32)
    path = jnp.einsum('si,sij->sj', leaf_hot, reach, precision=lax.Precision.HIGHEST)
    ranks = jnp.cumsum(path, axis=1) - path
    places = nodes.astype(jnp.float32)
    select = path[:, None, :] * (ranks[:, None, :] == places[None, :, None]).astype(jnp.float32)
    return jnp.einsum('spj,sjw->spw', select.astype(jnp.bfloat16), rows, preferred_element_type=jnp.float32).astype(jnp.bfloat16)

def request_attention(request, q_in, kv_in, reach, counts, cache, held_table, held_len, prev_owner):
    owner_dev = request // 2
    second = request % 2
    holder = jnp.where(second == 0, owner_dev, prev_owner[owner_dev]).astype(jnp.int32)
    row_id = (holder * 2 + second).astype(jnp.int32)
    page_ids = held_table[row_id] + holder * POOL
    held = cache[page_ids]
    key_rows = held[:, 0].reshape(MAXPAGES * PAGE, KV_HEADS, HEAD_DIM).astype(jnp.float32)
    value_rows = held[:, 1].reshape(MAXPAGES * PAGE, KV_HEADS, HEAD_DIM).astype(jnp.float32)
    first_row = (request * DRAFT).astype(jnp.int32)
    queries = lax.dynamic_slice_in_dim(q_in, first_row, DRAFT, 0).astype(jnp.float32).reshape(DRAFT, KV_HEADS, GROUP, HEAD_DIM)
    own_rows = lax.dynamic_slice_in_dim(kv_in, first_row, DRAFT, 0).astype(jnp.float32)
    draft_keys = own_rows[:, 0].reshape(DRAFT, KV_HEADS, HEAD_DIM)
    draft_values = own_rows[:, 1].reshape(DRAFT, KV_HEADS, HEAD_DIM)
    tree = lax.dynamic_index_in_dim(reach, request, 0, keepdims=False)
    count = lax.dynamic_index_in_dim(counts, request, 0, keepdims=False)
    allowed = (tree > 0.5) & (jnp.arange(DRAFT, dtype=jnp.int32)[None, :] < count)
    cached = jnp.arange(MAXPAGES * PAGE, dtype=jnp.int32) < held_len[row_id]
    scale = HEAD_DIM ** (-0.5)
    cache_scores = jnp.einsum('qghe,kge->ghqk', queries, key_rows) * scale
    cache_scores = jnp.where(cached, cache_scores, masked_score)
    tree_scores = jnp.einsum('qghe,kge->ghqk', queries, draft_keys) * scale
    tree_scores = jnp.where(allowed, tree_scores, masked_score)
    highest = jnp.maximum(lax.optimization_barrier(jnp.max(cache_scores, axis=-1)), lax.optimization_barrier(jnp.max(tree_scores, axis=-1)))
    cache_weights = jnp.where(cached, jnp.exp(cache_scores - highest[..., None]), 0.0)
    tree_weights = jnp.where(allowed, jnp.exp(tree_scores - highest[..., None]), 0.0)
    total = lax.optimization_barrier(jnp.sum(cache_weights, axis=-1)) + lax.optimization_barrier(jnp.sum(tree_weights, axis=-1))
    summed = jnp.einsum('ghqk,kge->ghqe', cache_weights, value_rows, precision=lax.Precision.HIGHEST)
    summed = summed + jnp.einsum('ghqk,kge->ghqe', tree_weights, draft_values, precision=lax.Precision.HIGHEST)
    result = summed / total[..., None]
    return jnp.transpose(result, (2, 0, 1, 3)).reshape(DRAFT, HEADS * HEAD_DIM).astype(jnp.bfloat16)

def reference(resid, q_in, kv_in, parents, counts, accept_leaf, cache, held_table, held_len, prev_owner, w_out, gain_mid, w_in, w_down, gain_next, w_next):
    reach = ancestors(parents)

    def one_request(request):
        return request_attention(request, q_in, kv_in, reach, counts, cache, held_table, held_len, prev_owner)
    attended = lax.map(one_request, jnp.arange(REQS, dtype=jnp.int32)).reshape(TOKENS, HEADS * HEAD_DIM)
    mixed = (resid.astype(jnp.float32) + jnp.dot(attended, w_out, preferred_element_type=jnp.float32)).astype(jnp.bfloat16)
    normed = rms_scale(mixed, gain_mid)
    hidden_out = (mixed.astype(jnp.float32) + swiglu_rows(normed, w_in, w_down)).astype(jnp.bfloat16)
    next_normed = rms_scale(hidden_out, gain_next)
    next_qkv = jnp.dot(next_normed, w_next, preferred_element_type=jnp.float32).astype(jnp.bfloat16)
    accepted = compact_path(reach, accept_leaf, kv_in.reshape(REQS, DRAFT, 2 * KV_HEADS * HEAD_DIM))
    accepted_kv = accepted.reshape(TOKENS, 2, KV_HEADS * HEAD_DIM)
    return (hidden_out, next_qkv, accepted_kv)
```

```python
import math

import jax
import jax.numpy as jnp
from jax import lax
from jax.sharding import Mesh, PartitionSpec as P

HEAD_DIM = 64
GROUP = 4


TAG = 128
REQ = ("a", "b")
GROUP_SPLIT = 4

norm_eps = 1e-05
masked_score = -1e30


def split_hi_lo(values):
    high = values.astype(jnp.bfloat16)
    low = (values - high.astype(jnp.float32)).astype(jnp.bfloat16)
    return jnp.concatenate([high, low], axis=1)


def ancestors(parents):
    count_nodes = parents.shape[-1]
    nodes = jnp.arange(count_nodes, dtype=jnp.int32)
    reach = (parents[..., :, None] == nodes).astype(jnp.float32) + jnp.eye(
        count_nodes, dtype=jnp.float32
    )
    for step in range(count_nodes.bit_length()):
        reach = jnp.minimum(
            jnp.einsum("sij,sjk->sik", reach, reach, precision=lax.Precision.HIGHEST), 1.0
        )
    return reach


def rms_scale(rows, gain):
    values = rows.astype(jnp.float32)
    factor = lax.rsqrt(jnp.mean(values * values, axis=-1, keepdims=True) + norm_eps)
    return (values * factor * gain.astype(jnp.float32)).astype(jnp.bfloat16)


def swiglu_rows(rows, w_in, w_down):
    dims = (((1,), (1,)), ((), ()))
    gate = lax.dot_general(rows, w_in[0], dims, preferred_element_type=jnp.float32)
    up_part = lax.dot_general(rows, w_in[1], dims, preferred_element_type=jnp.float32)
    hidden = (jax.nn.silu(gate) * up_part).astype(jnp.bfloat16)
    return jnp.dot(hidden, w_down, preferred_element_type=jnp.float32)


def compact_path(reach, leaves, rows):
    count_nodes = reach.shape[-1]
    nodes = jnp.arange(count_nodes, dtype=jnp.int32)
    leaf_hot = (nodes[None, :] == leaves[:, None]).astype(jnp.float32)
    path = jnp.einsum("si,sij->sj", leaf_hot, reach, precision=lax.Precision.HIGHEST)
    ranks = jnp.cumsum(path, axis=1) - path
    places = nodes.astype(jnp.float32)
    select = path[:, None, :] * (ranks[:, None, :] == places[None, :, None]).astype(jnp.float32)
    return jnp.einsum(
        "spj,sjw->spw", select.astype(jnp.bfloat16), rows, preferred_element_type=jnp.float32
    ).astype(jnp.bfloat16)


def per_device(
    resid,
    q_in,
    kv_in,
    parents,
    counts,
    accept_leaf,
    cache,
    held_table,
    held_len,
    prev_owner,
    w_out,
    gain_mid,
    w_in,
    w_down,
    gain_next,
    w_next,
):
    tree_len = parents.shape[1]
    kv_width = kv_in.shape[2]
    kv_local = kv_width // HEAD_DIM
    scale = HEAD_DIM ** (-0.5)
    queries = q_in.reshape(2, tree_len, kv_local, GROUP, HEAD_DIM)
    device_id = lax.axis_index(REQ)
    q_width = q_in.shape[1]
    dest_col = jnp.broadcast_to(prev_owner[0].astype(q_in.dtype), (tree_len, TAG))
    q_packet = jnp.concatenate([q_in[tree_len:], dest_col], axis=1)
    every_query = lax.all_gather(q_packet, REQ, axis=0, tiled=False)
    dests = every_query[:, 0, q_width].astype(jnp.int32)
    senders = jnp.arange(dests.shape[0], dtype=jnp.int32)
    sender = jnp.sum(jnp.where(dests == device_id, senders, 0))
    foreign = lax.dynamic_index_in_dim(every_query, sender, 0, keepdims=False)[:, :q_width]
    held_queries = jnp.stack([q_in[:tree_len], foreign]).reshape(
        2, tree_len, kv_local, GROUP, HEAD_DIM
    )
    page_len = cache.shape[2]
    block_pages = math.gcd(held_table.shape[1], max(1, 1024 // page_len))
    block_keys = block_pages * page_len
    num_blocks = held_table.shape[1] // block_pages
    positions = jnp.arange(block_keys, dtype=jnp.int32)

    def attend_block(block, state):
        running, total, accum = state
        page_ids = lax.dynamic_slice_in_dim(held_table, block * block_pages, block_pages, 1)
        gathered = cache[page_ids]
        key_rows = gathered[:, :, 0].reshape(2, block_keys, kv_local, HEAD_DIM)
        value_rows = gathered[:, :, 1].reshape(2, block_keys, kv_local, HEAD_DIM)
        scores = (
            jnp.einsum(
                "sqghe,skge->sghqk", held_queries, key_rows, preferred_element_type=jnp.float32
            )
            * scale
        )
        visible = (block * block_keys + positions)[None, :] < held_len[:, None]
        visible = visible[:, None, None, None, :]
        scores = jnp.where(visible, scores, masked_score)
        newest = jnp.maximum(running, jnp.max(scores, axis=-1))
        weights = jnp.where(visible, jnp.exp(scores - newest[..., None]), 0.0)
        factor = jnp.exp(running - newest)
        total = total * factor + jnp.sum(weights, axis=-1)
        update = jnp.einsum(
            "sghqk,skge->sghqe",
            weights,
            value_rows.astype(jnp.float32),
            precision=lax.Precision.HIGHEST,
        )
        accum = accum * factor[..., None] + update
        return (newest, total, accum)

    stat_shape = (2, kv_local, GROUP, tree_len)
    start_state = (
        jnp.full(stat_shape, masked_score, jnp.float32),
        jnp.zeros(stat_shape, jnp.float32),
        jnp.zeros(stat_shape + (HEAD_DIM,), jnp.float32),
    )
    own_w = jnp.stack([w_in[0], w_in[1], w_down])
    all_w = lax.all_gather(own_w, "a", axis=0, tiled=False)
    running, total, accum = lax.fori_loop(0, num_blocks, attend_block, start_state)
    all_w, running, total, accum = lax.optimization_barrier((all_w, running, total, accum))
    cache_out = accum / total[..., None]
    sent_out = jnp.transpose(cache_out[1], (2, 0, 1, 3)).reshape(
        tree_len, kv_local * GROUP * HEAD_DIM
    )
    sent_max = jnp.transpose(running[1], (2, 0, 1)).reshape(tree_len, kv_local * GROUP)
    sent_total = jnp.transpose(total[1], (2, 0, 1)).reshape(tree_len, kv_local * GROUP)
    stats = jnp.concatenate(
        [split_hi_lo(sent_max), split_hi_lo(sent_total)], axis=1
    )
    pad = jnp.zeros((tree_len, TAG - stats.shape[1]), jnp.bfloat16)
    r_packet = jnp.concatenate([sent_out.astype(jnp.bfloat16), stats, pad], axis=1)
    back = lax.all_gather(r_packet, REQ, axis=0, tiled=False)
    got = lax.dynamic_index_in_dim(back, prev_owner[0], 0, keepdims=False).astype(jnp.float32)
    heads = kv_local * GROUP
    o_w = heads * HEAD_DIM
    recv_out = got[:, :o_w].reshape(tree_len, kv_local, GROUP, HEAD_DIM)
    recv_max = (got[:, o_w : o_w + heads] + got[:, o_w + heads : o_w + 2 * heads]).reshape(
        tree_len, kv_local, GROUP
    )
    t0 = o_w + 2 * heads
    recv_total = (got[:, t0 : t0 + heads] + got[:, t0 + heads : t0 + 2 * heads]).reshape(
        tree_len, kv_local, GROUP
    )
    part_out = jnp.stack([cache_out[0], jnp.transpose(recv_out, (1, 2, 0, 3))])
    part_max = jnp.stack([running[0], jnp.transpose(recv_max, (1, 2, 0))])
    part_total = jnp.stack([total[0], jnp.transpose(recv_total, (1, 2, 0))])
    reach = ancestors(parents)
    live = jnp.arange(tree_len, dtype=jnp.int32)[None, :] < counts[:, None]
    allowed = ((reach > 0.5) & live[:, None, :])[:, None, None, :, :]
    draft_keys = kv_in[:, 0].reshape(2, tree_len, kv_local, HEAD_DIM)
    draft_values = kv_in[:, 1].reshape(2, tree_len, kv_local, HEAD_DIM)
    tree_scores = (
        jnp.einsum("sqghe,skge->sghqk", queries, draft_keys, preferred_element_type=jnp.float32)
        * scale
    )
    tree_scores = jnp.where(allowed, tree_scores, masked_score)
    tree_max = jnp.max(tree_scores, axis=-1)
    tree_weights = jnp.where(allowed, jnp.exp(tree_scores - tree_max[..., None]), 0.0)
    tree_total = jnp.sum(tree_weights, axis=-1)
    tree_accum = jnp.einsum(
        "sghqk,skge->sghqe",
        tree_weights,
        draft_values.astype(jnp.float32),
        precision=lax.Precision.HIGHEST,
    )
    overall = jnp.maximum(part_max, tree_max)
    cache_weight = part_total * jnp.exp(part_max - overall)
    tree_weight = jnp.exp(tree_max - overall)
    merged = (part_out * cache_weight[..., None] + tree_accum * tree_weight[..., None]) / (
        cache_weight + tree_total * tree_weight
    )[..., None]
    attended = (
        jnp.transpose(merged, (0, 3, 1, 2, 4))
        .reshape(2 * tree_len, kv_local * GROUP * HEAD_DIM)
        .astype(jnp.bfloat16)
    )
    partial_proj = jnp.dot(attended, w_out, preferred_element_type=jnp.float32)
    projected = lax.psum(partial_proj, "mlp")
    mixed = (resid.astype(jnp.float32) + projected).astype(jnp.bfloat16)
    normed = rms_scale(mixed, gain_mid)
    column = lax.axis_index("mlp")
    half_count = normed.shape[0] // lax.axis_size("mlp")
    group_rows = lax.all_gather(normed, "b", axis=0, tiled=True)
    dims = (((1,), (2,)), ((), ()))
    gate = lax.dot_general(group_rows, all_w[:, 0], dims, preferred_element_type=jnp.float32)
    up_part = lax.dot_general(group_rows, all_w[:, 1], dims, preferred_element_type=jnp.float32)
    hidden = (jax.nn.silu(gate) * up_part).astype(jnp.bfloat16)
    down_dims = (((1, 2), (0, 1)), ((), ()))
    partial = lax.dot_general(
        hidden, all_w[:, 2], down_dims, preferred_element_type=jnp.float32
    )
    mlp_half = lax.psum_scatter(partial, ("b", "mlp"), scatter_dimension=0, tiled=True)
    base_half = lax.dynamic_slice_in_dim(mixed, column * half_count, half_count, 0)
    out_half = (base_half.astype(jnp.float32) + mlp_half).astype(jnp.bfloat16)
    hidden_out = lax.all_gather(out_half, "mlp", axis=0, tiled=True)
    next_normed = rms_scale(hidden_out, gain_next)
    next_qkv = jnp.dot(next_normed, w_next, preferred_element_type=jnp.float32).astype(jnp.bfloat16)
    accepted = compact_path(reach, accept_leaf, kv_in.reshape(2, tree_len, 2 * kv_width))
    accepted_kv = accepted.reshape(2 * tree_len, 2, kv_width)
    return (hidden_out, next_qkv, accepted_kv)


def solution(mesh):
    devices = mesh.devices
    owners = devices.shape[0]
    sub_mesh = Mesh(
        devices.reshape(owners // GROUP_SPLIT, GROUP_SPLIT, devices.shape[1]), ("a", "b", "mlp")
    )
    R = REQ
    placed = (
        P(R, None),
        P(R, "mlp"),
        P(R, None, "mlp"),
        P(R, None),
        P(R),
        P(R),
        P(R, None, None, "mlp"),
        P(R, None),
        P(R),
        P(R),
        P("mlp", None),
        P(),
        P(None, R + ("mlp",), None),
        P(R + ("mlp",), None),
        P(),
        P(None, "mlp"),
    )
    return jax.shard_map(
        per_device,
        mesh=sub_mesh,
        in_specs=placed,
        out_specs=(P(R, None), P(R, "mlp"), P(R, None, "mlp")),
        check_vma=False,
    )
```

```python
import math

import jax
import jax.numpy as jnp
from jax import lax
from jax.sharding import Mesh, PartitionSpec as P

HEAD_DIM = 64
GROUP = 4


TAG = 128
REQ = ("z", "x", "y")

norm_eps = 1e-05
masked_score = -1e30


def split_hi_lo(values):
    high = values.astype(jnp.bfloat16)
    low = (values - high.astype(jnp.float32)).astype(jnp.bfloat16)
    return jnp.concatenate([high, low], axis=1)


def ring_gather(parts, axis, size):
    pieces = [parts]
    for shift in range(1, size):
        perm = [(i, (i + shift) % size) for i in range(size)]
        pieces.append(lax.ppermute(parts, axis, perm))
    return jnp.concatenate(pieces, axis=0)


def gather_weights(own_w):
    line = ring_gather(own_w[None], "x", lax.axis_size("x"))
    return ring_gather(line, "z", lax.axis_size("z"))


def ancestors(parents):
    count_nodes = parents.shape[-1]
    nodes = jnp.arange(count_nodes, dtype=jnp.int32)
    reach = (parents[..., :, None] == nodes).astype(jnp.float32) + jnp.eye(
        count_nodes, dtype=jnp.float32
    )
    for step in range(count_nodes.bit_length()):
        reach = jnp.minimum(
            jnp.einsum("sij,sjk->sik", reach, reach, precision=lax.Precision.HIGHEST), 1.0
        )
    return reach


def rms_scale(rows, gain):
    values = rows.astype(jnp.float32)
    factor = lax.rsqrt(jnp.mean(values * values, axis=-1, keepdims=True) + norm_eps)
    return (values * factor * gain.astype(jnp.float32)).astype(jnp.bfloat16)


def swiglu_rows(rows, w_in, w_down):
    dims = (((1,), (1,)), ((), ()))
    gate = lax.dot_general(rows, w_in[0], dims, preferred_element_type=jnp.float32)
    up_part = lax.dot_general(rows, w_in[1], dims, preferred_element_type=jnp.float32)
    hidden = (jax.nn.silu(gate) * up_part).astype(jnp.bfloat16)
    return jnp.dot(hidden, w_down, preferred_element_type=jnp.float32)


def compact_path(reach, leaves, rows):
    count_nodes = reach.shape[-1]
    nodes = jnp.arange(count_nodes, dtype=jnp.int32)
    leaf_hot = (nodes[None, :] == leaves[:, None]).astype(jnp.float32)
    path = jnp.einsum("si,sij->sj", leaf_hot, reach, precision=lax.Precision.HIGHEST)
    ranks = jnp.cumsum(path, axis=1) - path
    places = nodes.astype(jnp.float32)
    select = path[:, None, :] * (ranks[:, None, :] == places[None, :, None]).astype(jnp.float32)
    return jnp.einsum(
        "spj,sjw->spw", select.astype(jnp.bfloat16), rows, preferred_element_type=jnp.float32
    ).astype(jnp.bfloat16)


def per_device(
    resid,
    q_in,
    kv_in,
    parents,
    counts,
    accept_leaf,
    cache,
    held_table,
    held_len,
    prev_owner,
    w_out,
    gain_mid,
    w_in,
    w_down,
    gain_next,
    w_next,
):
    tree_len = parents.shape[1]
    kv_width = kv_in.shape[2]
    kv_local = kv_width // HEAD_DIM
    scale = HEAD_DIM ** (-0.5)
    queries = q_in.reshape(2, tree_len, kv_local, GROUP, HEAD_DIM)
    device_id = lax.axis_index(REQ)
    q_width = q_in.shape[1]
    dest_col = jnp.broadcast_to(prev_owner[0].astype(q_in.dtype), (tree_len, TAG))
    q_packet = jnp.concatenate([q_in[tree_len:], dest_col], axis=1)
    every_query = lax.all_gather(q_packet, REQ, axis=0, tiled=False)
    own_w = jnp.stack([w_in[0], w_in[1], w_down])
    all_w = gather_weights(own_w)
    page_len = cache.shape[2]
    block_pages = math.gcd(held_table.shape[1], max(1, 1024 // page_len))
    block_keys = block_pages * page_len
    num_blocks = held_table.shape[1] // block_pages
    positions = jnp.arange(block_keys, dtype=jnp.int32)

    def attend(slot, slot_queries, first, last, state):
        table = held_table[slot]
        length = held_len[slot]

        def attend_block(block, state):
            running, total, accum = state
            page_ids = lax.dynamic_slice_in_dim(table, block * block_pages, block_pages, 0)
            gathered = cache[page_ids]
            key_rows = gathered[:, 0].reshape(block_keys, kv_local, HEAD_DIM)
            value_rows = gathered[:, 1].reshape(block_keys, kv_local, HEAD_DIM)
            scores = (
                jnp.einsum(
                    "qghe,kge->ghqk", slot_queries, key_rows, preferred_element_type=jnp.float32
                )
                * scale
            )
            visible = (block * block_keys + positions) < length
            scores = jnp.where(visible, scores, masked_score)
            newest = jnp.maximum(running, jnp.max(scores, axis=-1))
            weights = jnp.where(visible, jnp.exp(scores - newest[..., None]), 0.0)
            factor = jnp.exp(running - newest)
            total = total * factor + jnp.sum(weights, axis=-1)
            update = jnp.einsum(
                "ghqk,kge->ghqe",
                weights,
                value_rows.astype(jnp.float32),
                precision=lax.Precision.HIGHEST,
            )
            accum = accum * factor[..., None] + update
            return (newest, total, accum)

        return lax.fori_loop(first, last, attend_block, state)

    stat_shape = (kv_local, GROUP, tree_len)
    start_state = (
        jnp.full(stat_shape, masked_score, jnp.float32),
        jnp.zeros(stat_shape, jnp.float32),
        jnp.zeros(stat_shape + (HEAD_DIM,), jnp.float32),
    )
    own_queries = queries[0]
    split = num_blocks // 2
    own_state = attend(0, own_queries, 0, split, start_state)
    own_state, every_query = lax.optimization_barrier((own_state, every_query))
    dests = every_query[:, 0, q_width].astype(jnp.int32)
    senders = jnp.arange(dests.shape[0], dtype=jnp.int32)
    sender = jnp.sum(jnp.where(dests == device_id, senders, 0))
    foreign = lax.dynamic_index_in_dim(every_query, sender, 0, keepdims=False)[:, :q_width]
    foreign = foreign.reshape(tree_len, kv_local, GROUP, HEAD_DIM)
    f_running, f_total, f_accum = attend(1, foreign, 0, num_blocks, start_state)
    f_out = f_accum / f_total[..., None]
    sent_out = jnp.transpose(f_out, (2, 0, 1, 3)).reshape(
        tree_len, kv_local * GROUP * HEAD_DIM
    )
    sent_max = jnp.transpose(f_running, (2, 0, 1)).reshape(tree_len, kv_local * GROUP)
    sent_total = jnp.transpose(f_total, (2, 0, 1)).reshape(tree_len, kv_local * GROUP)
    stats = jnp.concatenate(
        [split_hi_lo(sent_max), split_hi_lo(sent_total)], axis=1
    )
    pad = jnp.zeros((tree_len, TAG - stats.shape[1]), jnp.bfloat16)
    r_packet = jnp.concatenate([sent_out.astype(jnp.bfloat16), stats, pad], axis=1)
    r_packet, own_state = lax.optimization_barrier((r_packet, own_state))
    back = lax.all_gather(r_packet, REQ, axis=0, tiled=False)
    running, total, accum = attend(0, own_queries, split, num_blocks, own_state)
    all_w, running, total, accum = lax.optimization_barrier((all_w, running, total, accum))
    cache_out = accum / total[..., None]
    got = lax.dynamic_index_in_dim(back, prev_owner[0], 0, keepdims=False).astype(jnp.float32)
    heads = kv_local * GROUP
    o_w = heads * HEAD_DIM
    recv_out = got[:, :o_w].reshape(tree_len, kv_local, GROUP, HEAD_DIM)
    recv_max = (got[:, o_w : o_w + heads] + got[:, o_w + heads : o_w + 2 * heads]).reshape(
        tree_len, kv_local, GROUP
    )
    t0 = o_w + 2 * heads
    recv_total = (got[:, t0 : t0 + heads] + got[:, t0 + heads : t0 + 2 * heads]).reshape(
        tree_len, kv_local, GROUP
    )
    part_out = jnp.stack([cache_out, jnp.transpose(recv_out, (1, 2, 0, 3))])
    part_max = jnp.stack([running, jnp.transpose(recv_max, (1, 2, 0))])
    part_total = jnp.stack([total, jnp.transpose(recv_total, (1, 2, 0))])
    reach = ancestors(parents)
    live = jnp.arange(tree_len, dtype=jnp.int32)[None, :] < counts[:, None]
    allowed = ((reach > 0.5) & live[:, None, :])[:, None, None, :, :]
    draft_keys = kv_in[:, 0].reshape(2, tree_len, kv_local, HEAD_DIM)
    draft_values = kv_in[:, 1].reshape(2, tree_len, kv_local, HEAD_DIM)
    tree_scores = (
        jnp.einsum("sqghe,skge->sghqk", queries, draft_keys, preferred_element_type=jnp.float32)
        * scale
    )
    tree_scores = jnp.where(allowed, tree_scores, masked_score)
    tree_max = jnp.max(tree_scores, axis=-1)
    tree_weights = jnp.where(allowed, jnp.exp(tree_scores - tree_max[..., None]), 0.0)
    tree_total = jnp.sum(tree_weights, axis=-1)
    tree_accum = jnp.einsum(
        "sghqk,skge->sghqe",
        tree_weights,
        draft_values.astype(jnp.float32),
        precision=lax.Precision.HIGHEST,
    )
    overall = jnp.maximum(part_max, tree_max)
    cache_weight = part_total * jnp.exp(part_max - overall)
    tree_weight = jnp.exp(tree_max - overall)
    merged = (part_out * cache_weight[..., None] + tree_accum * tree_weight[..., None]) / (
        cache_weight + tree_total * tree_weight
    )[..., None]
    attended = (
        jnp.transpose(merged, (0, 3, 1, 2, 4))
        .reshape(2 * tree_len, kv_local * GROUP * HEAD_DIM)
        .astype(jnp.bfloat16)
    )
    partial_proj = jnp.dot(attended, w_out, preferred_element_type=jnp.float32)
    projected = partial_proj + lax.ppermute(partial_proj, "mlp", [(0, 1), (1, 0)])
    mixed = (resid.astype(jnp.float32) + projected).astype(jnp.bfloat16)
    normed = rms_scale(mixed, gain_mid)
    column = lax.axis_index("mlp")
    half_count = normed.shape[0] // lax.axis_size("mlp")
    group_rows = lax.all_gather(normed, "y", axis=0, tiled=True)
    dims = (((1,), (2,)), ((), ()))
    gate = lax.dot_general(group_rows, all_w[:, 0], dims, preferred_element_type=jnp.float32)
    up_part = lax.dot_general(group_rows, all_w[:, 1], dims, preferred_element_type=jnp.float32)
    hidden = (jax.nn.silu(gate) * up_part).astype(jnp.bfloat16)
    down_dims = (((1, 2), (0, 1)), ((), ()))
    partial = lax.dot_general(
        hidden, all_w[:, 2], down_dims, preferred_element_type=jnp.float32
    )
    mlp_half = lax.psum_scatter(partial, ("y", "mlp"), scatter_dimension=0, tiled=True)
    base_half = lax.dynamic_slice_in_dim(mixed, column * half_count, half_count, 0)
    out_half = (base_half.astype(jnp.float32) + mlp_half).astype(jnp.bfloat16)
    hidden_out = lax.all_gather(out_half, "mlp", axis=0, tiled=True)
    next_normed = rms_scale(hidden_out, gain_next)
    next_qkv = jnp.dot(next_normed, w_next, preferred_element_type=jnp.float32).astype(jnp.bfloat16)
    accepted = compact_path(reach, accept_leaf, kv_in.reshape(2, tree_len, 2 * kv_width))
    accepted_kv = accepted.reshape(2 * tree_len, 2, kv_width)
    return (hidden_out, next_qkv, accepted_kv)


def solution(mesh):
    devices = mesh.devices
    owners = devices.shape[0]
    lines = round(owners ** (1 / 3))
    sub_mesh = Mesh(
        devices.reshape(owners // (lines * lines), lines, lines, devices.shape[1]),
        ("z", "x", "y", "mlp"),
    )
    R = REQ
    placed = (
        P(R, None),
        P(R, "mlp"),
        P(R, None, "mlp"),
        P(R, None),
        P(R),
        P(R),
        P(R, None, None, "mlp"),
        P(R, None),
        P(R),
        P(R),
        P("mlp", None),
        P(),
        P(None, R + ("mlp",), None),
        P(R + ("mlp",), None),
        P(),
        P(None, "mlp"),
    )
    return jax.shard_map(
        per_device,
        mesh=sub_mesh,
        in_specs=placed,
        out_specs=(P(R, None), P(R, "mlp"), P(R, None, "mlp")),
        check_vma=False,
    )
```

```python
import math

import jax
import jax.numpy as jnp
from jax import lax
from jax.sharding import Mesh, PartitionSpec as P

HEAD_DIM = 64
GROUP = 4


TAG = 128
REQ = ("z", "x", "y")

norm_eps = 1e-05
masked_score = -1e30


def split_hi_lo(values):
    high = values.astype(jnp.bfloat16)
    low = (values - high.astype(jnp.float32)).astype(jnp.bfloat16)
    return jnp.concatenate([high, low], axis=1)


def gather_lines(packet):
    lines = lax.all_gather(packet, "y", axis=0, tiled=False)
    lines = lax.all_gather(lines, "x", axis=0, tiled=False)
    lines = lax.all_gather(lines, "z", axis=0, tiled=False)
    return lines.reshape((-1,) + packet.shape)


def ancestors(parents):
    count_nodes = parents.shape[-1]
    nodes = jnp.arange(count_nodes, dtype=jnp.int32)
    reach = (parents[..., :, None] == nodes).astype(jnp.float32) + jnp.eye(
        count_nodes, dtype=jnp.float32
    )
    for step in range(count_nodes.bit_length()):
        reach = jnp.minimum(
            jnp.einsum("sij,sjk->sik", reach, reach, precision=lax.Precision.HIGHEST), 1.0
        )
    return reach


def rms_scale(rows, gain):
    values = rows.astype(jnp.float32)
    factor = lax.rsqrt(jnp.mean(values * values, axis=-1, keepdims=True) + norm_eps)
    return (values * factor * gain.astype(jnp.float32)).astype(jnp.bfloat16)


def swiglu_rows(rows, w_in, w_down):
    dims = (((1,), (1,)), ((), ()))
    gate = lax.dot_general(rows, w_in[0], dims, preferred_element_type=jnp.float32)
    up_part = lax.dot_general(rows, w_in[1], dims, preferred_element_type=jnp.float32)
    hidden = (jax.nn.silu(gate) * up_part).astype(jnp.bfloat16)
    return jnp.dot(hidden, w_down, preferred_element_type=jnp.float32)


def compact_path(reach, leaves, rows):
    count_nodes = reach.shape[-1]
    nodes = jnp.arange(count_nodes, dtype=jnp.int32)
    leaf_hot = (nodes[None, :] == leaves[:, None]).astype(jnp.float32)
    path = jnp.einsum("si,sij->sj", leaf_hot, reach, precision=lax.Precision.HIGHEST)
    ranks = jnp.cumsum(path, axis=1) - path
    places = nodes.astype(jnp.float32)
    select = path[:, None, :] * (ranks[:, None, :] == places[None, :, None]).astype(jnp.float32)
    return jnp.einsum(
        "spj,sjw->spw", select.astype(jnp.bfloat16), rows, preferred_element_type=jnp.float32
    ).astype(jnp.bfloat16)


def per_device(
    resid,
    q_in,
    kv_in,
    parents,
    counts,
    accept_leaf,
    cache,
    held_table,
    held_len,
    prev_owner,
    w_out,
    gain_mid,
    w_in,
    w_down,
    gain_next,
    w_next,
):
    tree_len = parents.shape[1]
    kv_width = kv_in.shape[2]
    kv_local = kv_width // HEAD_DIM
    scale = HEAD_DIM ** (-0.5)
    queries = q_in.reshape(2, tree_len, kv_local, GROUP, HEAD_DIM)
    device_id = lax.axis_index(REQ)
    q_width = q_in.shape[1]
    dest_col = jnp.broadcast_to(prev_owner[0].astype(q_in.dtype), (tree_len, TAG))
    q_packet = jnp.concatenate([q_in[tree_len:], dest_col], axis=1)
    every_query = gather_lines(q_packet)
    own_w = jnp.stack([w_in[0], w_in[1], w_down])
    all_w = lax.all_gather(own_w, ("z", "x"), axis=0, tiled=False)
    page_len = cache.shape[2]
    block_pages = math.gcd(held_table.shape[1], max(1, 1024 // page_len))
    block_keys = block_pages * page_len
    num_blocks = held_table.shape[1] // block_pages
    positions = jnp.arange(block_keys, dtype=jnp.int32)

    def attend(slot, slot_queries, first, last, state):
        table = held_table[slot]
        length = held_len[slot]

        def attend_block(block, state):
            running, total, accum = state
            page_ids = lax.dynamic_slice_in_dim(table, block * block_pages, block_pages, 0)
            gathered = cache[page_ids]
            key_rows = gathered[:, 0].reshape(block_keys, kv_local, HEAD_DIM)
            value_rows = gathered[:, 1].reshape(block_keys, kv_local, HEAD_DIM)
            scores = (
                jnp.einsum(
                    "qghe,kge->ghqk", slot_queries, key_rows, preferred_element_type=jnp.float32
                )
                * scale
            )
            visible = (block * block_keys + positions) < length
            scores = jnp.where(visible, scores, masked_score)
            newest = jnp.maximum(running, jnp.max(scores, axis=-1))
            weights = jnp.where(visible, jnp.exp(scores - newest[..., None]), 0.0)
            factor = jnp.exp(running - newest)
            total = total * factor + jnp.sum(weights, axis=-1)
            update = jnp.einsum(
                "ghqk,kge->ghqe",
                weights,
                value_rows.astype(jnp.float32),
                precision=lax.Precision.HIGHEST,
            )
            accum = accum * factor[..., None] + update
            return (newest, total, accum)

        return lax.fori_loop(first, last, attend_block, state)

    stat_shape = (kv_local, GROUP, tree_len)
    start_state = (
        jnp.full(stat_shape, masked_score, jnp.float32),
        jnp.zeros(stat_shape, jnp.float32),
        jnp.zeros(stat_shape + (HEAD_DIM,), jnp.float32),
    )
    own_queries = queries[0]
    split = num_blocks // 2
    own_state = attend(0, own_queries, 0, split, start_state)
    own_state, every_query = lax.optimization_barrier((own_state, every_query))
    dests = every_query[:, 0, q_width].astype(jnp.int32)
    senders = jnp.arange(dests.shape[0], dtype=jnp.int32)
    sender = jnp.sum(jnp.where(dests == device_id, senders, 0))
    foreign = lax.dynamic_index_in_dim(every_query, sender, 0, keepdims=False)[:, :q_width]
    foreign = foreign.reshape(tree_len, kv_local, GROUP, HEAD_DIM)
    f_running, f_total, f_accum = attend(1, foreign, 0, num_blocks, start_state)
    f_out = f_accum / f_total[..., None]
    sent_out = jnp.transpose(f_out, (2, 0, 1, 3)).reshape(
        tree_len, kv_local * GROUP * HEAD_DIM
    )
    sent_max = jnp.transpose(f_running, (2, 0, 1)).reshape(tree_len, kv_local * GROUP)
    sent_total = jnp.transpose(f_total, (2, 0, 1)).reshape(tree_len, kv_local * GROUP)
    stats = jnp.concatenate(
        [split_hi_lo(sent_max), split_hi_lo(sent_total)], axis=1
    )
    pad = jnp.zeros((tree_len, TAG - stats.shape[1]), jnp.bfloat16)
    r_packet = jnp.concatenate([sent_out.astype(jnp.bfloat16), stats, pad], axis=1)
    r_packet, own_state = lax.optimization_barrier((r_packet, own_state))
    back = gather_lines(r_packet)
    running, total, accum = attend(0, own_queries, split, num_blocks, own_state)
    all_w, running, total, accum = lax.optimization_barrier((all_w, running, total, accum))
    cache_out = accum / total[..., None]
    got = lax.dynamic_index_in_dim(back, prev_owner[0], 0, keepdims=False).astype(jnp.float32)
    heads = kv_local * GROUP
    o_w = heads * HEAD_DIM
    recv_out = got[:, :o_w].reshape(tree_len, kv_local, GROUP, HEAD_DIM)
    recv_max = (got[:, o_w : o_w + heads] + got[:, o_w + heads : o_w + 2 * heads]).reshape(
        tree_len, kv_local, GROUP
    )
    t0 = o_w + 2 * heads
    recv_total = (got[:, t0 : t0 + heads] + got[:, t0 + heads : t0 + 2 * heads]).reshape(
        tree_len, kv_local, GROUP
    )
    part_out = jnp.stack([cache_out, jnp.transpose(recv_out, (1, 2, 0, 3))])
    part_max = jnp.stack([running, jnp.transpose(recv_max, (1, 2, 0))])
    part_total = jnp.stack([total, jnp.transpose(recv_total, (1, 2, 0))])
    reach = ancestors(parents)
    live = jnp.arange(tree_len, dtype=jnp.int32)[None, :] < counts[:, None]
    allowed = ((reach > 0.5) & live[:, None, :])[:, None, None, :, :]
    draft_keys = kv_in[:, 0].reshape(2, tree_len, kv_local, HEAD_DIM)
    draft_values = kv_in[:, 1].reshape(2, tree_len, kv_local, HEAD_DIM)
    tree_scores = (
        jnp.einsum("sqghe,skge->sghqk", queries, draft_keys, preferred_element_type=jnp.float32)
        * scale
    )
    tree_scores = jnp.where(allowed, tree_scores, masked_score)
    tree_max = jnp.max(tree_scores, axis=-1)
    tree_weights = jnp.where(allowed, jnp.exp(tree_scores - tree_max[..., None]), 0.0)
    tree_total = jnp.sum(tree_weights, axis=-1)
    tree_accum = jnp.einsum(
        "sghqk,skge->sghqe",
        tree_weights,
        draft_values.astype(jnp.float32),
        precision=lax.Precision.HIGHEST,
    )
    overall = jnp.maximum(part_max, tree_max)
    cache_weight = part_total * jnp.exp(part_max - overall)
    tree_weight = jnp.exp(tree_max - overall)
    merged = (part_out * cache_weight[..., None] + tree_accum * tree_weight[..., None]) / (
        cache_weight + tree_total * tree_weight
    )[..., None]
    attended = (
        jnp.transpose(merged, (0, 3, 1, 2, 4))
        .reshape(2 * tree_len, kv_local * GROUP * HEAD_DIM)
        .astype(jnp.bfloat16)
    )
    partial_proj = jnp.dot(attended, w_out, preferred_element_type=jnp.float32)
    projected = partial_proj + lax.ppermute(partial_proj, "mlp", [(0, 1), (1, 0)])
    mixed = (resid.astype(jnp.float32) + projected).astype(jnp.bfloat16)
    normed = rms_scale(mixed, gain_mid)
    column = lax.axis_index("mlp")
    half_count = normed.shape[0] // lax.axis_size("mlp")
    group_rows = lax.all_gather(normed, "y", axis=0, tiled=True)
    dims = (((1,), (2,)), ((), ()))
    gate = lax.dot_general(group_rows, all_w[:, 0], dims, preferred_element_type=jnp.float32)
    up_part = lax.dot_general(group_rows, all_w[:, 1], dims, preferred_element_type=jnp.float32)
    hidden = (jax.nn.silu(gate) * up_part).astype(jnp.bfloat16)
    down_dims = (((1, 2), (0, 1)), ((), ()))
    partial = lax.dot_general(
        hidden, all_w[:, 2], down_dims, preferred_element_type=jnp.float32
    )
    mlp_half = lax.psum_scatter(partial, ("y", "mlp"), scatter_dimension=0, tiled=True)
    base_half = lax.dynamic_slice_in_dim(mixed, column * half_count, half_count, 0)
    out_half = (base_half.astype(jnp.float32) + mlp_half).astype(jnp.bfloat16)
    hidden_out = lax.all_gather(out_half, "mlp", axis=0, tiled=True)
    next_normed = rms_scale(hidden_out, gain_next)
    next_qkv = jnp.dot(next_normed, w_next, preferred_element_type=jnp.float32).astype(jnp.bfloat16)
    accepted = compact_path(reach, accept_leaf, kv_in.reshape(2, tree_len, 2 * kv_width))
    accepted_kv = accepted.reshape(2 * tree_len, 2, kv_width)
    return (hidden_out, next_qkv, accepted_kv)


def solution(mesh):
    devices = mesh.devices
    owners = devices.shape[0]
    lines = round(owners ** (1 / 3))
    sub_mesh = Mesh(
        devices.reshape(owners // (lines * lines), lines, lines, devices.shape[1]),
        ("z", "x", "y", "mlp"),
    )
    R = REQ
    placed = (
        P(R, None),
        P(R, "mlp"),
        P(R, None, "mlp"),
        P(R, None),
        P(R),
        P(R),
        P(R, None, None, "mlp"),
        P(R, None),
        P(R),
        P(R),
        P("mlp", None),
        P(),
        P(None, R + ("mlp",), None),
        P(R + ("mlp",), None),
        P(),
        P(None, "mlp"),
    )
    return jax.shard_map(
        per_device,
        mesh=sub_mesh,
        in_specs=placed,
        out_specs=(P(R, None), P(R, "mlp"), P(R, None, "mlp")),
        check_vma=False,
    )
```

```python
import math

import jax
import jax.numpy as jnp
from jax import lax
from jax.sharding import Mesh, PartitionSpec as P

HEAD_DIM = 64
GROUP = 4


TAG = 128
REQ = ("z", "x", "y")

norm_eps = 1e-05
masked_score = -1e30


def split_hi_lo(values):
    high = values.astype(jnp.bfloat16)
    low = (values - high.astype(jnp.float32)).astype(jnp.bfloat16)
    return jnp.concatenate([high, low], axis=1)


def ancestors(parents):
    count_nodes = parents.shape[-1]
    nodes = jnp.arange(count_nodes, dtype=jnp.int32)
    reach = (parents[..., :, None] == nodes).astype(jnp.float32) + jnp.eye(
        count_nodes, dtype=jnp.float32
    )
    for step in range(count_nodes.bit_length()):
        reach = jnp.minimum(
            jnp.einsum("sij,sjk->sik", reach, reach, precision=lax.Precision.HIGHEST), 1.0
        )
    return reach


def rms_scale(rows, gain):
    values = rows.astype(jnp.float32)
    factor = lax.rsqrt(jnp.mean(values * values, axis=-1, keepdims=True) + norm_eps)
    return (values * factor * gain.astype(jnp.float32)).astype(jnp.bfloat16)


def swiglu_rows(rows, w_in, w_down):
    dims = (((1,), (1,)), ((), ()))
    gate = lax.dot_general(rows, w_in[0], dims, preferred_element_type=jnp.float32)
    up_part = lax.dot_general(rows, w_in[1], dims, preferred_element_type=jnp.float32)
    hidden = (jax.nn.silu(gate) * up_part).astype(jnp.bfloat16)
    return jnp.dot(hidden, w_down, preferred_element_type=jnp.float32)


def compact_path(reach, leaves, rows):
    count_nodes = reach.shape[-1]
    nodes = jnp.arange(count_nodes, dtype=jnp.int32)
    leaf_hot = (nodes[None, :] == leaves[:, None]).astype(jnp.float32)
    path = jnp.einsum("si,sij->sj", leaf_hot, reach, precision=lax.Precision.HIGHEST)
    ranks = jnp.cumsum(path, axis=1) - path
    places = nodes.astype(jnp.float32)
    select = path[:, None, :] * (ranks[:, None, :] == places[None, :, None]).astype(jnp.float32)
    return jnp.einsum(
        "spj,sjw->spw", select.astype(jnp.bfloat16), rows, preferred_element_type=jnp.float32
    ).astype(jnp.bfloat16)


def per_device(
    resid,
    q_in,
    kv_in,
    parents,
    counts,
    accept_leaf,
    cache,
    held_table,
    held_len,
    prev_owner,
    w_out,
    gain_mid,
    w_in,
    w_down,
    gain_next,
    w_next,
):
    tree_len = parents.shape[1]
    kv_width = kv_in.shape[2]
    kv_local = kv_width // HEAD_DIM
    scale = HEAD_DIM ** (-0.5)
    queries = q_in.reshape(2, tree_len, kv_local, GROUP, HEAD_DIM)
    device_id = lax.axis_index(REQ)
    q_width = q_in.shape[1]
    dest_col = jnp.broadcast_to(prev_owner[0].astype(q_in.dtype), (tree_len, TAG))
    q_packet = jnp.concatenate([q_in[tree_len:], dest_col], axis=1)
    every_query = lax.all_gather(q_packet, REQ, axis=0, tiled=False)
    own_w = jnp.stack([w_in[0], w_in[1], w_down])
    all_w = lax.all_gather(own_w, ("z", "x"), axis=0, tiled=False)
    page_len = cache.shape[2]
    block_pages = math.gcd(held_table.shape[1], max(1, 1024 // page_len))
    block_keys = block_pages * page_len
    num_blocks = held_table.shape[1] // block_pages
    positions = jnp.arange(block_keys, dtype=jnp.int32)

    def attend(slot, slot_queries, first, last, state):
        table = held_table[slot]
        length = held_len[slot]

        def attend_block(block, state):
            running, total, accum = state
            page_ids = lax.dynamic_slice_in_dim(table, block * block_pages, block_pages, 0)
            gathered = cache[page_ids]
            key_rows = gathered[:, 0].reshape(block_keys, kv_local, HEAD_DIM)
            value_rows = gathered[:, 1].reshape(block_keys, kv_local, HEAD_DIM)
            scores = (
                jnp.einsum(
                    "qghe,kge->ghqk", slot_queries, key_rows, preferred_element_type=jnp.float32
                )
                * scale
            )
            visible = (block * block_keys + positions) < length
            scores = jnp.where(visible, scores, masked_score)
            newest = jnp.maximum(running, jnp.max(scores, axis=-1))
            weights = jnp.where(visible, jnp.exp(scores - newest[..., None]), 0.0)
            factor = jnp.exp(running - newest)
            total = total * factor + jnp.sum(weights, axis=-1)
            update = jnp.einsum(
                "ghqk,kge->ghqe",
                weights,
                value_rows.astype(jnp.float32),
                precision=lax.Precision.HIGHEST,
            )
            accum = accum * factor[..., None] + update
            return (newest, total, accum)

        return lax.fori_loop(first, last, attend_block, state)

    stat_shape = (kv_local, GROUP, tree_len)
    start_state = (
        jnp.full(stat_shape, masked_score, jnp.float32),
        jnp.zeros(stat_shape, jnp.float32),
        jnp.zeros(stat_shape + (HEAD_DIM,), jnp.float32),
    )
    own_queries = queries[0]
    own_state = attend(0, own_queries, 0, num_blocks, start_state)
    own_state, every_query = lax.optimization_barrier((own_state, every_query))
    dests = every_query[:, 0, q_width].astype(jnp.int32)
    senders = jnp.arange(dests.shape[0], dtype=jnp.int32)
    sender = jnp.sum(jnp.where(dests == device_id, senders, 0))
    foreign = lax.dynamic_index_in_dim(every_query, sender, 0, keepdims=False)[:, :q_width]
    foreign = foreign.reshape(tree_len, kv_local, GROUP, HEAD_DIM)
    f_running, f_total, f_accum = attend(1, foreign, 0, num_blocks, start_state)
    all_w, f_running, f_total, f_accum = lax.optimization_barrier(
        (all_w, f_running, f_total, f_accum)
    )
    f_out = f_accum / f_total[..., None]
    sent_out = jnp.transpose(f_out, (2, 0, 1, 3)).reshape(
        tree_len, kv_local * GROUP * HEAD_DIM
    )
    sent_max = jnp.transpose(f_running, (2, 0, 1)).reshape(tree_len, kv_local * GROUP)
    sent_total = jnp.transpose(f_total, (2, 0, 1)).reshape(tree_len, kv_local * GROUP)
    stats = jnp.concatenate(
        [split_hi_lo(sent_max), split_hi_lo(sent_total)], axis=1
    )
    pad = jnp.zeros((tree_len, TAG - stats.shape[1]), jnp.bfloat16)
    r_packet = jnp.concatenate([sent_out.astype(jnp.bfloat16), stats, pad], axis=1)
    back = lax.all_gather(r_packet, REQ, axis=0, tiled=False)
    running, total, accum = own_state
    cache_out = accum / total[..., None]
    got = lax.dynamic_index_in_dim(back, prev_owner[0], 0, keepdims=False).astype(jnp.float32)
    heads = kv_local * GROUP
    o_w = heads * HEAD_DIM
    recv_out = got[:, :o_w].reshape(tree_len, kv_local, GROUP, HEAD_DIM)
    recv_max = (got[:, o_w : o_w + heads] + got[:, o_w + heads : o_w + 2 * heads]).reshape(
        tree_len, kv_local, GROUP
    )
    t0 = o_w + 2 * heads
    recv_total = (got[:, t0 : t0 + heads] + got[:, t0 + heads : t0 + 2 * heads]).reshape(
        tree_len, kv_local, GROUP
    )
    part_out = jnp.stack([cache_out, jnp.transpose(recv_out, (1, 2, 0, 3))])
    part_max = jnp.stack([running, jnp.transpose(recv_max, (1, 2, 0))])
    part_total = jnp.stack([total, jnp.transpose(recv_total, (1, 2, 0))])
    reach = ancestors(parents)
    live = jnp.arange(tree_len, dtype=jnp.int32)[None, :] < counts[:, None]
    allowed = ((reach > 0.5) & live[:, None, :])[:, None, None, :, :]
    draft_keys = kv_in[:, 0].reshape(2, tree_len, kv_local, HEAD_DIM)
    draft_values = kv_in[:, 1].reshape(2, tree_len, kv_local, HEAD_DIM)
    tree_scores = (
        jnp.einsum("sqghe,skge->sghqk", queries, draft_keys, preferred_element_type=jnp.float32)
        * scale
    )
    tree_scores = jnp.where(allowed, tree_scores, masked_score)
    tree_max = jnp.max(tree_scores, axis=-1)
    tree_weights = jnp.where(allowed, jnp.exp(tree_scores - tree_max[..., None]), 0.0)
    tree_total = jnp.sum(tree_weights, axis=-1)
    tree_accum = jnp.einsum(
        "sghqk,skge->sghqe",
        tree_weights,
        draft_values.astype(jnp.float32),
        precision=lax.Precision.HIGHEST,
    )
    overall = jnp.maximum(part_max, tree_max)
    cache_weight = part_total * jnp.exp(part_max - overall)
    tree_weight = jnp.exp(tree_max - overall)
    merged = (part_out * cache_weight[..., None] + tree_accum * tree_weight[..., None]) / (
        cache_weight + tree_total * tree_weight
    )[..., None]
    attended = (
        jnp.transpose(merged, (0, 3, 1, 2, 4))
        .reshape(2 * tree_len, kv_local * GROUP * HEAD_DIM)
        .astype(jnp.bfloat16)
    )
    partial_proj = jnp.dot(attended, w_out, preferred_element_type=jnp.float32)
    projected = partial_proj + lax.ppermute(partial_proj, "mlp", [(0, 1), (1, 0)])
    mixed = (resid.astype(jnp.float32) + projected).astype(jnp.bfloat16)
    normed = rms_scale(mixed, gain_mid)
    column = lax.axis_index("mlp")
    half_count = normed.shape[0] // lax.axis_size("mlp")
    group_rows = lax.all_gather(normed, "y", axis=0, tiled=True)
    dims = (((1,), (2,)), ((), ()))
    gate = lax.dot_general(group_rows, all_w[:, 0], dims, preferred_element_type=jnp.float32)
    up_part = lax.dot_general(group_rows, all_w[:, 1], dims, preferred_element_type=jnp.float32)
    hidden = (jax.nn.silu(gate) * up_part).astype(jnp.bfloat16)
    down_dims = (((1, 2), (0, 1)), ((), ()))
    partial = lax.dot_general(
        hidden, all_w[:, 2], down_dims, preferred_element_type=jnp.float32
    )
    mlp_half = lax.psum_scatter(partial, ("y", "mlp"), scatter_dimension=0, tiled=True)
    base_half = lax.dynamic_slice_in_dim(mixed, column * half_count, half_count, 0)
    out_half = (base_half.astype(jnp.float32) + mlp_half).astype(jnp.bfloat16)
    hidden_out = lax.all_gather(out_half, "mlp", axis=0, tiled=True)
    next_normed = rms_scale(hidden_out, gain_next)
    next_qkv = jnp.dot(next_normed, w_next, preferred_element_type=jnp.float32).astype(jnp.bfloat16)
    accepted = compact_path(reach, accept_leaf, kv_in.reshape(2, tree_len, 2 * kv_width))
    accepted_kv = accepted.reshape(2 * tree_len, 2, kv_width)
    return (hidden_out, next_qkv, accepted_kv)


def solution(mesh):
    devices = mesh.devices
    owners = devices.shape[0]
    lines = round(owners ** (1 / 3))
    sub_mesh = Mesh(
        devices.reshape(owners // (lines * lines), lines, lines, devices.shape[1]),
        ("z", "x", "y", "mlp"),
    )
    R = REQ
    placed = (
        P(R, None),
        P(R, "mlp"),
        P(R, None, "mlp"),
        P(R, None),
        P(R),
        P(R),
        P(R, None, None, "mlp"),
        P(R, None),
        P(R),
        P(R),
        P("mlp", None),
        P(),
        P(None, R + ("mlp",), None),
        P(R + ("mlp",), None),
        P(),
        P(None, "mlp"),
    )
    return jax.shard_map(
        per_device,
        mesh=sub_mesh,
        in_specs=placed,
        out_specs=(P(R, None), P(R, "mlp"), P(R, None, "mlp")),
        check_vma=False,
    )
```

```python
import math

import jax
import jax.numpy as jnp
from jax import lax
from jax.sharding import Mesh, PartitionSpec as P

HEAD_DIM = 64
GROUP = 4


TAG = 128
REQ = ("z", "x", "y")

norm_eps = 1e-05
masked_score = -1e30


def split_hi_lo(values):
    high = values.astype(jnp.bfloat16)
    low = (values - high.astype(jnp.float32)).astype(jnp.bfloat16)
    return jnp.concatenate([high, low], axis=1)


def ancestors(parents):
    count_nodes = parents.shape[-1]
    nodes = jnp.arange(count_nodes, dtype=jnp.int32)
    reach = (parents[..., :, None] == nodes).astype(jnp.float32) + jnp.eye(
        count_nodes, dtype=jnp.float32
    )
    for step in range(count_nodes.bit_length()):
        reach = jnp.minimum(
            jnp.einsum("sij,sjk->sik", reach, reach, precision=lax.Precision.HIGHEST), 1.0
        )
    return reach


def rms_scale(rows, gain):
    values = rows.astype(jnp.float32)
    factor = lax.rsqrt(jnp.mean(values * values, axis=-1, keepdims=True) + norm_eps)
    return (values * factor * gain.astype(jnp.float32)).astype(jnp.bfloat16)


def swiglu_rows(rows, w_in, w_down):
    dims = (((1,), (1,)), ((), ()))
    gate = lax.dot_general(rows, w_in[0], dims, preferred_element_type=jnp.float32)
    up_part = lax.dot_general(rows, w_in[1], dims, preferred_element_type=jnp.float32)
    hidden = (jax.nn.silu(gate) * up_part).astype(jnp.bfloat16)
    return jnp.dot(hidden, w_down, preferred_element_type=jnp.float32)


def compact_path(reach, leaves, rows):
    count_nodes = reach.shape[-1]
    nodes = jnp.arange(count_nodes, dtype=jnp.int32)
    leaf_hot = (nodes[None, :] == leaves[:, None]).astype(jnp.float32)
    path = jnp.einsum("si,sij->sj", leaf_hot, reach, precision=lax.Precision.HIGHEST)
    ranks = jnp.cumsum(path, axis=1) - path
    places = nodes.astype(jnp.float32)
    select = path[:, None, :] * (ranks[:, None, :] == places[None, :, None]).astype(jnp.float32)
    return jnp.einsum(
        "spj,sjw->spw", select.astype(jnp.bfloat16), rows, preferred_element_type=jnp.float32
    ).astype(jnp.bfloat16)


def per_device(
    resid,
    q_in,
    kv_in,
    parents,
    counts,
    accept_leaf,
    cache,
    held_table,
    held_len,
    prev_owner,
    w_out,
    gain_mid,
    w_in,
    w_down,
    gain_next,
    w_next,
):
    tree_len = parents.shape[1]
    kv_width = kv_in.shape[2]
    kv_local = kv_width // HEAD_DIM
    scale = HEAD_DIM ** (-0.5)
    queries = q_in.reshape(2, tree_len, kv_local, GROUP, HEAD_DIM)
    device_id = lax.axis_index(REQ)
    q_width = q_in.shape[1]
    dest_col = jnp.broadcast_to(prev_owner[0].astype(q_in.dtype), (tree_len, TAG))
    q_packet = jnp.concatenate([q_in[tree_len:], dest_col], axis=1)
    every_query = lax.all_gather(q_packet, REQ, axis=0, tiled=False)
    all_w = lax.all_gather(w_in, ("z", "x"), axis=1, tiled=False)
    page_len = cache.shape[2]
    pool_pages = cache.shape[0]
    pool_keys = cache[:, 0].reshape(pool_pages * page_len, kv_local, HEAD_DIM)
    pool_values = cache[:, 1].reshape(pool_pages * page_len, kv_local, HEAD_DIM)
    entries = held_table.shape[1]
    page_ids = jnp.arange(pool_pages, dtype=jnp.int32)
    entry_start = jnp.arange(entries, dtype=jnp.int32)[:, None] * page_len
    in_page = jnp.arange(page_len, dtype=jnp.int32)[None, :]

    def attend(slot, slot_queries, state):
        table = held_table[slot]
        length = held_len[slot]
        match = table[:, None] == page_ids[None, :]
        valid = (entry_start + in_page) < length
        visible = jnp.any(match[:, :, None] & valid[:, None, :], axis=0).reshape(-1)
        scores = (
            jnp.einsum("qghe,kge->ghqk", slot_queries, pool_keys, preferred_element_type=jnp.float32)
            * scale
        )
        scores = jnp.where(visible, scores, masked_score)
        running = jnp.max(scores, axis=-1)
        weights = jnp.where(visible, jnp.exp(scores - running[..., None]), 0.0)
        total = jnp.sum(weights, axis=-1)
        accum = jnp.einsum(
            "ghqk,kge->ghqe",
            weights,
            pool_values.astype(jnp.float32),
            precision=lax.Precision.HIGHEST,
        )
        return (running, total, accum)

    own_queries = queries[0]
    own_state = attend(0, own_queries, None)
    own_state, every_query = lax.optimization_barrier((own_state, every_query))
    dests = every_query[:, 0, q_width].astype(jnp.int32)
    senders = jnp.arange(dests.shape[0], dtype=jnp.int32)
    sender = jnp.sum(jnp.where(dests == device_id, senders, 0))
    foreign = lax.dynamic_index_in_dim(every_query, sender, 0, keepdims=False)[:, :q_width]
    foreign = foreign.reshape(tree_len, kv_local, GROUP, HEAD_DIM)
    f_running, f_total, f_accum = attend(1, foreign, None)
    all_w, f_running, f_total, f_accum = lax.optimization_barrier(
        (all_w, f_running, f_total, f_accum)
    )
    f_out = f_accum / f_total[..., None]
    sent_out = jnp.transpose(f_out, (2, 0, 1, 3)).reshape(
        tree_len, kv_local * GROUP * HEAD_DIM
    )
    sent_max = jnp.transpose(f_running, (2, 0, 1)).reshape(tree_len, kv_local * GROUP)
    sent_total = jnp.transpose(f_total, (2, 0, 1)).reshape(tree_len, kv_local * GROUP)
    stats = jnp.concatenate(
        [split_hi_lo(sent_max), split_hi_lo(sent_total)], axis=1
    )
    pad = jnp.zeros((tree_len, TAG - stats.shape[1]), jnp.bfloat16)
    r_packet = jnp.concatenate([sent_out.astype(jnp.bfloat16), stats, pad], axis=1)
    back = lax.all_gather(r_packet, REQ, axis=0, tiled=False)
    back, w_down = lax.optimization_barrier((back, w_down))
    all_down = lax.all_gather(w_down, ("z", "x"), axis=0, tiled=False)
    running, total, accum = own_state
    cache_out = accum / total[..., None]
    got = lax.dynamic_index_in_dim(back, prev_owner[0], 0, keepdims=False).astype(jnp.float32)
    heads = kv_local * GROUP
    o_w = heads * HEAD_DIM
    recv_out = got[:, :o_w].reshape(tree_len, kv_local, GROUP, HEAD_DIM)
    recv_max = (got[:, o_w : o_w + heads] + got[:, o_w + heads : o_w + 2 * heads]).reshape(
        tree_len, kv_local, GROUP
    )
    t0 = o_w + 2 * heads
    recv_total = (got[:, t0 : t0 + heads] + got[:, t0 + heads : t0 + 2 * heads]).reshape(
        tree_len, kv_local, GROUP
    )
    part_out = jnp.stack([cache_out, jnp.transpose(recv_out, (1, 2, 0, 3))])
    part_max = jnp.stack([running, jnp.transpose(recv_max, (1, 2, 0))])
    part_total = jnp.stack([total, jnp.transpose(recv_total, (1, 2, 0))])
    reach = ancestors(parents)
    live = jnp.arange(tree_len, dtype=jnp.int32)[None, :] < counts[:, None]
    allowed = ((reach > 0.5) & live[:, None, :])[:, None, None, :, :]
    draft_keys = kv_in[:, 0].reshape(2, tree_len, kv_local, HEAD_DIM)
    draft_values = kv_in[:, 1].reshape(2, tree_len, kv_local, HEAD_DIM)
    tree_scores = (
        jnp.einsum("sqghe,skge->sghqk", queries, draft_keys, preferred_element_type=jnp.float32)
        * scale
    )
    tree_scores = jnp.where(allowed, tree_scores, masked_score)
    tree_max = jnp.max(tree_scores, axis=-1)
    tree_weights = jnp.where(allowed, jnp.exp(tree_scores - tree_max[..., None]), 0.0)
    tree_total = jnp.sum(tree_weights, axis=-1)
    tree_accum = jnp.einsum(
        "sghqk,skge->sghqe",
        tree_weights,
        draft_values.astype(jnp.float32),
        precision=lax.Precision.HIGHEST,
    )
    overall = jnp.maximum(part_max, tree_max)
    cache_weight = part_total * jnp.exp(part_max - overall)
    tree_weight = jnp.exp(tree_max - overall)
    merged = (part_out * cache_weight[..., None] + tree_accum * tree_weight[..., None]) / (
        cache_weight + tree_total * tree_weight
    )[..., None]
    attended = (
        jnp.transpose(merged, (0, 3, 1, 2, 4))
        .reshape(2 * tree_len, kv_local * GROUP * HEAD_DIM)
        .astype(jnp.bfloat16)
    )
    partial_proj = jnp.dot(attended, w_out, preferred_element_type=jnp.float32)
    projected = partial_proj + lax.ppermute(partial_proj, "mlp", [(0, 1), (1, 0)])
    mixed = (resid.astype(jnp.float32) + projected).astype(jnp.bfloat16)
    normed = rms_scale(mixed, gain_mid)
    column = lax.axis_index("mlp")
    half_count = normed.shape[0] // lax.axis_size("mlp")
    group_rows = lax.all_gather(normed, "y", axis=0, tiled=True)
    dims = (((1,), (2,)), ((), ()))
    gate = lax.dot_general(group_rows, all_w[0], dims, preferred_element_type=jnp.float32)
    up_part = lax.dot_general(group_rows, all_w[1], dims, preferred_element_type=jnp.float32)
    hidden = (jax.nn.silu(gate) * up_part).astype(jnp.bfloat16)
    down_dims = (((1, 2), (0, 1)), ((), ()))
    partial = lax.dot_general(hidden, all_down, down_dims, preferred_element_type=jnp.float32)
    mlp_half = lax.psum_scatter(partial, ("y", "mlp"), scatter_dimension=0, tiled=True)
    base_half = lax.dynamic_slice_in_dim(mixed, column * half_count, half_count, 0)
    out_half = (base_half.astype(jnp.float32) + mlp_half).astype(jnp.bfloat16)
    hidden_out = lax.all_gather(out_half, "mlp", axis=0, tiled=True)
    next_normed = rms_scale(hidden_out, gain_next)
    next_qkv = jnp.dot(next_normed, w_next, preferred_element_type=jnp.float32).astype(jnp.bfloat16)
    accepted = compact_path(reach, accept_leaf, kv_in.reshape(2, tree_len, 2 * kv_width))
    accepted_kv = accepted.reshape(2 * tree_len, 2, kv_width)
    return (hidden_out, next_qkv, accepted_kv)


def solution(mesh):
    devices = mesh.devices
    owners = devices.shape[0]
    lines = round(owners ** (1 / 3))
    sub_mesh = Mesh(
        devices.reshape(owners // (lines * lines), lines, lines, devices.shape[1]),
        ("z", "x", "y", "mlp"),
    )
    R = REQ
    placed = (
        P(R, None),
        P(R, "mlp"),
        P(R, None, "mlp"),
        P(R, None),
        P(R),
        P(R),
        P(R, None, None, "mlp"),
        P(R, None),
        P(R),
        P(R),
        P("mlp", None),
        P(),
        P(None, R + ("mlp",), None),
        P(R + ("mlp",), None),
        P(),
        P(None, "mlp"),
    )
    return jax.shard_map(
        per_device,
        mesh=sub_mesh,
        in_specs=placed,
        out_specs=(P(R, None), P(R, "mlp"), P(R, None, "mlp")),
        check_vma=False,
    )
```

```python
import math

import jax
import jax.numpy as jnp
from jax import lax
from jax.sharding import Mesh, PartitionSpec as P

HEAD_DIM = 64
GROUP = 4


TAG = 128
REQ = ("z", "x", "y")

norm_eps = 1e-05
masked_score = -1e30


def split_hi_lo(values):
    high = values.astype(jnp.bfloat16)
    low = (values - high.astype(jnp.float32)).astype(jnp.bfloat16)
    return jnp.concatenate([high, low], axis=1)


def ancestors(parents):
    count_nodes = parents.shape[-1]
    nodes = jnp.arange(count_nodes, dtype=jnp.int32)
    reach = (parents[..., :, None] == nodes).astype(jnp.float32) + jnp.eye(
        count_nodes, dtype=jnp.float32
    )
    for step in range(count_nodes.bit_length()):
        reach = jnp.minimum(
            jnp.einsum("sij,sjk->sik", reach, reach, precision=lax.Precision.HIGHEST), 1.0
        )
    return reach


def rms_scale(rows, gain):
    values = rows.astype(jnp.float32)
    factor = lax.rsqrt(jnp.mean(values * values, axis=-1, keepdims=True) + norm_eps)
    return (values * factor * gain.astype(jnp.float32)).astype(jnp.bfloat16)


def swiglu_rows(rows, w_in, w_down):
    dims = (((1,), (1,)), ((), ()))
    gate = lax.dot_general(rows, w_in[0], dims, preferred_element_type=jnp.float32)
    up_part = lax.dot_general(rows, w_in[1], dims, preferred_element_type=jnp.float32)
    hidden = (jax.nn.silu(gate) * up_part).astype(jnp.bfloat16)
    return jnp.dot(hidden, w_down, preferred_element_type=jnp.float32)


def compact_path(reach, leaves, rows):
    count_nodes = reach.shape[-1]
    nodes = jnp.arange(count_nodes, dtype=jnp.int32)
    leaf_hot = (nodes[None, :] == leaves[:, None]).astype(jnp.float32)
    path = jnp.einsum("si,sij->sj", leaf_hot, reach, precision=lax.Precision.HIGHEST)
    ranks = jnp.cumsum(path, axis=1) - path
    places = nodes.astype(jnp.float32)
    select = path[:, None, :] * (ranks[:, None, :] == places[None, :, None]).astype(jnp.float32)
    return jnp.einsum(
        "spj,sjw->spw", select.astype(jnp.bfloat16), rows, preferred_element_type=jnp.float32
    ).astype(jnp.bfloat16)


def per_device(
    resid,
    q_in,
    kv_in,
    parents,
    counts,
    accept_leaf,
    cache,
    held_table,
    held_len,
    prev_owner,
    w_out,
    gain_mid,
    w_in,
    w_down,
    gain_next,
    w_next,
):
    tree_len = parents.shape[1]
    kv_width = kv_in.shape[2]
    kv_local = kv_width // HEAD_DIM
    scale = HEAD_DIM ** (-0.5)
    queries = q_in.reshape(2, tree_len, kv_local, GROUP, HEAD_DIM)
    device_id = lax.axis_index(REQ)
    q_width = q_in.shape[1]
    dest_col = jnp.broadcast_to(prev_owner[0].astype(q_in.dtype), (tree_len, TAG))
    q_packet = jnp.concatenate([q_in[tree_len:], dest_col], axis=1)
    every_query = lax.all_gather(q_packet, REQ, axis=0, tiled=False)
    own_w = jnp.stack([w_in[0], w_in[1], w_down])
    all_w = lax.all_gather(own_w, ("z", "x"), axis=0, tiled=False)
    page_len = cache.shape[2]
    block_pages = math.gcd(held_table.shape[1], max(1, 1024 // page_len))
    block_keys = block_pages * page_len
    num_blocks = held_table.shape[1] // block_pages
    positions = jnp.arange(block_keys, dtype=jnp.int32)

    def attend(slot, slot_queries, first, last, state):
        table = held_table[slot]
        length = held_len[slot]

        def attend_block(block, state):
            running, total, accum = state
            page_ids = lax.dynamic_slice_in_dim(table, block * block_pages, block_pages, 0)
            gathered = cache[page_ids]
            key_rows = gathered[:, 0].reshape(block_keys, kv_local, HEAD_DIM)
            value_rows = gathered[:, 1].reshape(block_keys, kv_local, HEAD_DIM)
            scores = (
                jnp.einsum(
                    "qghe,kge->ghqk", slot_queries, key_rows, preferred_element_type=jnp.float32
                )
                * scale
            )
            visible = (block * block_keys + positions) < length
            scores = jnp.where(visible, scores, masked_score)
            newest = jnp.maximum(running, jnp.max(scores, axis=-1))
            weights = jnp.where(visible, jnp.exp(scores - newest[..., None]), 0.0)
            factor = jnp.exp(running - newest)
            total = total * factor + jnp.sum(weights, axis=-1)
            update = jnp.einsum(
                "ghqk,kge->ghqe",
                weights,
                value_rows.astype(jnp.float32),
                precision=lax.Precision.HIGHEST,
            )
            accum = accum * factor[..., None] + update
            return (newest, total, accum)

        return lax.fori_loop(first, last, attend_block, state)

    stat_shape = (kv_local, GROUP, tree_len)
    start_state = (
        jnp.full(stat_shape, masked_score, jnp.float32),
        jnp.zeros(stat_shape, jnp.float32),
        jnp.zeros(stat_shape + (HEAD_DIM,), jnp.float32),
    )
    own_queries = queries[0]
    own_state = attend(0, own_queries, 0, num_blocks, start_state)
    own_state, every_query = lax.optimization_barrier((own_state, every_query))
    dests = every_query[:, 0, q_width].astype(jnp.int32)
    senders = jnp.arange(dests.shape[0], dtype=jnp.int32)
    sender = jnp.sum(jnp.where(dests == device_id, senders, 0))
    foreign = lax.dynamic_index_in_dim(every_query, sender, 0, keepdims=False)[:, :q_width]
    foreign = foreign.reshape(tree_len, kv_local, GROUP, HEAD_DIM)
    f_running, f_total, f_accum = attend(1, foreign, 0, num_blocks, start_state)
    all_w, f_running, f_total, f_accum = lax.optimization_barrier(
        (all_w, f_running, f_total, f_accum)
    )
    f_out = f_accum / f_total[..., None]
    sent_out = jnp.transpose(f_out, (2, 0, 1, 3)).reshape(
        tree_len, kv_local * GROUP * HEAD_DIM
    )
    sent_max = jnp.transpose(f_running, (2, 0, 1)).reshape(tree_len, kv_local * GROUP)
    sent_total = jnp.transpose(f_total, (2, 0, 1)).reshape(tree_len, kv_local * GROUP)
    stats = jnp.concatenate(
        [split_hi_lo(sent_max), split_hi_lo(sent_total)], axis=1
    )
    pad = jnp.zeros((tree_len, TAG - stats.shape[1]), jnp.bfloat16)
    r_packet = jnp.concatenate([sent_out.astype(jnp.bfloat16), stats, pad], axis=1)
    back = lax.all_gather(r_packet, REQ, axis=0, tiled=False)
    running, total, accum = own_state
    cache_out = accum / total[..., None]
    got = lax.dynamic_index_in_dim(back, prev_owner[0], 0, keepdims=False).astype(jnp.float32)
    heads = kv_local * GROUP
    o_w = heads * HEAD_DIM
    recv_out = got[:, :o_w].reshape(tree_len, kv_local, GROUP, HEAD_DIM)
    recv_max = (got[:, o_w : o_w + heads] + got[:, o_w + heads : o_w + 2 * heads]).reshape(
        tree_len, kv_local, GROUP
    )
    t0 = o_w + 2 * heads
    recv_total = (got[:, t0 : t0 + heads] + got[:, t0 + heads : t0 + 2 * heads]).reshape(
        tree_len, kv_local, GROUP
    )
    part_out = jnp.stack([cache_out, jnp.transpose(recv_out, (1, 2, 0, 3))])
    part_max = jnp.stack([running, jnp.transpose(recv_max, (1, 2, 0))])
    part_total = jnp.stack([total, jnp.transpose(recv_total, (1, 2, 0))])
    reach = ancestors(parents)
    live = jnp.arange(tree_len, dtype=jnp.int32)[None, :] < counts[:, None]
    allowed = ((reach > 0.5) & live[:, None, :])[:, None, None, :, :]
    draft_keys = kv_in[:, 0].reshape(2, tree_len, kv_local, HEAD_DIM)
    draft_values = kv_in[:, 1].reshape(2, tree_len, kv_local, HEAD_DIM)
    tree_scores = (
        jnp.einsum("sqghe,skge->sghqk", queries, draft_keys, preferred_element_type=jnp.float32)
        * scale
    )
    tree_scores = jnp.where(allowed, tree_scores, masked_score)
    tree_max = jnp.max(tree_scores, axis=-1)
    tree_weights = jnp.where(allowed, jnp.exp(tree_scores - tree_max[..., None]), 0.0)
    tree_total = jnp.sum(tree_weights, axis=-1)
    tree_accum = jnp.einsum(
        "sghqk,skge->sghqe",
        tree_weights,
        draft_values.astype(jnp.float32),
        precision=lax.Precision.HIGHEST,
    )
    overall = jnp.maximum(part_max, tree_max)
    cache_weight = part_total * jnp.exp(part_max - overall)
    tree_weight = jnp.exp(tree_max - overall)
    merged = (part_out * cache_weight[..., None] + tree_accum * tree_weight[..., None]) / (
        cache_weight + tree_total * tree_weight
    )[..., None]
    attended = (
        jnp.transpose(merged, (0, 3, 1, 2, 4))
        .reshape(2 * tree_len, kv_local * GROUP * HEAD_DIM)
        .astype(jnp.bfloat16)
    )
    partial_proj = jnp.dot(attended, w_out, preferred_element_type=jnp.float32)
    projected = partial_proj + lax.ppermute(partial_proj, "mlp", [(0, 1), (1, 0)])
    mixed = (resid.astype(jnp.float32) + projected).astype(jnp.bfloat16)
    normed = rms_scale(mixed, gain_mid)
    column = lax.axis_index("mlp")
    half_count = normed.shape[0] // lax.axis_size("mlp")
    ring = lax.axis_size("y")
    shifted = [normed]
    for shift in range(1, ring):
        perm = [(i, (i + shift) % ring) for i in range(ring)]
        shifted.append(lax.ppermute(normed, "y", perm))
    group_rows = jnp.concatenate(shifted, axis=0)
    dims = (((1,), (2,)), ((), ()))
    gate = lax.dot_general(group_rows, all_w[:, 0], dims, preferred_element_type=jnp.float32)
    up_part = lax.dot_general(group_rows, all_w[:, 1], dims, preferred_element_type=jnp.float32)
    hidden = (jax.nn.silu(gate) * up_part).astype(jnp.bfloat16)
    down_dims = (((1, 2), (0, 1)), ((), ()))
    partial = lax.dot_general(
        hidden, all_w[:, 2], down_dims, preferred_element_type=jnp.float32
    )
    halves = partial.reshape(ring, 2, half_count, partial.shape[1])
    mine = lax.dynamic_index_in_dim(halves, column, 1, keepdims=False)
    theirs = lax.dynamic_index_in_dim(halves, 1 - column, 1, keepdims=False)
    mine = mine + lax.ppermute(theirs, "mlp", [(0, 1), (1, 0)])
    mlp_half = mine[0]
    for shift in range(1, ring):
        perm = [(i, (i - shift) % ring) for i in range(ring)]
        mlp_half = mlp_half + lax.ppermute(mine[shift], "y", perm)
    base_half = lax.dynamic_slice_in_dim(mixed, column * half_count, half_count, 0)
    out_half = (base_half.astype(jnp.float32) + mlp_half).astype(jnp.bfloat16)
    hidden_out = lax.all_gather(out_half, "mlp", axis=0, tiled=True)
    next_normed = rms_scale(hidden_out, gain_next)
    next_qkv = jnp.dot(next_normed, w_next, preferred_element_type=jnp.float32).astype(jnp.bfloat16)
    accepted = compact_path(reach, accept_leaf, kv_in.reshape(2, tree_len, 2 * kv_width))
    accepted_kv = accepted.reshape(2 * tree_len, 2, kv_width)
    return (hidden_out, next_qkv, accepted_kv)


def solution(mesh):
    devices = mesh.devices
    owners = devices.shape[0]
    lines = round(owners ** (1 / 3))
    sub_mesh = Mesh(
        devices.reshape(owners // (lines * lines), lines, lines, devices.shape[1]),
        ("z", "x", "y", "mlp"),
    )
    R = REQ
    placed = (
        P(R, None),
        P(R, "mlp"),
        P(R, None, "mlp"),
        P(R, None),
        P(R),
        P(R),
        P(R, None, None, "mlp"),
        P(R, None),
        P(R),
        P(R),
        P("mlp", None),
        P(),
        P(None, R + ("mlp",), None),
        P(R + ("mlp",), None),
        P(),
        P(None, "mlp"),
    )
    return jax.shard_map(
        per_device,
        mesh=sub_mesh,
        in_specs=placed,
        out_specs=(P(R, None), P(R, "mlp"), P(R, None, "mlp")),
        check_vma=False,
    )
```

```python
import math

import jax
import jax.numpy as jnp
from jax import lax
from jax.sharding import Mesh, PartitionSpec as P

HEAD_DIM = 64
GROUP = 4


TAG = 128
REQ = ("z", "x", "y")

norm_eps = 1e-05
masked_score = -1e30


def split_hi_lo(values):
    high = values.astype(jnp.bfloat16)
    low = (values - high.astype(jnp.float32)).astype(jnp.bfloat16)
    return jnp.concatenate([high, low], axis=1)


def ancestors(parents):
    count_nodes = parents.shape[-1]
    nodes = jnp.arange(count_nodes, dtype=jnp.int32)
    reach = (parents[..., :, None] == nodes).astype(jnp.float32) + jnp.eye(
        count_nodes, dtype=jnp.float32
    )
    for step in range(count_nodes.bit_length()):
        reach = jnp.minimum(
            jnp.einsum("sij,sjk->sik", reach, reach, precision=lax.Precision.HIGHEST), 1.0
        )
    return reach


def rms_scale(rows, gain):
    values = rows.astype(jnp.float32)
    factor = lax.rsqrt(jnp.mean(values * values, axis=-1, keepdims=True) + norm_eps)
    return (values * factor * gain.astype(jnp.float32)).astype(jnp.bfloat16)


def swiglu_rows(rows, w_in, w_down):
    dims = (((1,), (1,)), ((), ()))
    gate = lax.dot_general(rows, w_in[0], dims, preferred_element_type=jnp.float32)
    up_part = lax.dot_general(rows, w_in[1], dims, preferred_element_type=jnp.float32)
    hidden = (jax.nn.silu(gate) * up_part).astype(jnp.bfloat16)
    return jnp.dot(hidden, w_down, preferred_element_type=jnp.float32)


def compact_path(reach, leaves, rows):
    count_nodes = reach.shape[-1]
    nodes = jnp.arange(count_nodes, dtype=jnp.int32)
    leaf_hot = (nodes[None, :] == leaves[:, None]).astype(jnp.float32)
    path = jnp.einsum("si,sij->sj", leaf_hot, reach, precision=lax.Precision.HIGHEST)
    ranks = jnp.cumsum(path, axis=1) - path
    places = nodes.astype(jnp.float32)
    select = path[:, None, :] * (ranks[:, None, :] == places[None, :, None]).astype(jnp.float32)
    return jnp.einsum(
        "spj,sjw->spw", select.astype(jnp.bfloat16), rows, preferred_element_type=jnp.float32
    ).astype(jnp.bfloat16)


def per_device(
    resid,
    q_in,
    kv_in,
    parents,
    counts,
    accept_leaf,
    cache,
    held_table,
    held_len,
    prev_owner,
    w_out,
    gain_mid,
    w_in,
    w_down,
    gain_next,
    w_next,
):
    tree_len = parents.shape[1]
    kv_width = kv_in.shape[2]
    kv_local = kv_width // HEAD_DIM
    scale = HEAD_DIM ** (-0.5)
    queries = q_in.reshape(2, tree_len, kv_local, GROUP, HEAD_DIM)
    device_id = lax.axis_index(REQ)
    q_width = q_in.shape[1]
    owners = lax.axis_size(REQ)
    marker = jnp.ones((tree_len, TAG), q_in.dtype)
    q_packet = jnp.concatenate([q_in[tree_len:], marker], axis=1)
    q_send = jnp.zeros((owners,) + q_packet.shape, q_packet.dtype)
    q_send = lax.dynamic_update_index_in_dim(q_send, q_packet, prev_owner[0], 0)
    every_query = lax.all_to_all(q_send, REQ, 0, 0, tiled=True)
    own_w = jnp.stack([w_in[0], w_in[1], w_down])
    all_w = lax.all_gather(own_w, ("z", "x"), axis=0, tiled=False)
    page_len = cache.shape[2]
    block_pages = math.gcd(held_table.shape[1], max(1, 1024 // page_len))
    block_keys = block_pages * page_len
    num_blocks = held_table.shape[1] // block_pages
    positions = jnp.arange(block_keys, dtype=jnp.int32)

    def attend(slot, slot_queries, first, last, state):
        table = held_table[slot]
        length = held_len[slot]

        def attend_block(block, state):
            running, total, accum = state
            page_ids = lax.dynamic_slice_in_dim(table, block * block_pages, block_pages, 0)
            gathered = cache[page_ids]
            key_rows = gathered[:, 0].reshape(block_keys, kv_local, HEAD_DIM)
            value_rows = gathered[:, 1].reshape(block_keys, kv_local, HEAD_DIM)
            scores = (
                jnp.einsum(
                    "qghe,kge->ghqk", slot_queries, key_rows, preferred_element_type=jnp.float32
                )
                * scale
            )
            visible = (block * block_keys + positions) < length
            scores = jnp.where(visible, scores, masked_score)
            newest = jnp.maximum(running, jnp.max(scores, axis=-1))
            weights = jnp.where(visible, jnp.exp(scores - newest[..., None]), 0.0)
            factor = jnp.exp(running - newest)
            total = total * factor + jnp.sum(weights, axis=-1)
            update = jnp.einsum(
                "ghqk,kge->ghqe",
                weights,
                value_rows.astype(jnp.float32),
                precision=lax.Precision.HIGHEST,
            )
            accum = accum * factor[..., None] + update
            return (newest, total, accum)

        return lax.fori_loop(first, last, attend_block, state)

    stat_shape = (kv_local, GROUP, tree_len)
    start_state = (
        jnp.full(stat_shape, masked_score, jnp.float32),
        jnp.zeros(stat_shape, jnp.float32),
        jnp.zeros(stat_shape + (HEAD_DIM,), jnp.float32),
    )
    own_queries = queries[0]
    own_state = attend(0, own_queries, 0, num_blocks, start_state)
    own_state, every_query = lax.optimization_barrier((own_state, every_query))
    marks = every_query[:, 0, q_width]
    senders = jnp.arange(marks.shape[0], dtype=jnp.int32)
    sender = jnp.sum(jnp.where(marks > 0.5, senders, 0))
    foreign = lax.dynamic_index_in_dim(every_query, sender, 0, keepdims=False)[:, :q_width]
    foreign = foreign.reshape(tree_len, kv_local, GROUP, HEAD_DIM)
    f_running, f_total, f_accum = attend(1, foreign, 0, num_blocks, start_state)
    all_w, f_running, f_total, f_accum = lax.optimization_barrier(
        (all_w, f_running, f_total, f_accum)
    )
    f_out = f_accum / f_total[..., None]
    sent_out = jnp.transpose(f_out, (2, 0, 1, 3)).reshape(
        tree_len, kv_local * GROUP * HEAD_DIM
    )
    sent_max = jnp.transpose(f_running, (2, 0, 1)).reshape(tree_len, kv_local * GROUP)
    sent_total = jnp.transpose(f_total, (2, 0, 1)).reshape(tree_len, kv_local * GROUP)
    stats = jnp.concatenate(
        [split_hi_lo(sent_max), split_hi_lo(sent_total)], axis=1
    )
    pad = jnp.zeros((tree_len, TAG - stats.shape[1]), jnp.bfloat16)
    r_packet = jnp.concatenate([sent_out.astype(jnp.bfloat16), stats, pad], axis=1)
    r_send = jnp.zeros((owners,) + r_packet.shape, r_packet.dtype)
    r_send = lax.dynamic_update_index_in_dim(r_send, r_packet, sender, 0)
    back = lax.all_to_all(r_send, REQ, 0, 0, tiled=True)
    running, total, accum = own_state
    cache_out = accum / total[..., None]
    got = lax.dynamic_index_in_dim(back, prev_owner[0], 0, keepdims=False).astype(jnp.float32)
    heads = kv_local * GROUP
    o_w = heads * HEAD_DIM
    recv_out = got[:, :o_w].reshape(tree_len, kv_local, GROUP, HEAD_DIM)
    recv_max = (got[:, o_w : o_w + heads] + got[:, o_w + heads : o_w + 2 * heads]).reshape(
        tree_len, kv_local, GROUP
    )
    t0 = o_w + 2 * heads
    recv_total = (got[:, t0 : t0 + heads] + got[:, t0 + heads : t0 + 2 * heads]).reshape(
        tree_len, kv_local, GROUP
    )
    part_out = jnp.stack([cache_out, jnp.transpose(recv_out, (1, 2, 0, 3))])
    part_max = jnp.stack([running, jnp.transpose(recv_max, (1, 2, 0))])
    part_total = jnp.stack([total, jnp.transpose(recv_total, (1, 2, 0))])
    reach = ancestors(parents)
    live = jnp.arange(tree_len, dtype=jnp.int32)[None, :] < counts[:, None]
    allowed = ((reach > 0.5) & live[:, None, :])[:, None, None, :, :]
    draft_keys = kv_in[:, 0].reshape(2, tree_len, kv_local, HEAD_DIM)
    draft_values = kv_in[:, 1].reshape(2, tree_len, kv_local, HEAD_DIM)
    tree_scores = (
        jnp.einsum("sqghe,skge->sghqk", queries, draft_keys, preferred_element_type=jnp.float32)
        * scale
    )
    tree_scores = jnp.where(allowed, tree_scores, masked_score)
    tree_max = jnp.max(tree_scores, axis=-1)
    tree_weights = jnp.where(allowed, jnp.exp(tree_scores - tree_max[..., None]), 0.0)
    tree_total = jnp.sum(tree_weights, axis=-1)
    tree_accum = jnp.einsum(
        "sghqk,skge->sghqe",
        tree_weights,
        draft_values.astype(jnp.float32),
        precision=lax.Precision.HIGHEST,
    )
    overall = jnp.maximum(part_max, tree_max)
    cache_weight = part_total * jnp.exp(part_max - overall)
    tree_weight = jnp.exp(tree_max - overall)
    merged = (part_out * cache_weight[..., None] + tree_accum * tree_weight[..., None]) / (
        cache_weight + tree_total * tree_weight
    )[..., None]
    attended = (
        jnp.transpose(merged, (0, 3, 1, 2, 4))
        .reshape(2 * tree_len, kv_local * GROUP * HEAD_DIM)
        .astype(jnp.bfloat16)
    )
    partial_proj = jnp.dot(attended, w_out, preferred_element_type=jnp.float32)
    projected = partial_proj + lax.ppermute(partial_proj, "mlp", [(0, 1), (1, 0)])
    mixed = (resid.astype(jnp.float32) + projected).astype(jnp.bfloat16)
    normed = rms_scale(mixed, gain_mid)
    column = lax.axis_index("mlp")
    half_count = normed.shape[0] // lax.axis_size("mlp")
    ring = lax.axis_size("y")
    shifted = [normed]
    for shift in range(1, ring):
        perm = [(i, (i + shift) % ring) for i in range(ring)]
        shifted.append(lax.ppermute(normed, "y", perm))
    group_rows = jnp.concatenate(shifted, axis=0)
    dims = (((1,), (2,)), ((), ()))
    gate = lax.dot_general(group_rows, all_w[:, 0], dims, preferred_element_type=jnp.float32)
    up_part = lax.dot_general(group_rows, all_w[:, 1], dims, preferred_element_type=jnp.float32)
    hidden = (jax.nn.silu(gate) * up_part).astype(jnp.bfloat16)
    down_dims = (((1, 2), (0, 1)), ((), ()))
    partial = lax.dot_general(
        hidden, all_w[:, 2], down_dims, preferred_element_type=jnp.float32
    )
    halves = partial.reshape(ring, 2, half_count, partial.shape[1])
    mine = lax.dynamic_index_in_dim(halves, column, 1, keepdims=False)
    theirs = lax.dynamic_index_in_dim(halves, 1 - column, 1, keepdims=False)
    mine = mine + lax.ppermute(theirs, "mlp", [(0, 1), (1, 0)])
    mlp_half = mine[0]
    for shift in range(1, ring):
        perm = [(i, (i - shift) % ring) for i in range(ring)]
        mlp_half = mlp_half + lax.ppermute(mine[shift], "y", perm)
    base_half = lax.dynamic_slice_in_dim(mixed, column * half_count, half_count, 0)
    out_half = (base_half.astype(jnp.float32) + mlp_half).astype(jnp.bfloat16)
    hidden_out = lax.all_gather(out_half, "mlp", axis=0, tiled=True)
    next_normed = rms_scale(hidden_out, gain_next)
    next_qkv = jnp.dot(next_normed, w_next, preferred_element_type=jnp.float32).astype(jnp.bfloat16)
    accepted = compact_path(reach, accept_leaf, kv_in.reshape(2, tree_len, 2 * kv_width))
    accepted_kv = accepted.reshape(2 * tree_len, 2, kv_width)
    return (hidden_out, next_qkv, accepted_kv)


def solution(mesh):
    devices = mesh.devices
    owners = devices.shape[0]
    lines = round(owners ** (1 / 3))
    sub_mesh = Mesh(
        devices.reshape(owners // (lines * lines), lines, lines, devices.shape[1]),
        ("z", "x", "y", "mlp"),
    )
    R = REQ
    placed = (
        P(R, None),
        P(R, "mlp"),
        P(R, None, "mlp"),
        P(R, None),
        P(R),
        P(R),
        P(R, None, None, "mlp"),
        P(R, None),
        P(R),
        P(R),
        P("mlp", None),
        P(),
        P(None, R + ("mlp",), None),
        P(R + ("mlp",), None),
        P(),
        P(None, "mlp"),
    )
    return jax.shard_map(
        per_device,
        mesh=sub_mesh,
        in_specs=placed,
        out_specs=(P(R, None), P(R, "mlp"), P(R, None, "mlp")),
        check_vma=False,
    )
```

```python
import math

import jax
import jax.numpy as jnp
from jax import lax
from jax.sharding import Mesh, PartitionSpec as P

HEAD_DIM = 64
GROUP = 4


TAG = 128
REQ = ("z", "x", "y")

norm_eps = 1e-05
masked_score = -1e30


def split_hi_lo(values):
    high = values.astype(jnp.bfloat16)
    low = (values - high.astype(jnp.float32)).astype(jnp.bfloat16)
    return jnp.concatenate([high, low], axis=1)


def ancestors(parents):
    count_nodes = parents.shape[-1]
    nodes = jnp.arange(count_nodes, dtype=jnp.int32)
    reach = (parents[..., :, None] == nodes).astype(jnp.float32) + jnp.eye(
        count_nodes, dtype=jnp.float32
    )
    for step in range(count_nodes.bit_length()):
        reach = jnp.minimum(
            jnp.einsum("sij,sjk->sik", reach, reach, precision=lax.Precision.HIGHEST), 1.0
        )
    return reach


def rms_scale(rows, gain):
    values = rows.astype(jnp.float32)
    factor = lax.rsqrt(jnp.mean(values * values, axis=-1, keepdims=True) + norm_eps)
    return (values * factor * gain.astype(jnp.float32)).astype(jnp.bfloat16)


def swiglu_rows(rows, w_in, w_down):
    dims = (((1,), (1,)), ((), ()))
    gate = lax.dot_general(rows, w_in[0], dims, preferred_element_type=jnp.float32)
    up_part = lax.dot_general(rows, w_in[1], dims, preferred_element_type=jnp.float32)
    hidden = (jax.nn.silu(gate) * up_part).astype(jnp.bfloat16)
    return jnp.dot(hidden, w_down, preferred_element_type=jnp.float32)


def compact_path(reach, leaves, rows):
    count_nodes = reach.shape[-1]
    nodes = jnp.arange(count_nodes, dtype=jnp.int32)
    leaf_hot = (nodes[None, :] == leaves[:, None]).astype(jnp.float32)
    path = jnp.einsum("si,sij->sj", leaf_hot, reach, precision=lax.Precision.HIGHEST)
    ranks = jnp.cumsum(path, axis=1) - path
    places = nodes.astype(jnp.float32)
    select = path[:, None, :] * (ranks[:, None, :] == places[None, :, None]).astype(jnp.float32)
    return jnp.einsum(
        "spj,sjw->spw", select.astype(jnp.bfloat16), rows, preferred_element_type=jnp.float32
    ).astype(jnp.bfloat16)


def per_device(
    resid,
    q_in,
    kv_in,
    parents,
    counts,
    accept_leaf,
    cache,
    held_table,
    held_len,
    prev_owner,
    w_out,
    gain_mid,
    w_in,
    w_down,
    gain_next,
    w_next,
):
    tree_len = parents.shape[1]
    kv_width = kv_in.shape[2]
    kv_local = kv_width // HEAD_DIM
    scale = HEAD_DIM ** (-0.5)
    queries = q_in.reshape(2, tree_len, kv_local, GROUP, HEAD_DIM)
    device_id = lax.axis_index(REQ)
    q_width = q_in.shape[1]
    owners = lax.axis_size(REQ)
    marker = jnp.ones((tree_len, TAG), q_in.dtype)
    q_packet = jnp.concatenate([q_in[tree_len:], marker], axis=1)
    q_send = jnp.zeros((owners,) + q_packet.shape, q_packet.dtype)
    q_send = lax.dynamic_update_index_in_dim(q_send, q_packet, prev_owner[0], 0)
    every_query = lax.all_to_all(q_send, REQ, 0, 0, tiled=True)
    own_w = jnp.stack([w_in[0], w_in[1], w_down])
    all_w = lax.all_gather(own_w, ("z", "x"), axis=0, tiled=False)
    page_len = cache.shape[2]
    block_pages = math.gcd(held_table.shape[1], max(1, 1024 // page_len))
    block_keys = block_pages * page_len
    num_blocks = held_table.shape[1] // block_pages
    positions = jnp.arange(block_keys, dtype=jnp.int32)

    def attend(slot, slot_queries, first, last, state):
        table = held_table[slot]
        length = held_len[slot]

        def attend_block(block, state):
            running, total, accum = state
            page_ids = lax.dynamic_slice_in_dim(table, block * block_pages, block_pages, 0)
            gathered = cache[page_ids]
            key_rows = gathered[:, 0].reshape(block_keys, kv_local, HEAD_DIM)
            value_rows = gathered[:, 1].reshape(block_keys, kv_local, HEAD_DIM)
            scores = (
                jnp.einsum(
                    "qghe,kge->ghqk", slot_queries, key_rows, preferred_element_type=jnp.float32
                )
                * scale
            )
            visible = (block * block_keys + positions) < length
            scores = jnp.where(visible, scores, masked_score)
            newest = jnp.maximum(running, jnp.max(scores, axis=-1))
            weights = jnp.where(visible, jnp.exp(scores - newest[..., None]), 0.0)
            factor = jnp.exp(running - newest)
            total = total * factor + jnp.sum(weights, axis=-1)
            update = jnp.einsum(
                "ghqk,kge->ghqe",
                weights,
                value_rows.astype(jnp.float32),
                precision=lax.Precision.HIGHEST,
            )
            accum = accum * factor[..., None] + update
            return (newest, total, accum)

        return lax.fori_loop(first, last, attend_block, state)

    stat_shape = (kv_local, GROUP, tree_len)
    start_state = (
        jnp.full(stat_shape, masked_score, jnp.float32),
        jnp.zeros(stat_shape, jnp.float32),
        jnp.zeros(stat_shape + (HEAD_DIM,), jnp.float32),
    )
    own_queries = queries[0]
    split = num_blocks // 2
    own_state = attend(0, own_queries, 0, split, start_state)
    own_state, every_query = lax.optimization_barrier((own_state, every_query))
    marks = every_query[:, 0, q_width]
    senders = jnp.arange(marks.shape[0], dtype=jnp.int32)
    sender = jnp.sum(jnp.where(marks > 0.5, senders, 0))
    foreign = lax.dynamic_index_in_dim(every_query, sender, 0, keepdims=False)[:, :q_width]
    foreign = foreign.reshape(tree_len, kv_local, GROUP, HEAD_DIM)
    f_running, f_total, f_accum = attend(1, foreign, 0, num_blocks, start_state)
    f_out = f_accum / f_total[..., None]
    sent_out = jnp.transpose(f_out, (2, 0, 1, 3)).reshape(
        tree_len, kv_local * GROUP * HEAD_DIM
    )
    sent_max = jnp.transpose(f_running, (2, 0, 1)).reshape(tree_len, kv_local * GROUP)
    sent_total = jnp.transpose(f_total, (2, 0, 1)).reshape(tree_len, kv_local * GROUP)
    stats = jnp.concatenate(
        [split_hi_lo(sent_max), split_hi_lo(sent_total)], axis=1
    )
    pad = jnp.zeros((tree_len, TAG - stats.shape[1]), jnp.bfloat16)
    r_packet = jnp.concatenate([sent_out.astype(jnp.bfloat16), stats, pad], axis=1)
    r_send = jnp.zeros((owners,) + r_packet.shape, r_packet.dtype)
    r_send = lax.dynamic_update_index_in_dim(r_send, r_packet, sender, 0)
    r_send, own_state = lax.optimization_barrier((r_send, own_state))
    back = lax.all_to_all(r_send, REQ, 0, 0, tiled=True)
    running, total, accum = attend(0, own_queries, split, num_blocks, own_state)
    all_w, running, total, accum = lax.optimization_barrier((all_w, running, total, accum))
    cache_out = accum / total[..., None]
    got = lax.dynamic_index_in_dim(back, prev_owner[0], 0, keepdims=False).astype(jnp.float32)
    heads = kv_local * GROUP
    o_w = heads * HEAD_DIM
    recv_out = got[:, :o_w].reshape(tree_len, kv_local, GROUP, HEAD_DIM)
    recv_max = (got[:, o_w : o_w + heads] + got[:, o_w + heads : o_w + 2 * heads]).reshape(
        tree_len, kv_local, GROUP
    )
    t0 = o_w + 2 * heads
    recv_total = (got[:, t0 : t0 + heads] + got[:, t0 + heads : t0 + 2 * heads]).reshape(
        tree_len, kv_local, GROUP
    )
    part_out = jnp.stack([cache_out, jnp.transpose(recv_out, (1, 2, 0, 3))])
    part_max = jnp.stack([running, jnp.transpose(recv_max, (1, 2, 0))])
    part_total = jnp.stack([total, jnp.transpose(recv_total, (1, 2, 0))])
    reach = ancestors(parents)
    live = jnp.arange(tree_len, dtype=jnp.int32)[None, :] < counts[:, None]
    allowed = ((reach > 0.5) & live[:, None, :])[:, None, None, :, :]
    draft_keys = kv_in[:, 0].reshape(2, tree_len, kv_local, HEAD_DIM)
    draft_values = kv_in[:, 1].reshape(2, tree_len, kv_local, HEAD_DIM)
    tree_scores = (
        jnp.einsum("sqghe,skge->sghqk", queries, draft_keys, preferred_element_type=jnp.float32)
        * scale
    )
    tree_scores = jnp.where(allowed, tree_scores, masked_score)
    tree_max = jnp.max(tree_scores, axis=-1)
    tree_weights = jnp.where(allowed, jnp.exp(tree_scores - tree_max[..., None]), 0.0)
    tree_total = jnp.sum(tree_weights, axis=-1)
    tree_accum = jnp.einsum(
        "sghqk,skge->sghqe",
        tree_weights,
        draft_values.astype(jnp.float32),
        precision=lax.Precision.HIGHEST,
    )
    overall = jnp.maximum(part_max, tree_max)
    cache_weight = part_total * jnp.exp(part_max - overall)
    tree_weight = jnp.exp(tree_max - overall)
    merged = (part_out * cache_weight[..., None] + tree_accum * tree_weight[..., None]) / (
        cache_weight + tree_total * tree_weight
    )[..., None]
    attended = (
        jnp.transpose(merged, (0, 3, 1, 2, 4))
        .reshape(2 * tree_len, kv_local * GROUP * HEAD_DIM)
        .astype(jnp.bfloat16)
    )
    partial_proj = jnp.dot(attended, w_out, preferred_element_type=jnp.float32)
    projected = partial_proj + lax.ppermute(partial_proj, "mlp", [(0, 1), (1, 0)])
    mixed = (resid.astype(jnp.float32) + projected).astype(jnp.bfloat16)
    normed = rms_scale(mixed, gain_mid)
    column = lax.axis_index("mlp")
    half_count = normed.shape[0] // lax.axis_size("mlp")
    ring = lax.axis_size("y")
    shifted = [normed]
    for shift in range(1, ring):
        perm = [(i, (i + shift) % ring) for i in range(ring)]
        shifted.append(lax.ppermute(normed, "y", perm))
    group_rows = jnp.concatenate(shifted, axis=0)
    dims = (((1,), (2,)), ((), ()))
    gate = lax.dot_general(group_rows, all_w[:, 0], dims, preferred_element_type=jnp.float32)
    up_part = lax.dot_general(group_rows, all_w[:, 1], dims, preferred_element_type=jnp.float32)
    hidden = (jax.nn.silu(gate) * up_part).astype(jnp.bfloat16)
    down_dims = (((1, 2), (0, 1)), ((), ()))
    partial = lax.dot_general(
        hidden, all_w[:, 2], down_dims, preferred_element_type=jnp.float32
    )
    halves = partial.reshape(ring, 2, half_count, partial.shape[1])
    mine = lax.dynamic_index_in_dim(halves, column, 1, keepdims=False)
    theirs = lax.dynamic_index_in_dim(halves, 1 - column, 1, keepdims=False)
    mine = mine + lax.ppermute(theirs, "mlp", [(0, 1), (1, 0)])
    mlp_half = mine[0]
    for shift in range(1, ring):
        perm = [(i, (i - shift) % ring) for i in range(ring)]
        mlp_half = mlp_half + lax.ppermute(mine[shift], "y", perm)
    base_half = lax.dynamic_slice_in_dim(mixed, column * half_count, half_count, 0)
    out_half = (base_half.astype(jnp.float32) + mlp_half).astype(jnp.bfloat16)
    hidden_out = lax.all_gather(out_half, "mlp", axis=0, tiled=True)
    next_normed = rms_scale(hidden_out, gain_next)
    next_qkv = jnp.dot(next_normed, w_next, preferred_element_type=jnp.float32).astype(jnp.bfloat16)
    accepted = compact_path(reach, accept_leaf, kv_in.reshape(2, tree_len, 2 * kv_width))
    accepted_kv = accepted.reshape(2 * tree_len, 2, kv_width)
    return (hidden_out, next_qkv, accepted_kv)


def solution(mesh):
    devices = mesh.devices
    owners = devices.shape[0]
    lines = round(owners ** (1 / 3))
    sub_mesh = Mesh(
        devices.reshape(owners // (lines * lines), lines, lines, devices.shape[1]),
        ("z", "x", "y", "mlp"),
    )
    R = REQ
    placed = (
        P(R, None),
        P(R, "mlp"),
        P(R, None, "mlp"),
        P(R, None),
        P(R),
        P(R),
        P(R, None, None, "mlp"),
        P(R, None),
        P(R),
        P(R),
        P("mlp", None),
        P(),
        P(None, R + ("mlp",), None),
        P(R + ("mlp",), None),
        P(),
        P(None, "mlp"),
    )
    return jax.shard_map(
        per_device,
        mesh=sub_mesh,
        in_specs=placed,
        out_specs=(P(R, None), P(R, "mlp"), P(R, None, "mlp")),
        check_vma=False,
    )
```

```python
import math

import jax
import jax.numpy as jnp
from jax import lax
from jax.sharding import Mesh, PartitionSpec as P

HEAD_DIM = 64
GROUP = 4


TAG = 128
REQ = ("z", "x", "y")

norm_eps = 1e-05
masked_score = -1e30


def split_hi_lo(values):
    high = values.astype(jnp.bfloat16)
    low = (values - high.astype(jnp.float32)).astype(jnp.bfloat16)
    return jnp.concatenate([high, low], axis=1)


def ancestors(parents):
    count_nodes = parents.shape[-1]
    nodes = jnp.arange(count_nodes, dtype=jnp.int32)
    reach = (parents[..., :, None] == nodes).astype(jnp.float32) + jnp.eye(
        count_nodes, dtype=jnp.float32
    )
    for step in range(count_nodes.bit_length()):
        reach = jnp.minimum(
            jnp.einsum("sij,sjk->sik", reach, reach, precision=lax.Precision.HIGHEST), 1.0
        )
    return reach


def rms_scale(rows, gain):
    values = rows.astype(jnp.float32)
    factor = lax.rsqrt(jnp.mean(values * values, axis=-1, keepdims=True) + norm_eps)
    return (values * factor * gain.astype(jnp.float32)).astype(jnp.bfloat16)


def swiglu_rows(rows, w_in, w_down):
    dims = (((1,), (1,)), ((), ()))
    gate = lax.dot_general(rows, w_in[0], dims, preferred_element_type=jnp.float32)
    up_part = lax.dot_general(rows, w_in[1], dims, preferred_element_type=jnp.float32)
    hidden = (jax.nn.silu(gate) * up_part).astype(jnp.bfloat16)
    return jnp.dot(hidden, w_down, preferred_element_type=jnp.float32)


def compact_path(reach, leaves, rows):
    count_nodes = reach.shape[-1]
    nodes = jnp.arange(count_nodes, dtype=jnp.int32)
    leaf_hot = (nodes[None, :] == leaves[:, None]).astype(jnp.float32)
    path = jnp.einsum("si,sij->sj", leaf_hot, reach, precision=lax.Precision.HIGHEST)
    ranks = jnp.cumsum(path, axis=1) - path
    places = nodes.astype(jnp.float32)
    select = path[:, None, :] * (ranks[:, None, :] == places[None, :, None]).astype(jnp.float32)
    return jnp.einsum(
        "spj,sjw->spw", select.astype(jnp.bfloat16), rows, preferred_element_type=jnp.float32
    ).astype(jnp.bfloat16)


def per_device(
    resid,
    q_in,
    kv_in,
    parents,
    counts,
    accept_leaf,
    cache,
    held_table,
    held_len,
    prev_owner,
    w_out,
    gain_mid,
    w_in,
    w_down,
    gain_next,
    w_next,
):
    tree_len = parents.shape[1]
    kv_width = kv_in.shape[2]
    kv_local = kv_width // HEAD_DIM
    scale = HEAD_DIM ** (-0.5)
    queries = q_in.reshape(2, tree_len, kv_local, GROUP, HEAD_DIM)
    device_id = lax.axis_index(REQ)
    q_width = q_in.shape[1]
    owners = lax.axis_size(REQ)
    marker = jnp.ones((tree_len, TAG), q_in.dtype)
    q_packet = jnp.concatenate([q_in[tree_len:], marker], axis=1)
    q_send = jnp.zeros((owners,) + q_packet.shape, q_packet.dtype)
    q_send = lax.dynamic_update_index_in_dim(q_send, q_packet, prev_owner[0], 0)
    every_query = lax.all_to_all(q_send, REQ, 0, 0, tiled=True)
    own_w = jnp.stack([w_in[0], w_in[1], w_down])
    all_w = lax.all_gather(own_w, ("z", "x"), axis=0, tiled=False)
    page_len = cache.shape[2]
    num_blocks = cache.shape[0]
    width = kv_local * HEAD_DIM
    entries = held_table.shape[1]
    entry_start = jnp.arange(entries, dtype=jnp.int32)[:, None] * page_len
    in_page = jnp.arange(page_len, dtype=jnp.int32)[None, :]
    head_eye = jnp.eye(kv_local, dtype=jnp.float32)
    rows = kv_local * GROUP * tree_len

    def attend(slot, slot_queries, first, last, state):
        running, total, accum = state
        table = held_table[slot]
        length = held_len[slot]
        page_ids = jnp.arange(first, last, dtype=jnp.int32)
        match = table[:, None] == page_ids[None, :]
        valid = (entry_start + in_page) < length
        visible = jnp.any(match[:, :, None] & valid[:, None, :], axis=0).reshape(-1)
        key_rows = cache[first:last, 0].reshape((last - first) * page_len, width)
        value_rows = cache[first:last, 1].reshape((last - first) * page_len, width)
        spread = jnp.einsum(
            "qghe,gf->ghqfe", slot_queries, head_eye.astype(slot_queries.dtype)
        ).reshape(rows, width)
        scores = (
            lax.dot_general(
                spread, key_rows, (((1,), (1,)), ((), ())), preferred_element_type=jnp.float32
            )
            * scale
        )
        scores = jnp.where(visible, scores, masked_score)
        old = running.reshape(rows)
        newest = jnp.maximum(old, jnp.max(scores, axis=-1))
        weights = jnp.where(visible, jnp.exp(scores - newest[:, None]), 0.0)
        factor = jnp.exp(old - newest)
        total = total.reshape(rows) * factor + jnp.sum(weights, axis=-1)
        high = weights.astype(jnp.bfloat16)
        low = (weights - high.astype(jnp.float32)).astype(jnp.bfloat16)
        full = jnp.dot(high, value_rows, preferred_element_type=jnp.float32) + jnp.dot(
            low, value_rows, preferred_element_type=jnp.float32
        )
        update = jnp.einsum(
            "ghqfe,gf->ghqe",
            full.reshape(kv_local, GROUP, tree_len, kv_local, HEAD_DIM),
            head_eye,
            precision=lax.Precision.HIGHEST,
        )
        accum = accum * factor.reshape(kv_local, GROUP, tree_len)[..., None] + update
        return (
            newest.reshape(kv_local, GROUP, tree_len),
            total.reshape(kv_local, GROUP, tree_len),
            accum,
        )

    stat_shape = (kv_local, GROUP, tree_len)
    start_state = (
        jnp.full(stat_shape, masked_score, jnp.float32),
        jnp.zeros(stat_shape, jnp.float32),
        jnp.zeros(stat_shape + (HEAD_DIM,), jnp.float32),
    )
    own_queries = queries[0]
    own_state = start_state
    marks = every_query[:, 0, q_width]
    senders = jnp.arange(marks.shape[0], dtype=jnp.int32)
    sender = jnp.sum(jnp.where(marks > 0.5, senders, 0))
    foreign = lax.dynamic_index_in_dim(every_query, sender, 0, keepdims=False)[:, :q_width]
    foreign = foreign.reshape(tree_len, kv_local, GROUP, HEAD_DIM)
    f_running, f_total, f_accum = attend(1, foreign, 0, num_blocks, start_state)
    f_out = f_accum / f_total[..., None]
    sent_out = jnp.transpose(f_out, (2, 0, 1, 3)).reshape(
        tree_len, kv_local * GROUP * HEAD_DIM
    )
    sent_max = jnp.transpose(f_running, (2, 0, 1)).reshape(tree_len, kv_local * GROUP)
    sent_total = jnp.transpose(f_total, (2, 0, 1)).reshape(tree_len, kv_local * GROUP)
    stats = jnp.concatenate(
        [split_hi_lo(sent_max), split_hi_lo(sent_total)], axis=1
    )
    pad = jnp.zeros((tree_len, TAG - stats.shape[1]), jnp.bfloat16)
    r_packet = jnp.concatenate([sent_out.astype(jnp.bfloat16), stats, pad], axis=1)
    r_send = jnp.zeros((owners,) + r_packet.shape, r_packet.dtype)
    r_send = lax.dynamic_update_index_in_dim(r_send, r_packet, sender, 0)
    r_send, own_state = lax.optimization_barrier((r_send, own_state))
    back = lax.all_to_all(r_send, REQ, 0, 0, tiled=True)
    running, total, accum = attend(0, own_queries, 0, num_blocks, own_state)
    all_w, running, total, accum = lax.optimization_barrier((all_w, running, total, accum))
    cache_out = accum / total[..., None]
    got = lax.dynamic_index_in_dim(back, prev_owner[0], 0, keepdims=False).astype(jnp.float32)
    heads = kv_local * GROUP
    o_w = heads * HEAD_DIM
    recv_out = got[:, :o_w].reshape(tree_len, kv_local, GROUP, HEAD_DIM)
    recv_max = (got[:, o_w : o_w + heads] + got[:, o_w + heads : o_w + 2 * heads]).reshape(
        tree_len, kv_local, GROUP
    )
    t0 = o_w + 2 * heads
    recv_total = (got[:, t0 : t0 + heads] + got[:, t0 + heads : t0 + 2 * heads]).reshape(
        tree_len, kv_local, GROUP
    )
    part_out = jnp.stack([cache_out, jnp.transpose(recv_out, (1, 2, 0, 3))])
    part_max = jnp.stack([running, jnp.transpose(recv_max, (1, 2, 0))])
    part_total = jnp.stack([total, jnp.transpose(recv_total, (1, 2, 0))])
    reach = ancestors(parents)
    live = jnp.arange(tree_len, dtype=jnp.int32)[None, :] < counts[:, None]
    allowed = ((reach > 0.5) & live[:, None, :])[:, None, None, :, :]
    draft_keys = kv_in[:, 0].reshape(2, tree_len, kv_local, HEAD_DIM)
    draft_values = kv_in[:, 1].reshape(2, tree_len, kv_local, HEAD_DIM)
    tree_scores = (
        jnp.einsum("sqghe,skge->sghqk", queries, draft_keys, preferred_element_type=jnp.float32)
        * scale
    )
    tree_scores = jnp.where(allowed, tree_scores, masked_score)
    tree_max = jnp.max(tree_scores, axis=-1)
    tree_weights = jnp.where(allowed, jnp.exp(tree_scores - tree_max[..., None]), 0.0)
    tree_total = jnp.sum(tree_weights, axis=-1)
    tree_accum = jnp.einsum(
        "sghqk,skge->sghqe",
        tree_weights,
        draft_values.astype(jnp.float32),
        precision=lax.Precision.HIGHEST,
    )
    overall = jnp.maximum(part_max, tree_max)
    cache_weight = part_total * jnp.exp(part_max - overall)
    tree_weight = jnp.exp(tree_max - overall)
    merged = (part_out * cache_weight[..., None] + tree_accum * tree_weight[..., None]) / (
        cache_weight + tree_total * tree_weight
    )[..., None]
    attended = (
        jnp.transpose(merged, (0, 3, 1, 2, 4))
        .reshape(2 * tree_len, kv_local * GROUP * HEAD_DIM)
        .astype(jnp.bfloat16)
    )
    partial_proj = jnp.dot(attended, w_out, preferred_element_type=jnp.float32)
    projected = partial_proj + lax.ppermute(partial_proj, "mlp", [(0, 1), (1, 0)])
    mixed = (resid.astype(jnp.float32) + projected).astype(jnp.bfloat16)
    normed = rms_scale(mixed, gain_mid)
    column = lax.axis_index("mlp")
    half_count = normed.shape[0] // lax.axis_size("mlp")
    ring = lax.axis_size("y")
    shifted = [normed]
    for shift in range(1, ring):
        perm = [(i, (i + shift) % ring) for i in range(ring)]
        shifted.append(lax.ppermute(normed, "y", perm))
    group_rows = jnp.concatenate(shifted, axis=0)
    dims = (((1,), (2,)), ((), ()))
    gate = lax.dot_general(group_rows, all_w[:, 0], dims, preferred_element_type=jnp.float32)
    up_part = lax.dot_general(group_rows, all_w[:, 1], dims, preferred_element_type=jnp.float32)
    hidden = (jax.nn.silu(gate) * up_part).astype(jnp.bfloat16)
    down_dims = (((1, 2), (0, 1)), ((), ()))
    partial = lax.dot_general(
        hidden, all_w[:, 2], down_dims, preferred_element_type=jnp.float32
    )
    halves = partial.reshape(ring, 2, half_count, partial.shape[1])
    mine = lax.dynamic_index_in_dim(halves, column, 1, keepdims=False)
    theirs = lax.dynamic_index_in_dim(halves, 1 - column, 1, keepdims=False)
    mine = mine + lax.ppermute(theirs, "mlp", [(0, 1), (1, 0)])
    mlp_half = mine[0]
    for shift in range(1, ring):
        perm = [(i, (i - shift) % ring) for i in range(ring)]
        mlp_half = mlp_half + lax.ppermute(mine[shift], "y", perm)
    base_half = lax.dynamic_slice_in_dim(mixed, column * half_count, half_count, 0)
    out_half = (base_half.astype(jnp.float32) + mlp_half).astype(jnp.bfloat16)
    hidden_out = lax.all_gather(out_half, "mlp", axis=0, tiled=True)
    next_normed = rms_scale(hidden_out, gain_next)
    next_qkv = jnp.dot(next_normed, w_next, preferred_element_type=jnp.float32).astype(jnp.bfloat16)
    accepted = compact_path(reach, accept_leaf, kv_in.reshape(2, tree_len, 2 * kv_width))
    accepted_kv = accepted.reshape(2 * tree_len, 2, kv_width)
    return (hidden_out, next_qkv, accepted_kv)


def solution(mesh):
    devices = mesh.devices
    owners = devices.shape[0]
    lines = round(owners ** (1 / 3))
    sub_mesh = Mesh(
        devices.reshape(owners // (lines * lines), lines, lines, devices.shape[1]),
        ("z", "x", "y", "mlp"),
    )
    R = REQ
    placed = (
        P(R, None),
        P(R, "mlp"),
        P(R, None, "mlp"),
        P(R, None),
        P(R),
        P(R),
        P(R, None, None, "mlp"),
        P(R, None),
        P(R),
        P(R),
        P("mlp", None),
        P(),
        P(None, R + ("mlp",), None),
        P(R + ("mlp",), None),
        P(),
        P(None, "mlp"),
    )
    return jax.shard_map(
        per_device,
        mesh=sub_mesh,
        in_specs=placed,
        out_specs=(P(R, None), P(R, "mlp"), P(R, None, "mlp")),
        check_vma=False,
    )
```

```python
import math

import jax
import jax.numpy as jnp
from jax import lax
from jax.sharding import Mesh, PartitionSpec as P

HEAD_DIM = 64
GROUP = 4


TAG = 128
REQ = ("z", "x", "y")

norm_eps = 1e-05
masked_score = -1e30


def route(packet, dest, mark):
    plane = lax.axis_size("x") * lax.axis_size("y")
    first = jnp.zeros((lax.axis_size("z"),) + packet.shape, packet.dtype)
    first = lax.dynamic_update_index_in_dim(first, packet, dest // plane, 0)
    middle = lax.all_to_all(first, "z", 0, 0, tiled=True)
    real = middle[:, 0, mark] > 0.5
    target = middle[:, 0, mark + 1].astype(jnp.int32) % plane
    spots = jnp.arange(plane, dtype=jnp.int32)
    pick = (target[None, :] == spots[:, None]) & real[None, :]
    second = jnp.sum(jnp.where(pick[:, :, None, None], middle[None], 0), axis=1)
    second = second.astype(packet.dtype)
    arrived = lax.all_to_all(second, ("x", "y"), 0, 0, tiled=True)
    return jnp.sum(arrived.astype(jnp.float32), axis=0).astype(packet.dtype)


def split_hi_lo(values):
    high = values.astype(jnp.bfloat16)
    low = (values - high.astype(jnp.float32)).astype(jnp.bfloat16)
    return jnp.concatenate([high, low], axis=1)


def ancestors(parents):
    count_nodes = parents.shape[-1]
    nodes = jnp.arange(count_nodes, dtype=jnp.int32)
    reach = (parents[..., :, None] == nodes).astype(jnp.float32) + jnp.eye(
        count_nodes, dtype=jnp.float32
    )
    for step in range(count_nodes.bit_length()):
        reach = jnp.minimum(
            jnp.einsum("sij,sjk->sik", reach, reach, precision=lax.Precision.HIGHEST), 1.0
        )
    return reach


def rms_scale(rows, gain):
    values = rows.astype(jnp.float32)
    factor = lax.rsqrt(jnp.mean(values * values, axis=-1, keepdims=True) + norm_eps)
    return (values * factor * gain.astype(jnp.float32)).astype(jnp.bfloat16)


def swiglu_rows(rows, w_in, w_down):
    dims = (((1,), (1,)), ((), ()))
    gate = lax.dot_general(rows, w_in[0], dims, preferred_element_type=jnp.float32)
    up_part = lax.dot_general(rows, w_in[1], dims, preferred_element_type=jnp.float32)
    hidden = (jax.nn.silu(gate) * up_part).astype(jnp.bfloat16)
    return jnp.dot(hidden, w_down, preferred_element_type=jnp.float32)


def compact_path(reach, leaves, rows):
    count_nodes = reach.shape[-1]
    nodes = jnp.arange(count_nodes, dtype=jnp.int32)
    leaf_hot = (nodes[None, :] == leaves[:, None]).astype(jnp.float32)
    path = jnp.einsum("si,sij->sj", leaf_hot, reach, precision=lax.Precision.HIGHEST)
    ranks = jnp.cumsum(path, axis=1) - path
    places = nodes.astype(jnp.float32)
    select = path[:, None, :] * (ranks[:, None, :] == places[None, :, None]).astype(jnp.float32)
    return jnp.einsum(
        "spj,sjw->spw", select.astype(jnp.bfloat16), rows, preferred_element_type=jnp.float32
    ).astype(jnp.bfloat16)


def per_device(
    resid,
    q_in,
    kv_in,
    parents,
    counts,
    accept_leaf,
    cache,
    held_table,
    held_len,
    prev_owner,
    w_out,
    gain_mid,
    w_in,
    w_down,
    gain_next,
    w_next,
):
    tree_len = parents.shape[1]
    kv_width = kv_in.shape[2]
    kv_local = kv_width // HEAD_DIM
    scale = HEAD_DIM ** (-0.5)
    queries = q_in.reshape(2, tree_len, kv_local, GROUP, HEAD_DIM)
    device_id = lax.axis_index(REQ)
    q_width = q_in.shape[1]
    q_tags = jnp.zeros((tree_len, TAG), jnp.float32)
    q_tags = q_tags.at[:, 0].set(1.0).at[:, 1].set(prev_owner[0]).at[:, 2].set(device_id)
    q_packet = jnp.concatenate([q_in[tree_len:], q_tags.astype(q_in.dtype)], axis=1)
    every_query = route(q_packet, prev_owner[0], q_width)
    own_w = jnp.stack([w_in[0], w_in[1], w_down])
    all_w = lax.all_gather(own_w, ("z", "x"), axis=0, tiled=False)
    page_len = cache.shape[2]
    num_blocks = cache.shape[0]
    width = kv_local * HEAD_DIM
    entries = held_table.shape[1]
    entry_start = jnp.arange(entries, dtype=jnp.int32)[:, None] * page_len
    in_page = jnp.arange(page_len, dtype=jnp.int32)[None, :]
    head_eye = jnp.eye(kv_local, dtype=jnp.float32)
    rows = kv_local * GROUP * tree_len

    def attend(slot, slot_queries, first, last, state):
        running, total, accum = state
        table = held_table[slot]
        length = held_len[slot]
        page_ids = jnp.arange(first, last, dtype=jnp.int32)
        match = table[:, None] == page_ids[None, :]
        valid = (entry_start + in_page) < length
        visible = jnp.any(match[:, :, None] & valid[:, None, :], axis=0).reshape(-1)
        key_rows = cache[first:last, 0].reshape((last - first) * page_len, width)
        value_rows = cache[first:last, 1].reshape((last - first) * page_len, width)
        spread = jnp.einsum(
            "qghe,gf->ghqfe", slot_queries, head_eye.astype(slot_queries.dtype)
        ).reshape(rows, width)
        scores = (
            lax.dot_general(
                spread, key_rows, (((1,), (1,)), ((), ())), preferred_element_type=jnp.float32
            )
            * scale
        )
        scores = jnp.where(visible, scores, masked_score)
        old = running.reshape(rows)
        newest = jnp.maximum(old, jnp.max(scores, axis=-1))
        weights = jnp.where(visible, jnp.exp(scores - newest[:, None]), 0.0)
        factor = jnp.exp(old - newest)
        total = total.reshape(rows) * factor + jnp.sum(weights, axis=-1)
        high = weights.astype(jnp.bfloat16)
        low = (weights - high.astype(jnp.float32)).astype(jnp.bfloat16)
        full = jnp.dot(high, value_rows, preferred_element_type=jnp.float32) + jnp.dot(
            low, value_rows, preferred_element_type=jnp.float32
        )
        update = jnp.einsum(
            "ghqfe,gf->ghqe",
            full.reshape(kv_local, GROUP, tree_len, kv_local, HEAD_DIM),
            head_eye,
            precision=lax.Precision.HIGHEST,
        )
        accum = accum * factor.reshape(kv_local, GROUP, tree_len)[..., None] + update
        return (
            newest.reshape(kv_local, GROUP, tree_len),
            total.reshape(kv_local, GROUP, tree_len),
            accum,
        )

    stat_shape = (kv_local, GROUP, tree_len)
    start_state = (
        jnp.full(stat_shape, masked_score, jnp.float32),
        jnp.zeros(stat_shape, jnp.float32),
        jnp.zeros(stat_shape + (HEAD_DIM,), jnp.float32),
    )
    own_queries = queries[0]
    own_state = start_state
    sender = every_query[0, q_width + 2].astype(jnp.int32)
    foreign = every_query[:, :q_width]
    foreign = foreign.reshape(tree_len, kv_local, GROUP, HEAD_DIM)
    f_running, f_total, f_accum = attend(1, foreign, 0, num_blocks, start_state)
    f_out = f_accum / f_total[..., None]
    sent_out = jnp.transpose(f_out, (2, 0, 1, 3)).reshape(
        tree_len, kv_local * GROUP * HEAD_DIM
    )
    sent_max = jnp.transpose(f_running, (2, 0, 1)).reshape(tree_len, kv_local * GROUP)
    sent_total = jnp.transpose(f_total, (2, 0, 1)).reshape(tree_len, kv_local * GROUP)
    stats = jnp.concatenate(
        [split_hi_lo(sent_max), split_hi_lo(sent_total)], axis=1
    )
    r_tags = jnp.zeros((tree_len, TAG - stats.shape[1]), jnp.float32)
    r_tags = r_tags.at[:, 0].set(1.0).at[:, 1].set(sender)
    r_packet = jnp.concatenate(
        [sent_out.astype(jnp.bfloat16), stats, r_tags.astype(jnp.bfloat16)], axis=1
    )
    r_packet, own_state = lax.optimization_barrier((r_packet, own_state))
    got = route(r_packet, sender, sent_out.shape[1] + stats.shape[1]).astype(jnp.float32)
    running, total, accum = attend(0, own_queries, 0, num_blocks, own_state)
    all_w, running, total, accum = lax.optimization_barrier((all_w, running, total, accum))
    cache_out = accum / total[..., None]
    heads = kv_local * GROUP
    o_w = heads * HEAD_DIM
    recv_out = got[:, :o_w].reshape(tree_len, kv_local, GROUP, HEAD_DIM)
    recv_max = (got[:, o_w : o_w + heads] + got[:, o_w + heads : o_w + 2 * heads]).reshape(
        tree_len, kv_local, GROUP
    )
    t0 = o_w + 2 * heads
    recv_total = (got[:, t0 : t0 + heads] + got[:, t0 + heads : t0 + 2 * heads]).reshape(
        tree_len, kv_local, GROUP
    )
    part_out = jnp.stack([cache_out, jnp.transpose(recv_out, (1, 2, 0, 3))])
    part_max = jnp.stack([running, jnp.transpose(recv_max, (1, 2, 0))])
    part_total = jnp.stack([total, jnp.transpose(recv_total, (1, 2, 0))])
    reach = ancestors(parents)
    live = jnp.arange(tree_len, dtype=jnp.int32)[None, :] < counts[:, None]
    allowed = ((reach > 0.5) & live[:, None, :])[:, None, None, :, :]
    draft_keys = kv_in[:, 0].reshape(2, tree_len, kv_local, HEAD_DIM)
    draft_values = kv_in[:, 1].reshape(2, tree_len, kv_local, HEAD_DIM)
    tree_scores = (
        jnp.einsum("sqghe,skge->sghqk", queries, draft_keys, preferred_element_type=jnp.float32)
        * scale
    )
    tree_scores = jnp.where(allowed, tree_scores, masked_score)
    tree_max = jnp.max(tree_scores, axis=-1)
    tree_weights = jnp.where(allowed, jnp.exp(tree_scores - tree_max[..., None]), 0.0)
    tree_total = jnp.sum(tree_weights, axis=-1)
    tree_accum = jnp.einsum(
        "sghqk,skge->sghqe",
        tree_weights,
        draft_values.astype(jnp.float32),
        precision=lax.Precision.HIGHEST,
    )
    overall = jnp.maximum(part_max, tree_max)
    cache_weight = part_total * jnp.exp(part_max - overall)
    tree_weight = jnp.exp(tree_max - overall)
    merged = (part_out * cache_weight[..., None] + tree_accum * tree_weight[..., None]) / (
        cache_weight + tree_total * tree_weight
    )[..., None]
    attended = (
        jnp.transpose(merged, (0, 3, 1, 2, 4))
        .reshape(2 * tree_len, kv_local * GROUP * HEAD_DIM)
        .astype(jnp.bfloat16)
    )
    partial_proj = jnp.dot(attended, w_out, preferred_element_type=jnp.float32)
    projected = partial_proj + lax.ppermute(partial_proj, "mlp", [(0, 1), (1, 0)])
    mixed = (resid.astype(jnp.float32) + projected).astype(jnp.bfloat16)
    normed = rms_scale(mixed, gain_mid)
    column = lax.axis_index("mlp")
    half_count = normed.shape[0] // lax.axis_size("mlp")
    ring = lax.axis_size("y")
    shifted = [normed]
    for shift in range(1, ring):
        perm = [(i, (i + shift) % ring) for i in range(ring)]
        shifted.append(lax.ppermute(normed, "y", perm))
    group_rows = jnp.concatenate(shifted, axis=0)
    dims = (((1,), (2,)), ((), ()))
    gate = lax.dot_general(group_rows, all_w[:, 0], dims, preferred_element_type=jnp.float32)
    up_part = lax.dot_general(group_rows, all_w[:, 1], dims, preferred_element_type=jnp.float32)
    hidden = (jax.nn.silu(gate) * up_part).astype(jnp.bfloat16)
    down_dims = (((1, 2), (0, 1)), ((), ()))
    partial = lax.dot_general(
        hidden, all_w[:, 2], down_dims, preferred_element_type=jnp.float32
    )
    halves = partial.reshape(ring, 2, half_count, partial.shape[1])
    mine = lax.dynamic_index_in_dim(halves, column, 1, keepdims=False)
    theirs = lax.dynamic_index_in_dim(halves, 1 - column, 1, keepdims=False)
    mine = mine + lax.ppermute(theirs, "mlp", [(0, 1), (1, 0)])
    mlp_half = mine[0]
    for shift in range(1, ring):
        perm = [(i, (i - shift) % ring) for i in range(ring)]
        mlp_half = mlp_half + lax.ppermute(mine[shift], "y", perm)
    base_half = lax.dynamic_slice_in_dim(mixed, column * half_count, half_count, 0)
    out_half = (base_half.astype(jnp.float32) + mlp_half).astype(jnp.bfloat16)
    hidden_out = lax.all_gather(out_half, "mlp", axis=0, tiled=True)
    next_normed = rms_scale(hidden_out, gain_next)
    next_qkv = jnp.dot(next_normed, w_next, preferred_element_type=jnp.float32).astype(jnp.bfloat16)
    accepted = compact_path(reach, accept_leaf, kv_in.reshape(2, tree_len, 2 * kv_width))
    accepted_kv = accepted.reshape(2 * tree_len, 2, kv_width)
    return (hidden_out, next_qkv, accepted_kv)


def solution(mesh):
    devices = mesh.devices
    owners = devices.shape[0]
    lines = round(owners ** (1 / 3))
    sub_mesh = Mesh(
        devices.reshape(owners // (lines * lines), lines, lines, devices.shape[1]),
        ("z", "x", "y", "mlp"),
    )
    R = REQ
    placed = (
        P(R, None),
        P(R, "mlp"),
        P(R, None, "mlp"),
        P(R, None),
        P(R),
        P(R),
        P(R, None, None, "mlp"),
        P(R, None),
        P(R),
        P(R),
        P("mlp", None),
        P(),
        P(None, R + ("mlp",), None),
        P(R + ("mlp",), None),
        P(),
        P(None, "mlp"),
    )
    return jax.shard_map(
        per_device,
        mesh=sub_mesh,
        in_specs=placed,
        out_specs=(P(R, None), P(R, "mlp"), P(R, None, "mlp")),
        check_vma=False,
    )
```

```python
import math

import jax
import jax.numpy as jnp
from jax import lax
from jax.sharding import Mesh, PartitionSpec as P

HEAD_DIM = 64
GROUP = 4


TAG = 128
REQ = ("z", "x", "y")

norm_eps = 1e-05
masked_score = -1e30


def route(packet, dest, mark):
    plane = lax.axis_size("x") * lax.axis_size("y")
    first = jnp.zeros((lax.axis_size("z"),) + packet.shape, packet.dtype)
    first = lax.dynamic_update_index_in_dim(first, packet, dest // plane, 0)
    middle = lax.all_to_all(first, "z", 0, 0, tiled=True)
    real = middle[:, 0, mark] > 0.5
    target = middle[:, 0, mark + 1].astype(jnp.int32) % plane
    spots = jnp.arange(plane, dtype=jnp.int32)
    pick = (target[None, :] == spots[:, None]) & real[None, :]
    second = jnp.sum(jnp.where(pick[:, :, None, None], middle[None], 0), axis=1)
    second = second.astype(packet.dtype)
    arrived = lax.all_to_all(second, ("x", "y"), 0, 0, tiled=True)
    return jnp.sum(arrived.astype(jnp.float32), axis=0).astype(packet.dtype)


def split_hi_lo(values):
    high = values.astype(jnp.bfloat16)
    low = (values - high.astype(jnp.float32)).astype(jnp.bfloat16)
    return jnp.concatenate([high, low], axis=1)


def ancestors(parents):
    count_nodes = parents.shape[-1]
    nodes = jnp.arange(count_nodes, dtype=jnp.int32)
    reach = (parents[..., :, None] == nodes).astype(jnp.float32) + jnp.eye(
        count_nodes, dtype=jnp.float32
    )
    for step in range(count_nodes.bit_length()):
        reach = jnp.minimum(
            jnp.einsum(
                "sij,sjk->sik",
                reach.astype(jnp.bfloat16),
                reach.astype(jnp.bfloat16),
                preferred_element_type=jnp.float32,
            ),
            1.0,
        )
    return reach


def rms_scale(rows, gain):
    values = rows.astype(jnp.float32)
    factor = lax.rsqrt(jnp.mean(values * values, axis=-1, keepdims=True) + norm_eps)
    return (values * factor * gain.astype(jnp.float32)).astype(jnp.bfloat16)


def swiglu_rows(rows, w_in, w_down):
    dims = (((1,), (1,)), ((), ()))
    gate = lax.dot_general(rows, w_in[0], dims, preferred_element_type=jnp.float32)
    up_part = lax.dot_general(rows, w_in[1], dims, preferred_element_type=jnp.float32)
    hidden = (jax.nn.silu(gate) * up_part).astype(jnp.bfloat16)
    return jnp.dot(hidden, w_down, preferred_element_type=jnp.float32)


def compact_path(reach, leaves, rows):
    count_nodes = reach.shape[-1]
    nodes = jnp.arange(count_nodes, dtype=jnp.int32)
    leaf_hot = (nodes[None, :] == leaves[:, None]).astype(jnp.float32)
    path = jnp.einsum(
        "si,sij->sj",
        leaf_hot.astype(jnp.bfloat16),
        reach.astype(jnp.bfloat16),
        preferred_element_type=jnp.float32,
    )
    ranks = jnp.cumsum(path, axis=1) - path
    places = nodes.astype(jnp.float32)
    select = path[:, None, :] * (ranks[:, None, :] == places[None, :, None]).astype(jnp.float32)
    return jnp.einsum(
        "spj,sjw->spw", select.astype(jnp.bfloat16), rows, preferred_element_type=jnp.float32
    ).astype(jnp.bfloat16)


def per_device(
    resid,
    q_in,
    kv_in,
    parents,
    counts,
    accept_leaf,
    cache,
    held_table,
    held_len,
    prev_owner,
    w_out,
    gain_mid,
    w_in,
    w_down,
    gain_next,
    w_next,
):
    tree_len = parents.shape[1]
    kv_width = kv_in.shape[2]
    kv_local = kv_width // HEAD_DIM
    scale = HEAD_DIM ** (-0.5)
    queries = q_in.reshape(2, tree_len, kv_local, GROUP, HEAD_DIM)
    device_id = lax.axis_index(REQ)
    q_width = q_in.shape[1]
    q_tags = jnp.zeros((tree_len, TAG), jnp.float32)
    q_tags = q_tags.at[:, 0].set(1.0).at[:, 1].set(prev_owner[0]).at[:, 2].set(device_id)
    q_packet = jnp.concatenate([q_in[tree_len:], q_tags.astype(q_in.dtype)], axis=1)
    every_query = route(q_packet, prev_owner[0], q_width)
    own_w = jnp.stack([w_in[0], w_in[1], w_down])
    all_w = lax.all_gather(own_w, ("z", "x"), axis=0, tiled=False)
    page_len = cache.shape[2]
    num_blocks = cache.shape[0]
    width = kv_local * HEAD_DIM
    entries = held_table.shape[1]
    entry_start = jnp.arange(entries, dtype=jnp.int32)[:, None] * page_len
    in_page = jnp.arange(page_len, dtype=jnp.int32)[None, :]
    head_eye = jnp.eye(kv_local, dtype=jnp.float32)
    rows = kv_local * GROUP * tree_len

    def attend(slot, slot_queries, first, last, state):
        running, total, accum = state
        table = held_table[slot]
        length = held_len[slot]
        page_ids = jnp.arange(first, last, dtype=jnp.int32)
        match = table[:, None] == page_ids[None, :]
        valid = (entry_start + in_page) < length
        visible = jnp.any(match[:, :, None] & valid[:, None, :], axis=0).reshape(-1)
        key_rows = cache[first:last, 0].reshape((last - first) * page_len, width)
        value_rows = cache[first:last, 1].reshape((last - first) * page_len, width)
        spread = jnp.einsum(
            "qghe,gf->ghqfe", slot_queries, head_eye.astype(slot_queries.dtype)
        ).reshape(rows, width)
        scores = (
            lax.dot_general(
                spread, key_rows, (((1,), (1,)), ((), ())), preferred_element_type=jnp.float32
            )
            * scale
        )
        scores = jnp.where(visible, scores, masked_score)
        old = running.reshape(rows)
        newest = jnp.maximum(old, jnp.max(scores, axis=-1))
        weights = jnp.where(visible, jnp.exp(scores - newest[:, None]), 0.0)
        factor = jnp.exp(old - newest)
        total = total.reshape(rows) * factor + jnp.sum(weights, axis=-1)
        high = weights.astype(jnp.bfloat16)
        low = (weights - high.astype(jnp.float32)).astype(jnp.bfloat16)
        full = jnp.dot(high, value_rows, preferred_element_type=jnp.float32) + jnp.dot(
            low, value_rows, preferred_element_type=jnp.float32
        )
        blocks = full.reshape(kv_local, GROUP, tree_len, kv_local, HEAD_DIM)
        update = jnp.stack([blocks[g, :, :, g] for g in range(kv_local)])
        accum = accum * factor.reshape(kv_local, GROUP, tree_len)[..., None] + update
        return (
            newest.reshape(kv_local, GROUP, tree_len),
            total.reshape(kv_local, GROUP, tree_len),
            accum,
        )

    stat_shape = (kv_local, GROUP, tree_len)
    start_state = (
        jnp.full(stat_shape, masked_score, jnp.float32),
        jnp.zeros(stat_shape, jnp.float32),
        jnp.zeros(stat_shape + (HEAD_DIM,), jnp.float32),
    )
    own_queries = queries[0]
    own_state = start_state
    sender = every_query[0, q_width + 2].astype(jnp.int32)
    foreign = every_query[:, :q_width]
    foreign = foreign.reshape(tree_len, kv_local, GROUP, HEAD_DIM)
    f_running, f_total, f_accum = attend(1, foreign, 0, num_blocks, start_state)
    f_out = f_accum / f_total[..., None]
    sent_out = jnp.transpose(f_out, (2, 0, 1, 3)).reshape(
        tree_len, kv_local * GROUP * HEAD_DIM
    )
    sent_max = jnp.transpose(f_running, (2, 0, 1)).reshape(tree_len, kv_local * GROUP)
    sent_total = jnp.transpose(f_total, (2, 0, 1)).reshape(tree_len, kv_local * GROUP)
    stats = jnp.concatenate(
        [split_hi_lo(sent_max), split_hi_lo(sent_total)], axis=1
    )
    r_tags = jnp.zeros((tree_len, TAG - stats.shape[1]), jnp.float32)
    r_tags = r_tags.at[:, 0].set(1.0).at[:, 1].set(sender)
    r_packet = jnp.concatenate(
        [sent_out.astype(jnp.bfloat16), stats, r_tags.astype(jnp.bfloat16)], axis=1
    )
    r_packet, own_state = lax.optimization_barrier((r_packet, own_state))
    got = route(r_packet, sender, sent_out.shape[1] + stats.shape[1]).astype(jnp.float32)
    running, total, accum = attend(0, own_queries, 0, num_blocks, own_state)
    all_w, running, total, accum = lax.optimization_barrier((all_w, running, total, accum))
    cache_out = accum / total[..., None]
    heads = kv_local * GROUP
    o_w = heads * HEAD_DIM
    recv_out = got[:, :o_w].reshape(tree_len, kv_local, GROUP, HEAD_DIM)
    recv_max = (got[:, o_w : o_w + heads] + got[:, o_w + heads : o_w + 2 * heads]).reshape(
        tree_len, kv_local, GROUP
    )
    t0 = o_w + 2 * heads
    recv_total = (got[:, t0 : t0 + heads] + got[:, t0 + heads : t0 + 2 * heads]).reshape(
        tree_len, kv_local, GROUP
    )
    part_out = jnp.stack([cache_out, jnp.transpose(recv_out, (1, 2, 0, 3))])
    part_max = jnp.stack([running, jnp.transpose(recv_max, (1, 2, 0))])
    part_total = jnp.stack([total, jnp.transpose(recv_total, (1, 2, 0))])
    reach = ancestors(parents)
    live = jnp.arange(tree_len, dtype=jnp.int32)[None, :] < counts[:, None]
    allowed = ((reach > 0.5) & live[:, None, :])[:, None, None, :, :]
    draft_keys = kv_in[:, 0].reshape(2, tree_len, kv_local, HEAD_DIM)
    draft_values = kv_in[:, 1].reshape(2, tree_len, kv_local, HEAD_DIM)
    tree_scores = (
        jnp.einsum("sqghe,skge->sghqk", queries, draft_keys, preferred_element_type=jnp.float32)
        * scale
    )
    tree_scores = jnp.where(allowed, tree_scores, masked_score)
    tree_max = jnp.max(tree_scores, axis=-1)
    tree_weights = jnp.where(allowed, jnp.exp(tree_scores - tree_max[..., None]), 0.0)
    tree_total = jnp.sum(tree_weights, axis=-1)
    tree_high = tree_weights.astype(jnp.bfloat16)
    tree_low = (tree_weights - tree_high.astype(jnp.float32)).astype(jnp.bfloat16)
    tree_accum = jnp.einsum(
        "sghqk,skge->sghqe", tree_high, draft_values, preferred_element_type=jnp.float32
    ) + jnp.einsum(
        "sghqk,skge->sghqe", tree_low, draft_values, preferred_element_type=jnp.float32
    )
    overall = jnp.maximum(part_max, tree_max)
    cache_weight = part_total * jnp.exp(part_max - overall)
    tree_weight = jnp.exp(tree_max - overall)
    merged = (part_out * cache_weight[..., None] + tree_accum * tree_weight[..., None]) / (
        cache_weight + tree_total * tree_weight
    )[..., None]
    attended = (
        jnp.transpose(merged, (0, 3, 1, 2, 4))
        .reshape(2 * tree_len, kv_local * GROUP * HEAD_DIM)
        .astype(jnp.bfloat16)
    )
    partial_proj = jnp.dot(attended, w_out, preferred_element_type=jnp.float32)
    projected = partial_proj + lax.ppermute(partial_proj, "mlp", [(0, 1), (1, 0)])
    mixed = (resid.astype(jnp.float32) + projected).astype(jnp.bfloat16)
    normed = rms_scale(mixed, gain_mid)
    column = lax.axis_index("mlp")
    half_count = normed.shape[0] // lax.axis_size("mlp")
    ring = lax.axis_size("y")
    shifted = [normed]
    for shift in range(1, ring):
        perm = [(i, (i + shift) % ring) for i in range(ring)]
        shifted.append(lax.ppermute(normed, "y", perm))
    group_rows = jnp.concatenate(shifted, axis=0)
    dims = (((1,), (2,)), ((), ()))
    gate = lax.dot_general(group_rows, all_w[:, 0], dims, preferred_element_type=jnp.float32)
    up_part = lax.dot_general(group_rows, all_w[:, 1], dims, preferred_element_type=jnp.float32)
    hidden = (jax.nn.silu(gate) * up_part).astype(jnp.bfloat16)
    down_dims = (((1, 2), (0, 1)), ((), ()))
    partial = lax.dot_general(
        hidden, all_w[:, 2], down_dims, preferred_element_type=jnp.float32
    )
    halves = partial.reshape(ring, 2, half_count, partial.shape[1])
    mine = lax.dynamic_index_in_dim(halves, column, 1, keepdims=False)
    theirs = lax.dynamic_index_in_dim(halves, 1 - column, 1, keepdims=False)
    mine = mine + lax.ppermute(theirs, "mlp", [(0, 1), (1, 0)])
    mlp_half = mine[0]
    for shift in range(1, ring):
        perm = [(i, (i - shift) % ring) for i in range(ring)]
        mlp_half = mlp_half + lax.ppermute(mine[shift], "y", perm)
    base_half = lax.dynamic_slice_in_dim(mixed, column * half_count, half_count, 0)
    out_half = (base_half.astype(jnp.float32) + mlp_half).astype(jnp.bfloat16)
    hidden_out = lax.all_gather(out_half, "mlp", axis=0, tiled=True)
    next_normed = rms_scale(hidden_out, gain_next)
    next_qkv = jnp.dot(next_normed, w_next, preferred_element_type=jnp.float32).astype(jnp.bfloat16)
    accepted = compact_path(reach, accept_leaf, kv_in.reshape(2, tree_len, 2 * kv_width))
    accepted_kv = accepted.reshape(2 * tree_len, 2, kv_width)
    return (hidden_out, next_qkv, accepted_kv)


def solution(mesh):
    devices = mesh.devices
    owners = devices.shape[0]
    lines = round(owners ** (1 / 3))
    sub_mesh = Mesh(
        devices.reshape(owners // (lines * lines), lines, lines, devices.shape[1]),
        ("z", "x", "y", "mlp"),
    )
    R = REQ
    placed = (
        P(R, None),
        P(R, "mlp"),
        P(R, None, "mlp"),
        P(R, None),
        P(R),
        P(R),
        P(R, None, None, "mlp"),
        P(R, None),
        P(R),
        P(R),
        P("mlp", None),
        P(),
        P(None, R + ("mlp",), None),
        P(R + ("mlp",), None),
        P(),
        P(None, "mlp"),
    )
    return jax.shard_map(
        per_device,
        mesh=sub_mesh,
        in_specs=placed,
        out_specs=(P(R, None), P(R, "mlp"), P(R, None, "mlp")),
        check_vma=False,
    )
```

```python
import math

import jax
import jax.numpy as jnp
from jax import lax
from jax.sharding import Mesh, PartitionSpec as P

HEAD_DIM = 64
GROUP = 4


TAG = 128
REQ = ("z", "x", "y")

norm_eps = 1e-05
masked_score = -1e30


def route(packet, dest, mark):
    plane = lax.axis_size("x") * lax.axis_size("y")
    first = jnp.zeros((lax.axis_size("z"),) + packet.shape, packet.dtype)
    first = lax.dynamic_update_index_in_dim(first, packet, dest // plane, 0)
    middle = lax.all_to_all(first, "z", 0, 0, tiled=True)
    real = middle[:, 0, mark] > 0.5
    target = middle[:, 0, mark + 1].astype(jnp.int32) % plane
    spots = jnp.arange(plane, dtype=jnp.int32)
    pick = (target[None, :] == spots[:, None]) & real[None, :]
    second = jnp.sum(jnp.where(pick[:, :, None, None], middle[None], 0), axis=1)
    second = second.astype(packet.dtype)
    arrived = lax.all_to_all(second, ("x", "y"), 0, 0, tiled=True)
    return jnp.sum(arrived.astype(jnp.float32), axis=0).astype(packet.dtype)


def split_hi_lo(values):
    high = values.astype(jnp.bfloat16)
    low = (values - high.astype(jnp.float32)).astype(jnp.bfloat16)
    return jnp.concatenate([high, low], axis=1)


def ancestors(parents):
    count_nodes = parents.shape[-1]
    nodes = jnp.arange(count_nodes, dtype=jnp.int32)
    reach = (parents[..., :, None] == nodes).astype(jnp.float32) + jnp.eye(
        count_nodes, dtype=jnp.float32
    )
    for step in range(count_nodes.bit_length()):
        reach = jnp.minimum(
            jnp.einsum(
                "sij,sjk->sik",
                reach.astype(jnp.bfloat16),
                reach.astype(jnp.bfloat16),
                preferred_element_type=jnp.float32,
            ),
            1.0,
        )
    return reach


def rms_scale(rows, gain):
    values = rows.astype(jnp.float32)
    factor = lax.rsqrt(jnp.mean(values * values, axis=-1, keepdims=True) + norm_eps)
    return (values * factor * gain.astype(jnp.float32)).astype(jnp.bfloat16)


def swiglu_rows(rows, w_in, w_down):
    dims = (((1,), (1,)), ((), ()))
    gate = lax.dot_general(rows, w_in[0], dims, preferred_element_type=jnp.float32)
    up_part = lax.dot_general(rows, w_in[1], dims, preferred_element_type=jnp.float32)
    hidden = (jax.nn.silu(gate) * up_part).astype(jnp.bfloat16)
    return jnp.dot(hidden, w_down, preferred_element_type=jnp.float32)


def compact_path(reach, leaves, rows):
    count_nodes = reach.shape[-1]
    nodes = jnp.arange(count_nodes, dtype=jnp.int32)
    leaf_hot = (nodes[None, :] == leaves[:, None]).astype(jnp.float32)
    path = jnp.einsum(
        "si,sij->sj",
        leaf_hot.astype(jnp.bfloat16),
        reach.astype(jnp.bfloat16),
        preferred_element_type=jnp.float32,
    )
    ranks = jnp.cumsum(path, axis=1) - path
    places = nodes.astype(jnp.float32)
    select = path[:, None, :] * (ranks[:, None, :] == places[None, :, None]).astype(jnp.float32)
    return jnp.einsum(
        "spj,sjw->spw", select.astype(jnp.bfloat16), rows, preferred_element_type=jnp.float32
    ).astype(jnp.bfloat16)


def per_device(
    resid,
    q_in,
    kv_in,
    parents,
    counts,
    accept_leaf,
    cache,
    held_table,
    held_len,
    prev_owner,
    w_out,
    gain_mid,
    w_in,
    w_down,
    gain_next,
    w_next,
):
    tree_len = parents.shape[1]
    kv_width = kv_in.shape[2]
    kv_local = kv_width // HEAD_DIM
    scale = HEAD_DIM ** (-0.5)
    queries = q_in.reshape(2, tree_len, kv_local, GROUP, HEAD_DIM)
    device_id = lax.axis_index(REQ)
    q_width = q_in.shape[1]
    q_tags = jnp.zeros((tree_len, TAG), jnp.float32)
    q_tags = q_tags.at[:, 0].set(1.0).at[:, 1].set(prev_owner[0]).at[:, 2].set(device_id)
    q_packet = jnp.concatenate([q_in[tree_len:], q_tags.astype(q_in.dtype)], axis=1)
    every_query = route(q_packet, prev_owner[0], q_width)
    own_w = jnp.stack([w_in[0], w_in[1], w_down])
    all_w = lax.all_gather(own_w, ("z", "x"), axis=0, tiled=False)
    page_len = cache.shape[2]
    num_blocks = cache.shape[0]
    width = kv_local * HEAD_DIM
    entries = held_table.shape[1]
    entry_start = jnp.arange(entries, dtype=jnp.int32)[:, None] * page_len
    in_page = jnp.arange(page_len, dtype=jnp.int32)[None, :]
    head_eye = jnp.eye(kv_local, dtype=jnp.float32)
    rows = kv_local * GROUP * tree_len

    def attend(slot, slot_queries, first, last, state):
        running, total, accum = state
        table = held_table[slot]
        length = held_len[slot]
        page_ids = jnp.arange(first, last, dtype=jnp.int32)
        match = table[:, None] == page_ids[None, :]
        valid = (entry_start + in_page) < length
        visible = jnp.any(match[:, :, None] & valid[:, None, :], axis=0).reshape(-1)
        key_rows = cache[first:last, 0].reshape((last - first) * page_len, width)
        value_rows = cache[first:last, 1].reshape((last - first) * page_len, width)
        spread = jnp.einsum(
            "qghe,gf->ghqfe", slot_queries, head_eye.astype(slot_queries.dtype)
        ).reshape(rows, width)
        scores = (
            lax.dot_general(
                spread, key_rows, (((1,), (1,)), ((), ())), preferred_element_type=jnp.float32
            )
            * scale
        )
        scores = jnp.where(visible, scores, masked_score)
        old = running.reshape(rows)
        newest = jnp.maximum(old, jnp.max(scores, axis=-1))
        weights = jnp.where(visible, jnp.exp(scores - newest[:, None]), 0.0)
        factor = jnp.exp(old - newest)
        total = total.reshape(rows) * factor + jnp.sum(weights, axis=-1)
        full = jnp.dot(
            weights.astype(jnp.bfloat16), value_rows, preferred_element_type=jnp.float32
        )
        blocks = full.reshape(kv_local, GROUP, tree_len, kv_local, HEAD_DIM)
        update = jnp.stack([blocks[g, :, :, g] for g in range(kv_local)])
        accum = accum * factor.reshape(kv_local, GROUP, tree_len)[..., None] + update
        return (
            newest.reshape(kv_local, GROUP, tree_len),
            total.reshape(kv_local, GROUP, tree_len),
            accum,
        )

    stat_shape = (kv_local, GROUP, tree_len)
    start_state = (
        jnp.full(stat_shape, masked_score, jnp.float32),
        jnp.zeros(stat_shape, jnp.float32),
        jnp.zeros(stat_shape + (HEAD_DIM,), jnp.float32),
    )
    own_queries = queries[0]
    own_state = start_state
    sender = every_query[0, q_width + 2].astype(jnp.int32)
    foreign = every_query[:, :q_width]
    foreign = foreign.reshape(tree_len, kv_local, GROUP, HEAD_DIM)
    f_running, f_total, f_accum = attend(1, foreign, 0, num_blocks, start_state)
    f_out = f_accum / f_total[..., None]
    sent_out = jnp.transpose(f_out, (2, 0, 1, 3)).reshape(
        tree_len, kv_local * GROUP * HEAD_DIM
    )
    sent_max = jnp.transpose(f_running, (2, 0, 1)).reshape(tree_len, kv_local * GROUP)
    sent_total = jnp.transpose(f_total, (2, 0, 1)).reshape(tree_len, kv_local * GROUP)
    stats = jnp.concatenate(
        [split_hi_lo(sent_max), split_hi_lo(sent_total)], axis=1
    )
    r_tags = jnp.zeros((tree_len, TAG - stats.shape[1]), jnp.float32)
    r_tags = r_tags.at[:, 0].set(1.0).at[:, 1].set(sender)
    r_packet = jnp.concatenate(
        [sent_out.astype(jnp.bfloat16), stats, r_tags.astype(jnp.bfloat16)], axis=1
    )
    r_packet, own_state = lax.optimization_barrier((r_packet, own_state))
    got = route(r_packet, sender, sent_out.shape[1] + stats.shape[1]).astype(jnp.float32)
    running, total, accum = attend(0, own_queries, 0, num_blocks, own_state)
    all_w, running, total, accum = lax.optimization_barrier((all_w, running, total, accum))
    cache_out = accum / total[..., None]
    heads = kv_local * GROUP
    o_w = heads * HEAD_DIM
    recv_out = got[:, :o_w].reshape(tree_len, kv_local, GROUP, HEAD_DIM)
    recv_max = (got[:, o_w : o_w + heads] + got[:, o_w + heads : o_w + 2 * heads]).reshape(
        tree_len, kv_local, GROUP
    )
    t0 = o_w + 2 * heads
    recv_total = (got[:, t0 : t0 + heads] + got[:, t0 + heads : t0 + 2 * heads]).reshape(
        tree_len, kv_local, GROUP
    )
    part_out = jnp.stack([cache_out, jnp.transpose(recv_out, (1, 2, 0, 3))])
    part_max = jnp.stack([running, jnp.transpose(recv_max, (1, 2, 0))])
    part_total = jnp.stack([total, jnp.transpose(recv_total, (1, 2, 0))])
    reach = ancestors(parents)
    live = jnp.arange(tree_len, dtype=jnp.int32)[None, :] < counts[:, None]
    allowed = ((reach > 0.5) & live[:, None, :])[:, None, None, :, :]
    draft_keys = kv_in[:, 0].reshape(2, tree_len, kv_local, HEAD_DIM)
    draft_values = kv_in[:, 1].reshape(2, tree_len, kv_local, HEAD_DIM)
    tree_scores = (
        jnp.einsum("sqghe,skge->sghqk", queries, draft_keys, preferred_element_type=jnp.float32)
        * scale
    )
    tree_scores = jnp.where(allowed, tree_scores, masked_score)
    tree_max = jnp.max(tree_scores, axis=-1)
    tree_weights = jnp.where(allowed, jnp.exp(tree_scores - tree_max[..., None]), 0.0)
    tree_total = jnp.sum(tree_weights, axis=-1)
    tree_high = tree_weights.astype(jnp.bfloat16)
    tree_low = (tree_weights - tree_high.astype(jnp.float32)).astype(jnp.bfloat16)
    tree_accum = jnp.einsum(
        "sghqk,skge->sghqe", tree_high, draft_values, preferred_element_type=jnp.float32
    ) + jnp.einsum(
        "sghqk,skge->sghqe", tree_low, draft_values, preferred_element_type=jnp.float32
    )
    overall = jnp.maximum(part_max, tree_max)
    cache_weight = part_total * jnp.exp(part_max - overall)
    tree_weight = jnp.exp(tree_max - overall)
    merged = (part_out * cache_weight[..., None] + tree_accum * tree_weight[..., None]) / (
        cache_weight + tree_total * tree_weight
    )[..., None]
    attended = (
        jnp.transpose(merged, (0, 3, 1, 2, 4))
        .reshape(2 * tree_len, kv_local * GROUP * HEAD_DIM)
        .astype(jnp.bfloat16)
    )
    partial_proj = jnp.dot(attended, w_out, preferred_element_type=jnp.float32)
    projected = partial_proj + lax.ppermute(partial_proj, "mlp", [(0, 1), (1, 0)])
    mixed = (resid.astype(jnp.float32) + projected).astype(jnp.bfloat16)
    normed = rms_scale(mixed, gain_mid)
    column = lax.axis_index("mlp")
    half_count = normed.shape[0] // lax.axis_size("mlp")
    ring = lax.axis_size("y")
    shifted = [normed]
    for shift in range(1, ring):
        perm = [(i, (i + shift) % ring) for i in range(ring)]
        shifted.append(lax.ppermute(normed, "y", perm))
    group_rows = jnp.concatenate(shifted, axis=0)
    dims = (((1,), (2,)), ((), ()))
    gate = lax.dot_general(group_rows, all_w[:, 0], dims, preferred_element_type=jnp.float32)
    up_part = lax.dot_general(group_rows, all_w[:, 1], dims, preferred_element_type=jnp.float32)
    hidden = (jax.nn.silu(gate) * up_part).astype(jnp.bfloat16)
    down_dims = (((1, 2), (0, 1)), ((), ()))
    partial = lax.dot_general(
        hidden, all_w[:, 2], down_dims, preferred_element_type=jnp.float32
    )
    halves = partial.reshape(ring, 2, half_count, partial.shape[1])
    mine = lax.dynamic_index_in_dim(halves, column, 1, keepdims=False)
    theirs = lax.dynamic_index_in_dim(halves, 1 - column, 1, keepdims=False)
    mine = mine + lax.ppermute(theirs, "mlp", [(0, 1), (1, 0)])
    mlp_half = mine[0]
    for shift in range(1, ring):
        perm = [(i, (i - shift) % ring) for i in range(ring)]
        mlp_half = mlp_half + lax.ppermute(mine[shift], "y", perm)
    base_half = lax.dynamic_slice_in_dim(mixed, column * half_count, half_count, 0)
    out_half = (base_half.astype(jnp.float32) + mlp_half).astype(jnp.bfloat16)
    hidden_out = lax.all_gather(out_half, "mlp", axis=0, tiled=True)
    next_normed = rms_scale(hidden_out, gain_next)
    next_qkv = jnp.dot(next_normed, w_next, preferred_element_type=jnp.float32).astype(jnp.bfloat16)
    accepted = compact_path(reach, accept_leaf, kv_in.reshape(2, tree_len, 2 * kv_width))
    accepted_kv = accepted.reshape(2 * tree_len, 2, kv_width)
    return (hidden_out, next_qkv, accepted_kv)


def solution(mesh):
    devices = mesh.devices
    owners = devices.shape[0]
    lines = round(owners ** (1 / 3))
    sub_mesh = Mesh(
        devices.reshape(owners // (lines * lines), lines, lines, devices.shape[1]),
        ("z", "x", "y", "mlp"),
    )
    R = REQ
    placed = (
        P(R, None),
        P(R, "mlp"),
        P(R, None, "mlp"),
        P(R, None),
        P(R),
        P(R),
        P(R, None, None, "mlp"),
        P(R, None),
        P(R),
        P(R),
        P("mlp", None),
        P(),
        P(None, R + ("mlp",), None),
        P(R + ("mlp",), None),
        P(),
        P(None, "mlp"),
    )
    return jax.shard_map(
        per_device,
        mesh=sub_mesh,
        in_specs=placed,
        out_specs=(P(R, None), P(R, "mlp"), P(R, None, "mlp")),
        check_vma=False,
    )
```

```python
import math

import jax
import jax.numpy as jnp
from jax import lax
from jax.sharding import Mesh, PartitionSpec as P

HEAD_DIM = 64
GROUP = 4


TAG = 128
REQ = ("z", "x", "y")

norm_eps = 1e-05
masked_score = -1e30


def route(packet, dest, mark, carry):
    plane = lax.axis_size("x") * lax.axis_size("y")
    first = jnp.zeros((lax.axis_size("z"),) + packet.shape, packet.dtype)
    first = lax.dynamic_update_index_in_dim(first, packet, dest // plane, 0)
    middle = lax.all_to_all(first, "z", 0, 0, tiled=True)
    middle, carry = lax.optimization_barrier((middle, carry))
    real = middle[:, 0, mark] > 0.5
    target = middle[:, 0, mark + 1].astype(jnp.int32) % plane
    spots = jnp.arange(plane, dtype=jnp.int32)
    pick = (target[None, :] == spots[:, None]) & real[None, :]
    second = jnp.sum(jnp.where(pick[:, :, None, None], middle[None], 0), axis=1)
    second = second.astype(packet.dtype)
    arrived = lax.all_to_all(second, ("x", "y"), 0, 0, tiled=True)
    return jnp.sum(arrived.astype(jnp.float32), axis=0).astype(packet.dtype), carry


def split_hi_lo(values):
    high = values.astype(jnp.bfloat16)
    low = (values - high.astype(jnp.float32)).astype(jnp.bfloat16)
    return jnp.concatenate([high, low], axis=1)


def ancestors(parents):
    count_nodes = parents.shape[-1]
    nodes = jnp.arange(count_nodes, dtype=jnp.int32)
    reach = (parents[..., :, None] == nodes).astype(jnp.float32) + jnp.eye(
        count_nodes, dtype=jnp.float32
    )
    for step in range(count_nodes.bit_length()):
        reach = jnp.minimum(
            jnp.einsum(
                "sij,sjk->sik",
                reach.astype(jnp.bfloat16),
                reach.astype(jnp.bfloat16),
                preferred_element_type=jnp.float32,
            ),
            1.0,
        )
    return reach


def rms_scale(rows, gain):
    values = rows.astype(jnp.float32)
    factor = lax.rsqrt(jnp.mean(values * values, axis=-1, keepdims=True) + norm_eps)
    return (values * factor * gain.astype(jnp.float32)).astype(jnp.bfloat16)


def swiglu_rows(rows, w_in, w_down):
    dims = (((1,), (1,)), ((), ()))
    gate = lax.dot_general(rows, w_in[0], dims, preferred_element_type=jnp.float32)
    up_part = lax.dot_general(rows, w_in[1], dims, preferred_element_type=jnp.float32)
    hidden = (jax.nn.silu(gate) * up_part).astype(jnp.bfloat16)
    return jnp.dot(hidden, w_down, preferred_element_type=jnp.float32)


def compact_path(reach, leaves, rows):
    count_nodes = reach.shape[-1]
    nodes = jnp.arange(count_nodes, dtype=jnp.int32)
    leaf_hot = (nodes[None, :] == leaves[:, None]).astype(jnp.float32)
    path = jnp.einsum(
        "si,sij->sj",
        leaf_hot.astype(jnp.bfloat16),
        reach.astype(jnp.bfloat16),
        preferred_element_type=jnp.float32,
    )
    ranks = jnp.cumsum(path, axis=1) - path
    places = nodes.astype(jnp.float32)
    select = path[:, None, :] * (ranks[:, None, :] == places[None, :, None]).astype(jnp.float32)
    return jnp.einsum(
        "spj,sjw->spw", select.astype(jnp.bfloat16), rows, preferred_element_type=jnp.float32
    ).astype(jnp.bfloat16)


def per_device(
    resid,
    q_in,
    kv_in,
    parents,
    counts,
    accept_leaf,
    cache,
    held_table,
    held_len,
    prev_owner,
    w_out,
    gain_mid,
    w_in,
    w_down,
    gain_next,
    w_next,
):
    tree_len = parents.shape[1]
    kv_width = kv_in.shape[2]
    kv_local = kv_width // HEAD_DIM
    scale = HEAD_DIM ** (-0.5)
    queries = q_in.reshape(2, tree_len, kv_local, GROUP, HEAD_DIM)
    device_id = lax.axis_index(REQ)
    q_width = q_in.shape[1]
    q_tags = jnp.zeros((tree_len, TAG), jnp.float32)
    q_tags = q_tags.at[:, 0].set(1.0).at[:, 1].set(prev_owner[0]).at[:, 2].set(device_id)
    q_packet = jnp.concatenate([q_in[tree_len:], q_tags.astype(q_in.dtype)], axis=1)
    every_query, _ = route(q_packet, prev_owner[0], q_width, q_width)
    own_w = jnp.stack([w_in[0], w_in[1], w_down])
    all_w = lax.all_gather(own_w, ("z", "x"), axis=0, tiled=False)
    page_len = cache.shape[2]
    num_blocks = cache.shape[0]
    width = kv_local * HEAD_DIM
    entries = held_table.shape[1]
    entry_start = jnp.arange(entries, dtype=jnp.int32)[:, None] * page_len
    in_page = jnp.arange(page_len, dtype=jnp.int32)[None, :]
    head_eye = jnp.eye(kv_local, dtype=jnp.float32)
    rows = kv_local * GROUP * tree_len

    def attend(slot, slot_queries, first, last, state):
        running, total, accum = state
        table = held_table[slot]
        length = held_len[slot]
        page_ids = jnp.arange(first, last, dtype=jnp.int32)
        match = table[:, None] == page_ids[None, :]
        valid = (entry_start + in_page) < length
        visible = jnp.any(match[:, :, None] & valid[:, None, :], axis=0).reshape(-1)
        key_rows = cache[first:last, 0].reshape((last - first) * page_len, width)
        value_rows = cache[first:last, 1].reshape((last - first) * page_len, width)
        spread = jnp.einsum(
            "qghe,gf->ghqfe", slot_queries, head_eye.astype(slot_queries.dtype)
        ).reshape(rows, width)
        scores = (
            lax.dot_general(
                spread, key_rows, (((1,), (1,)), ((), ())), preferred_element_type=jnp.float32
            )
            * scale
        )
        scores = jnp.where(visible, scores, masked_score)
        old = running.reshape(rows)
        newest = jnp.maximum(old, jnp.max(scores, axis=-1))
        weights = jnp.where(visible, jnp.exp(scores - newest[:, None]), 0.0)
        factor = jnp.exp(old - newest)
        total = total.reshape(rows) * factor + jnp.sum(weights, axis=-1)
        high = weights.astype(jnp.bfloat16)
        low = (weights - high.astype(jnp.float32)).astype(jnp.bfloat16)
        full = jnp.dot(high, value_rows, preferred_element_type=jnp.float32) + jnp.dot(
            low, value_rows, preferred_element_type=jnp.float32
        )
        blocks = full.reshape(kv_local, GROUP, tree_len, kv_local, HEAD_DIM)
        update = jnp.stack([blocks[g, :, :, g] for g in range(kv_local)])
        accum = accum * factor.reshape(kv_local, GROUP, tree_len)[..., None] + update
        return (
            newest.reshape(kv_local, GROUP, tree_len),
            total.reshape(kv_local, GROUP, tree_len),
            accum,
        )

    stat_shape = (kv_local, GROUP, tree_len)
    start_state = (
        jnp.full(stat_shape, masked_score, jnp.float32),
        jnp.zeros(stat_shape, jnp.float32),
        jnp.zeros(stat_shape + (HEAD_DIM,), jnp.float32),
    )
    own_queries = queries[0]
    own_state = start_state
    sender = every_query[0, q_width + 2].astype(jnp.int32)
    foreign = every_query[:, :q_width]
    foreign = foreign.reshape(tree_len, kv_local, GROUP, HEAD_DIM)
    f_running, f_total, f_accum = attend(1, foreign, 0, num_blocks, start_state)
    f_out = f_accum / f_total[..., None]
    sent_out = jnp.transpose(f_out, (2, 0, 1, 3)).reshape(
        tree_len, kv_local * GROUP * HEAD_DIM
    )
    sent_max = jnp.transpose(f_running, (2, 0, 1)).reshape(tree_len, kv_local * GROUP)
    sent_total = jnp.transpose(f_total, (2, 0, 1)).reshape(tree_len, kv_local * GROUP)
    stats = jnp.concatenate(
        [split_hi_lo(sent_max), split_hi_lo(sent_total)], axis=1
    )
    r_tags = jnp.zeros((tree_len, TAG - stats.shape[1]), jnp.float32)
    r_tags = r_tags.at[:, 0].set(1.0).at[:, 1].set(sender)
    r_packet = jnp.concatenate(
        [sent_out.astype(jnp.bfloat16), stats, r_tags.astype(jnp.bfloat16)], axis=1
    )
    r_packet, own_state = lax.optimization_barrier((r_packet, own_state))
    half = num_blocks // 2
    own_state = attend(0, own_queries, 0, half, own_state)
    got, own_state = route(r_packet, sender, sent_out.shape[1] + stats.shape[1], own_state)
    got = got.astype(jnp.float32)
    running, total, accum = attend(0, own_queries, half, num_blocks, own_state)
    all_w, running, total, accum = lax.optimization_barrier((all_w, running, total, accum))
    cache_out = accum / total[..., None]
    heads = kv_local * GROUP
    o_w = heads * HEAD_DIM
    recv_out = got[:, :o_w].reshape(tree_len, kv_local, GROUP, HEAD_DIM)
    recv_max = (got[:, o_w : o_w + heads] + got[:, o_w + heads : o_w + 2 * heads]).reshape(
        tree_len, kv_local, GROUP
    )
    t0 = o_w + 2 * heads
    recv_total = (got[:, t0 : t0 + heads] + got[:, t0 + heads : t0 + 2 * heads]).reshape(
        tree_len, kv_local, GROUP
    )
    part_out = jnp.stack([cache_out, jnp.transpose(recv_out, (1, 2, 0, 3))])
    part_max = jnp.stack([running, jnp.transpose(recv_max, (1, 2, 0))])
    part_total = jnp.stack([total, jnp.transpose(recv_total, (1, 2, 0))])
    reach = ancestors(parents)
    live = jnp.arange(tree_len, dtype=jnp.int32)[None, :] < counts[:, None]
    allowed = ((reach > 0.5) & live[:, None, :])[:, None, None, :, :]
    draft_keys = kv_in[:, 0].reshape(2, tree_len, kv_local, HEAD_DIM)
    draft_values = kv_in[:, 1].reshape(2, tree_len, kv_local, HEAD_DIM)
    tree_scores = (
        jnp.einsum("sqghe,skge->sghqk", queries, draft_keys, preferred_element_type=jnp.float32)
        * scale
    )
    tree_scores = jnp.where(allowed, tree_scores, masked_score)
    tree_max = jnp.max(tree_scores, axis=-1)
    tree_weights = jnp.where(allowed, jnp.exp(tree_scores - tree_max[..., None]), 0.0)
    tree_total = jnp.sum(tree_weights, axis=-1)
    tree_high = tree_weights.astype(jnp.bfloat16)
    tree_low = (tree_weights - tree_high.astype(jnp.float32)).astype(jnp.bfloat16)
    tree_accum = jnp.einsum(
        "sghqk,skge->sghqe", tree_high, draft_values, preferred_element_type=jnp.float32
    ) + jnp.einsum(
        "sghqk,skge->sghqe", tree_low, draft_values, preferred_element_type=jnp.float32
    )
    overall = jnp.maximum(part_max, tree_max)
    cache_weight = part_total * jnp.exp(part_max - overall)
    tree_weight = jnp.exp(tree_max - overall)
    merged = (part_out * cache_weight[..., None] + tree_accum * tree_weight[..., None]) / (
        cache_weight + tree_total * tree_weight
    )[..., None]
    attended = (
        jnp.transpose(merged, (0, 3, 1, 2, 4))
        .reshape(2 * tree_len, kv_local * GROUP * HEAD_DIM)
        .astype(jnp.bfloat16)
    )
    partial_proj = jnp.dot(attended, w_out, preferred_element_type=jnp.float32)
    projected = partial_proj + lax.ppermute(partial_proj, "mlp", [(0, 1), (1, 0)])
    mixed = (resid.astype(jnp.float32) + projected).astype(jnp.bfloat16)
    normed = rms_scale(mixed, gain_mid)
    column = lax.axis_index("mlp")
    half_count = normed.shape[0] // lax.axis_size("mlp")
    ring = lax.axis_size("y")
    shifted = [normed]
    for shift in range(1, ring):
        perm = [(i, (i + shift) % ring) for i in range(ring)]
        shifted.append(lax.ppermute(normed, "y", perm))
    group_rows = jnp.concatenate(shifted, axis=0)
    dims = (((1,), (2,)), ((), ()))
    gate = lax.dot_general(group_rows, all_w[:, 0], dims, preferred_element_type=jnp.float32)
    up_part = lax.dot_general(group_rows, all_w[:, 1], dims, preferred_element_type=jnp.float32)
    hidden = (jax.nn.silu(gate) * up_part).astype(jnp.bfloat16)
    down_dims = (((1, 2), (0, 1)), ((), ()))
    partial = lax.dot_general(
        hidden, all_w[:, 2], down_dims, preferred_element_type=jnp.float32
    )
    halves = partial.reshape(ring, 2, half_count, partial.shape[1])
    mine = lax.dynamic_index_in_dim(halves, column, 1, keepdims=False)
    theirs = lax.dynamic_index_in_dim(halves, 1 - column, 1, keepdims=False)
    mine = mine + lax.ppermute(theirs, "mlp", [(0, 1), (1, 0)])
    mlp_half = mine[0]
    for shift in range(1, ring):
        perm = [(i, (i - shift) % ring) for i in range(ring)]
        mlp_half = mlp_half + lax.ppermute(mine[shift], "y", perm)
    base_half = lax.dynamic_slice_in_dim(mixed, column * half_count, half_count, 0)
    out_half = (base_half.astype(jnp.float32) + mlp_half).astype(jnp.bfloat16)
    hidden_out = lax.all_gather(out_half, "mlp", axis=0, tiled=True)
    next_normed = rms_scale(hidden_out, gain_next)
    next_qkv = jnp.dot(next_normed, w_next, preferred_element_type=jnp.float32).astype(jnp.bfloat16)
    accepted = compact_path(reach, accept_leaf, kv_in.reshape(2, tree_len, 2 * kv_width))
    accepted_kv = accepted.reshape(2 * tree_len, 2, kv_width)
    return (hidden_out, next_qkv, accepted_kv)


def solution(mesh):
    devices = mesh.devices
    owners = devices.shape[0]
    lines = round(owners ** (1 / 3))
    sub_mesh = Mesh(
        devices.reshape(owners // (lines * lines), lines, lines, devices.shape[1]),
        ("z", "x", "y", "mlp"),
    )
    R = REQ
    placed = (
        P(R, None),
        P(R, "mlp"),
        P(R, None, "mlp"),
        P(R, None),
        P(R),
        P(R),
        P(R, None, None, "mlp"),
        P(R, None),
        P(R),
        P(R),
        P("mlp", None),
        P(),
        P(None, R + ("mlp",), None),
        P(R + ("mlp",), None),
        P(),
        P(None, "mlp"),
    )
    return jax.shard_map(
        per_device,
        mesh=sub_mesh,
        in_specs=placed,
        out_specs=(P(R, None), P(R, "mlp"), P(R, None, "mlp")),
        check_vma=False,
    )
```

```python
import math

import jax
import jax.numpy as jnp
from jax import lax
from jax.sharding import Mesh, PartitionSpec as P

HEAD_DIM = 64
GROUP = 4


TAG = 128
REQ = ("z", "x", "y")

norm_eps = 1e-05
masked_score = -1e30


def route(packet, dest, mark):
    plane = lax.axis_size("x") * lax.axis_size("y")
    first = jnp.zeros((lax.axis_size("z"),) + packet.shape, packet.dtype)
    first = lax.dynamic_update_index_in_dim(first, packet, dest // plane, 0)
    middle = lax.all_to_all(first, "z", 0, 0, tiled=True)
    real = middle[:, 0, mark] > 0.5
    target = middle[:, 0, mark + 1].astype(jnp.int32) % plane
    spots = jnp.arange(plane, dtype=jnp.int32)
    pick = (target[None, :] == spots[:, None]) & real[None, :]
    second = jnp.sum(jnp.where(pick[:, :, None, None], middle[None], 0), axis=1)
    second = second.astype(packet.dtype)
    arrived = lax.all_to_all(second, ("x", "y"), 0, 0, tiled=True)
    return jnp.sum(arrived.astype(jnp.float32), axis=0).astype(packet.dtype)


def split_hi_lo(values):
    high = values.astype(jnp.bfloat16)
    low = (values - high.astype(jnp.float32)).astype(jnp.bfloat16)
    return jnp.concatenate([high, low], axis=1)


def ancestors(parents):
    count_nodes = parents.shape[-1]
    nodes = jnp.arange(count_nodes, dtype=jnp.int32)
    reach = (parents[..., :, None] == nodes).astype(jnp.float32) + jnp.eye(
        count_nodes, dtype=jnp.float32
    )
    for step in range(count_nodes.bit_length()):
        reach = jnp.minimum(
            jnp.einsum(
                "sij,sjk->sik",
                reach.astype(jnp.bfloat16),
                reach.astype(jnp.bfloat16),
                preferred_element_type=jnp.float32,
            ),
            1.0,
        )
    return reach


def rms_scale(rows, gain):
    values = rows.astype(jnp.float32)
    factor = lax.rsqrt(jnp.mean(values * values, axis=-1, keepdims=True) + norm_eps)
    return (values * factor * gain.astype(jnp.float32)).astype(jnp.bfloat16)


def swiglu_rows(rows, w_in, w_down):
    dims = (((1,), (1,)), ((), ()))
    gate = lax.dot_general(rows, w_in[0], dims, preferred_element_type=jnp.float32)
    up_part = lax.dot_general(rows, w_in[1], dims, preferred_element_type=jnp.float32)
    hidden = (jax.nn.silu(gate) * up_part).astype(jnp.bfloat16)
    return jnp.dot(hidden, w_down, preferred_element_type=jnp.float32)


def compact_path(reach, leaves, rows):
    count_nodes = reach.shape[-1]
    nodes = jnp.arange(count_nodes, dtype=jnp.int32)
    leaf_hot = (nodes[None, :] == leaves[:, None]).astype(jnp.float32)
    path = jnp.einsum(
        "si,sij->sj",
        leaf_hot.astype(jnp.bfloat16),
        reach.astype(jnp.bfloat16),
        preferred_element_type=jnp.float32,
    )
    ranks = jnp.cumsum(path, axis=1) - path
    places = nodes.astype(jnp.float32)
    select = path[:, None, :] * (ranks[:, None, :] == places[None, :, None]).astype(jnp.float32)
    return jnp.einsum(
        "spj,sjw->spw", select.astype(jnp.bfloat16), rows, preferred_element_type=jnp.float32
    ).astype(jnp.bfloat16)


def per_device(
    resid,
    q_in,
    kv_in,
    parents,
    counts,
    accept_leaf,
    cache,
    held_table,
    held_len,
    prev_owner,
    w_out,
    gain_mid,
    w_in,
    w_down,
    gain_next,
    w_next,
):
    tree_len = parents.shape[1]
    kv_width = kv_in.shape[2]
    kv_local = kv_width // HEAD_DIM
    scale = HEAD_DIM ** (-0.5)
    queries = q_in.reshape(2, tree_len, kv_local, GROUP, HEAD_DIM)
    device_id = lax.axis_index(REQ)
    q_width = q_in.shape[1]
    q_tags = jnp.zeros((tree_len, TAG), jnp.float32)
    q_tags = q_tags.at[:, 0].set(1.0).at[:, 1].set(prev_owner[0]).at[:, 2].set(device_id)
    q_packet = jnp.concatenate([q_in[tree_len:], q_tags.astype(q_in.dtype)], axis=1)
    every_query = route(q_packet, prev_owner[0], q_width)
    own_w = jnp.stack([w_in[0], w_in[1], w_down])
    all_w = lax.all_gather(own_w, ("z", "x"), axis=0, tiled=False)
    page_len = cache.shape[2]
    num_blocks = cache.shape[0]
    width = kv_local * HEAD_DIM
    entries = held_table.shape[1]
    entry_start = jnp.arange(entries, dtype=jnp.int32)[:, None] * page_len
    in_page = jnp.arange(page_len, dtype=jnp.int32)[None, :]
    head_eye = jnp.eye(kv_local, dtype=jnp.float32)
    rows = kv_local * GROUP * tree_len

    def attend(slot, slot_queries, first, last, state):
        running, total, accum = state
        table = held_table[slot]
        length = held_len[slot]
        page_ids = jnp.arange(first, last, dtype=jnp.int32)
        match = table[:, None] == page_ids[None, :]
        valid = (entry_start + in_page) < length
        visible = jnp.any(match[:, :, None] & valid[:, None, :], axis=0).reshape(-1)
        key_rows = cache[first:last, 0].reshape((last - first) * page_len, width)
        value_rows = cache[first:last, 1].reshape((last - first) * page_len, width)
        spread = jnp.einsum(
            "qghe,gf->ghqfe", slot_queries, head_eye.astype(slot_queries.dtype)
        ).reshape(rows, width)
        scores = (
            lax.dot_general(
                spread, key_rows, (((1,), (1,)), ((), ())), preferred_element_type=jnp.float32
            )
            * scale
        )
        scores = jnp.where(visible, scores, masked_score)
        old = running.reshape(rows)
        newest = jnp.maximum(old, jnp.max(scores, axis=-1))
        weights = jnp.exp(scores - newest[:, None])
        factor = jnp.exp(old - newest)
        total = total.reshape(rows) * factor + jnp.sum(weights, axis=-1)
        high = weights.astype(jnp.bfloat16)
        low = (weights - high.astype(jnp.float32)).astype(jnp.bfloat16)
        full = jnp.dot(high, value_rows, preferred_element_type=jnp.float32) + jnp.dot(
            low, value_rows, preferred_element_type=jnp.float32
        )
        blocks = full.reshape(kv_local, GROUP, tree_len, kv_local, HEAD_DIM)
        update = jnp.stack([blocks[g, :, :, g] for g in range(kv_local)])
        accum = accum * factor.reshape(kv_local, GROUP, tree_len)[..., None] + update
        return (
            newest.reshape(kv_local, GROUP, tree_len),
            total.reshape(kv_local, GROUP, tree_len),
            accum,
        )

    stat_shape = (kv_local, GROUP, tree_len)
    start_state = (
        jnp.full(stat_shape, masked_score, jnp.float32),
        jnp.zeros(stat_shape, jnp.float32),
        jnp.zeros(stat_shape + (HEAD_DIM,), jnp.float32),
    )
    own_queries = queries[0]
    own_state = start_state
    sender = every_query[0, q_width + 2].astype(jnp.int32)
    foreign = every_query[:, :q_width]
    foreign = foreign.reshape(tree_len, kv_local, GROUP, HEAD_DIM)
    f_running, f_total, f_accum = attend(1, foreign, 0, num_blocks, start_state)
    f_out = f_accum / f_total[..., None]
    sent_out = jnp.transpose(f_out, (2, 0, 1, 3)).reshape(
        tree_len, kv_local * GROUP * HEAD_DIM
    )
    sent_max = jnp.transpose(f_running, (2, 0, 1)).reshape(tree_len, kv_local * GROUP)
    sent_total = jnp.transpose(f_total, (2, 0, 1)).reshape(tree_len, kv_local * GROUP)
    stats = jnp.concatenate(
        [split_hi_lo(sent_max), split_hi_lo(sent_total)], axis=1
    )
    r_tags = jnp.zeros((tree_len, TAG - stats.shape[1]), jnp.float32)
    r_tags = r_tags.at[:, 0].set(1.0).at[:, 1].set(sender)
    r_packet = jnp.concatenate(
        [sent_out.astype(jnp.bfloat16), stats, r_tags.astype(jnp.bfloat16)], axis=1
    )
    r_packet, own_state = lax.optimization_barrier((r_packet, own_state))
    got = route(r_packet, sender, sent_out.shape[1] + stats.shape[1]).astype(jnp.float32)
    running, total, accum = attend(0, own_queries, 0, num_blocks, own_state)
    all_w, running, total, accum = lax.optimization_barrier((all_w, running, total, accum))
    cache_out = accum / total[..., None]
    heads = kv_local * GROUP
    o_w = heads * HEAD_DIM
    recv_out = got[:, :o_w].reshape(tree_len, kv_local, GROUP, HEAD_DIM)
    recv_max = (got[:, o_w : o_w + heads] + got[:, o_w + heads : o_w + 2 * heads]).reshape(
        tree_len, kv_local, GROUP
    )
    t0 = o_w + 2 * heads
    recv_total = (got[:, t0 : t0 + heads] + got[:, t0 + heads : t0 + 2 * heads]).reshape(
        tree_len, kv_local, GROUP
    )
    part_out = jnp.stack([cache_out, jnp.transpose(recv_out, (1, 2, 0, 3))])
    part_max = jnp.stack([running, jnp.transpose(recv_max, (1, 2, 0))])
    part_total = jnp.stack([total, jnp.transpose(recv_total, (1, 2, 0))])
    reach = ancestors(parents)
    live = jnp.arange(tree_len, dtype=jnp.int32)[None, :] < counts[:, None]
    allowed = ((reach > 0.5) & live[:, None, :])[:, None, None, :, :]
    draft_keys = kv_in[:, 0].reshape(2, tree_len, kv_local, HEAD_DIM)
    draft_values = kv_in[:, 1].reshape(2, tree_len, kv_local, HEAD_DIM)
    tree_scores = (
        jnp.einsum("sqghe,skge->sghqk", queries, draft_keys, preferred_element_type=jnp.float32)
        * scale
    )
    tree_scores = jnp.where(allowed, tree_scores, masked_score)
    tree_max = jnp.max(tree_scores, axis=-1)
    tree_weights = jnp.where(allowed, jnp.exp(tree_scores - tree_max[..., None]), 0.0)
    tree_total = jnp.sum(tree_weights, axis=-1)
    tree_high = tree_weights.astype(jnp.bfloat16)
    tree_low = (tree_weights - tree_high.astype(jnp.float32)).astype(jnp.bfloat16)
    tree_accum = jnp.einsum(
        "sghqk,skge->sghqe", tree_high, draft_values, preferred_element_type=jnp.float32
    ) + jnp.einsum(
        "sghqk,skge->sghqe", tree_low, draft_values, preferred_element_type=jnp.float32
    )
    overall = jnp.maximum(part_max, tree_max)
    cache_weight = part_total * jnp.exp(part_max - overall)
    tree_weight = jnp.exp(tree_max - overall)
    merged = (part_out * cache_weight[..., None] + tree_accum * tree_weight[..., None]) / (
        cache_weight + tree_total * tree_weight
    )[..., None]
    attended = (
        jnp.transpose(merged, (0, 3, 1, 2, 4))
        .reshape(2 * tree_len, kv_local * GROUP * HEAD_DIM)
        .astype(jnp.bfloat16)
    )
    partial_proj = jnp.dot(attended, w_out, preferred_element_type=jnp.float32)
    projected = partial_proj + lax.ppermute(partial_proj, "mlp", [(0, 1), (1, 0)])
    mixed = (resid.astype(jnp.float32) + projected).astype(jnp.bfloat16)
    normed = rms_scale(mixed, gain_mid)
    column = lax.axis_index("mlp")
    half_count = normed.shape[0] // lax.axis_size("mlp")
    ring = lax.axis_size("y")
    shifted = [normed]
    for shift in range(1, ring):
        perm = [(i, (i + shift) % ring) for i in range(ring)]
        shifted.append(lax.ppermute(normed, "y", perm))
    group_rows = jnp.concatenate(shifted, axis=0)
    dims = (((1,), (2,)), ((), ()))
    gate = lax.dot_general(group_rows, all_w[:, 0], dims, preferred_element_type=jnp.float32)
    up_part = lax.dot_general(group_rows, all_w[:, 1], dims, preferred_element_type=jnp.float32)
    hidden = (jax.nn.silu(gate) * up_part).astype(jnp.bfloat16)
    down_dims = (((1, 2), (0, 1)), ((), ()))
    partial = lax.dot_general(
        hidden, all_w[:, 2], down_dims, preferred_element_type=jnp.float32
    )
    halves = partial.reshape(ring, 2, half_count, partial.shape[1])
    mine = lax.dynamic_index_in_dim(halves, column, 1, keepdims=False)
    theirs = lax.dynamic_index_in_dim(halves, 1 - column, 1, keepdims=False)
    mine = mine + lax.ppermute(theirs, "mlp", [(0, 1), (1, 0)])
    mlp_half = mine[0]
    for shift in range(1, ring):
        perm = [(i, (i - shift) % ring) for i in range(ring)]
        mlp_half = mlp_half + lax.ppermute(mine[shift], "y", perm)
    base_half = lax.dynamic_slice_in_dim(mixed, column * half_count, half_count, 0)
    out_half = (base_half.astype(jnp.float32) + mlp_half).astype(jnp.bfloat16)
    hidden_out = lax.all_gather(out_half, "mlp", axis=0, tiled=True)
    next_normed = rms_scale(hidden_out, gain_next)
    next_qkv = jnp.dot(next_normed, w_next, preferred_element_type=jnp.float32).astype(jnp.bfloat16)
    accepted = compact_path(reach, accept_leaf, kv_in.reshape(2, tree_len, 2 * kv_width))
    accepted_kv = accepted.reshape(2 * tree_len, 2, kv_width)
    return (hidden_out, next_qkv, accepted_kv)


def solution(mesh):
    devices = mesh.devices
    owners = devices.shape[0]
    lines = round(owners ** (1 / 3))
    sub_mesh = Mesh(
        devices.reshape(owners // (lines * lines), lines, lines, devices.shape[1]),
        ("z", "x", "y", "mlp"),
    )
    R = REQ
    placed = (
        P(R, None),
        P(R, "mlp"),
        P(R, None, "mlp"),
        P(R, None),
        P(R),
        P(R),
        P(R, None, None, "mlp"),
        P(R, None),
        P(R),
        P(R),
        P("mlp", None),
        P(),
        P(None, R + ("mlp",), None),
        P(R + ("mlp",), None),
        P(),
        P(None, "mlp"),
    )
    return jax.shard_map(
        per_device,
        mesh=sub_mesh,
        in_specs=placed,
        out_specs=(P(R, None), P(R, "mlp"), P(R, None, "mlp")),
        check_vma=False,
    )
```

```python
import math

import jax
import jax.numpy as jnp
from jax import lax
from jax.sharding import Mesh, PartitionSpec as P

HEAD_DIM = 64
GROUP = 4


TAG = 128
REQ = ("z", "x", "y")

norm_eps = 1e-05
masked_score = -1e30


def route(packet, dest, mark):
    plane = lax.axis_size("x") * lax.axis_size("y")
    first = jnp.zeros((lax.axis_size("z"),) + packet.shape, packet.dtype)
    first = lax.dynamic_update_index_in_dim(first, packet, dest // plane, 0)
    middle = lax.all_to_all(first, "z", 0, 0, tiled=True)
    real = middle[:, 0, mark] > 0.5
    target = middle[:, 0, mark + 1].astype(jnp.int32) % plane
    spots = jnp.arange(plane, dtype=jnp.int32)
    pick = (target[None, :] == spots[:, None]) & real[None, :]
    second = jnp.sum(jnp.where(pick[:, :, None, None], middle[None], 0), axis=1)
    second = second.astype(packet.dtype)
    arrived = lax.all_to_all(second, ("x", "y"), 0, 0, tiled=True)
    return jnp.sum(arrived.astype(jnp.float32), axis=0).astype(packet.dtype)


def split_hi_lo(values):
    high = values.astype(jnp.bfloat16)
    low = (values - high.astype(jnp.float32)).astype(jnp.bfloat16)
    return jnp.concatenate([high, low], axis=1)


def ancestors(parents):
    count_nodes = parents.shape[-1]
    nodes = jnp.arange(count_nodes, dtype=jnp.int32)
    reach = (parents[..., :, None] == nodes).astype(jnp.float32) + jnp.eye(
        count_nodes, dtype=jnp.float32
    )
    for step in range(count_nodes.bit_length()):
        reach = jnp.minimum(
            jnp.einsum(
                "sij,sjk->sik",
                reach.astype(jnp.bfloat16),
                reach.astype(jnp.bfloat16),
                preferred_element_type=jnp.float32,
            ),
            1.0,
        )
    return reach


def rms_scale(rows, gain):
    values = rows.astype(jnp.float32)
    factor = lax.rsqrt(jnp.mean(values * values, axis=-1, keepdims=True) + norm_eps)
    return (values * factor * gain.astype(jnp.float32)).astype(jnp.bfloat16)


def swiglu_rows(rows, w_in, w_down):
    dims = (((1,), (1,)), ((), ()))
    gate = lax.dot_general(rows, w_in[0], dims, preferred_element_type=jnp.float32)
    up_part = lax.dot_general(rows, w_in[1], dims, preferred_element_type=jnp.float32)
    hidden = (jax.nn.silu(gate) * up_part).astype(jnp.bfloat16)
    return jnp.dot(hidden, w_down, preferred_element_type=jnp.float32)


def compact_path(reach, leaves, rows):
    count_nodes = reach.shape[-1]
    nodes = jnp.arange(count_nodes, dtype=jnp.int32)
    leaf_hot = (nodes[None, :] == leaves[:, None]).astype(jnp.float32)
    path = jnp.einsum(
        "si,sij->sj",
        leaf_hot.astype(jnp.bfloat16),
        reach.astype(jnp.bfloat16),
        preferred_element_type=jnp.float32,
    )
    ranks = jnp.cumsum(path, axis=1) - path
    places = nodes.astype(jnp.float32)
    select = path[:, None, :] * (ranks[:, None, :] == places[None, :, None]).astype(jnp.float32)
    return jnp.einsum(
        "spj,sjw->spw", select.astype(jnp.bfloat16), rows, preferred_element_type=jnp.float32
    ).astype(jnp.bfloat16)


def per_device(
    resid,
    q_in,
    kv_in,
    parents,
    counts,
    accept_leaf,
    cache,
    held_table,
    held_len,
    prev_owner,
    w_out,
    gain_mid,
    w_in,
    w_down,
    gain_next,
    w_next,
):
    tree_len = parents.shape[1]
    kv_width = kv_in.shape[2]
    kv_local = kv_width // HEAD_DIM
    scale = HEAD_DIM ** (-0.5)
    queries = q_in.reshape(2, tree_len, kv_local, GROUP, HEAD_DIM)
    device_id = lax.axis_index(REQ)
    q_width = q_in.shape[1]
    q_tags = jnp.zeros((tree_len, TAG), jnp.float32)
    q_tags = q_tags.at[:, 0].set(1.0).at[:, 1].set(prev_owner[0]).at[:, 2].set(device_id)
    q_packet = jnp.concatenate([q_in[tree_len:], q_tags.astype(q_in.dtype)], axis=1)
    every_query = route(q_packet, prev_owner[0], q_width)
    own_w = jnp.stack([w_in[0], w_in[1], w_down])
    all_w = lax.all_gather(own_w, ("z", "x"), axis=0, tiled=False)
    page_len = cache.shape[2]
    num_blocks = cache.shape[0]
    width = kv_local * HEAD_DIM
    entries = held_table.shape[1]
    entry_start = jnp.arange(entries, dtype=jnp.int32)[:, None] * page_len
    in_page = jnp.arange(page_len, dtype=jnp.int32)[None, :]
    head_eye = jnp.eye(kv_local, dtype=jnp.float32)
    rows = kv_local * GROUP * tree_len

    def attend(slot, slot_queries, first, last, state):
        running, total, accum = state
        table = held_table[slot]
        length = held_len[slot]
        page_ids = jnp.arange(first, last, dtype=jnp.int32)
        match = table[:, None] == page_ids[None, :]
        valid = (entry_start + in_page) < length
        visible = jnp.any(match[:, :, None] & valid[:, None, :], axis=0).reshape(-1)
        key_rows = cache[first:last, 0].reshape((last - first) * page_len, width)
        value_rows = cache[first:last, 1].reshape((last - first) * page_len, width)
        spread = jnp.einsum(
            "qghe,gf->ghqfe", slot_queries, head_eye.astype(slot_queries.dtype)
        ).reshape(rows, width)
        scores = (
            lax.dot_general(
                spread, key_rows, (((1,), (1,)), ((), ())), preferred_element_type=jnp.float32
            )
            * scale
        )
        scores = jnp.where(visible, scores, masked_score)
        old = running.reshape(rows)
        newest = jnp.maximum(old, jnp.max(scores, axis=-1))
        weights = jnp.exp(scores - newest[:, None])
        factor = jnp.exp(old - newest)
        total = total.reshape(rows) * factor + jnp.sum(weights, axis=-1)
        high = weights.astype(jnp.bfloat16)
        low = (weights - high.astype(jnp.float32)).astype(jnp.bfloat16)
        full = jnp.dot(high, value_rows, preferred_element_type=jnp.float32) + jnp.dot(
            low, value_rows, preferred_element_type=jnp.float32
        )
        blocks = full.reshape(kv_local, GROUP, tree_len, kv_local, HEAD_DIM)
        update = jnp.stack([blocks[g, :, :, g] for g in range(kv_local)])
        accum = accum * factor.reshape(kv_local, GROUP, tree_len)[..., None] + update
        return (
            newest.reshape(kv_local, GROUP, tree_len),
            total.reshape(kv_local, GROUP, tree_len),
            accum,
        )

    stat_shape = (kv_local, GROUP, tree_len)
    start_state = (
        jnp.full(stat_shape, masked_score, jnp.float32),
        jnp.zeros(stat_shape, jnp.float32),
        jnp.zeros(stat_shape + (HEAD_DIM,), jnp.float32),
    )
    own_queries = queries[0]
    own_state = start_state
    sender = every_query[0, q_width + 2].astype(jnp.int32)
    foreign = every_query[:, :q_width]
    foreign = foreign.reshape(tree_len, kv_local, GROUP, HEAD_DIM)
    f_running, f_total, f_accum = attend(1, foreign, 0, num_blocks, start_state)
    f_out = f_accum / f_total[..., None]
    sent_out = jnp.transpose(f_out, (2, 0, 1, 3)).reshape(
        tree_len, kv_local * GROUP * HEAD_DIM
    )
    sent_max = jnp.transpose(f_running, (2, 0, 1)).reshape(tree_len, kv_local * GROUP)
    sent_total = jnp.transpose(f_total, (2, 0, 1)).reshape(tree_len, kv_local * GROUP)
    stats = jnp.concatenate(
        [split_hi_lo(sent_max), split_hi_lo(sent_total)], axis=1
    )
    r_tags = jnp.zeros((tree_len, TAG - stats.shape[1]), jnp.float32)
    r_tags = r_tags.at[:, 0].set(1.0).at[:, 1].set(sender)
    r_packet = jnp.concatenate(
        [sent_out.astype(jnp.bfloat16), stats, r_tags.astype(jnp.bfloat16)], axis=1
    )
    r_packet, own_state = lax.optimization_barrier((r_packet, own_state))
    got = route(r_packet, sender, sent_out.shape[1] + stats.shape[1]).astype(jnp.float32)
    running, total, accum = attend(0, own_queries, 0, num_blocks, own_state)
    all_w, running, total, accum = lax.optimization_barrier((all_w, running, total, accum))
    cache_out = accum / total[..., None]
    heads = kv_local * GROUP
    o_w = heads * HEAD_DIM
    recv_out = got[:, :o_w].reshape(tree_len, kv_local, GROUP, HEAD_DIM)
    recv_max = (got[:, o_w : o_w + heads] + got[:, o_w + heads : o_w + 2 * heads]).reshape(
        tree_len, kv_local, GROUP
    )
    t0 = o_w + 2 * heads
    recv_total = (got[:, t0 : t0 + heads] + got[:, t0 + heads : t0 + 2 * heads]).reshape(
        tree_len, kv_local, GROUP
    )
    part_out = jnp.stack([cache_out, jnp.transpose(recv_out, (1, 2, 0, 3))])
    part_max = jnp.stack([running, jnp.transpose(recv_max, (1, 2, 0))])
    part_total = jnp.stack([total, jnp.transpose(recv_total, (1, 2, 0))])
    reach = ancestors(parents)
    live = jnp.arange(tree_len, dtype=jnp.int32)[None, :] < counts[:, None]
    allowed = ((reach > 0.5) & live[:, None, :])[:, None, None, :, :]
    draft_keys = kv_in[:, 0].reshape(2, tree_len, kv_local, HEAD_DIM)
    draft_values = kv_in[:, 1].reshape(2, tree_len, kv_local, HEAD_DIM)
    tree_scores = (
        jnp.einsum("sqghe,skge->sghqk", queries, draft_keys, preferred_element_type=jnp.float32)
        * scale
    )
    tree_scores = jnp.where(allowed, tree_scores, masked_score)
    tree_max = jnp.max(tree_scores, axis=-1)
    tree_weights = jnp.where(allowed, jnp.exp(tree_scores - tree_max[..., None]), 0.0)
    tree_total = jnp.sum(tree_weights, axis=-1)
    tree_high = tree_weights.astype(jnp.bfloat16)
    tree_low = (tree_weights - tree_high.astype(jnp.float32)).astype(jnp.bfloat16)
    tree_accum = jnp.einsum(
        "sghqk,skge->sghqe", tree_high, draft_values, preferred_element_type=jnp.float32
    ) + jnp.einsum(
        "sghqk,skge->sghqe", tree_low, draft_values, preferred_element_type=jnp.float32
    )
    overall = jnp.maximum(part_max, tree_max)
    cache_weight = part_total * jnp.exp(part_max - overall)
    tree_weight = jnp.exp(tree_max - overall)
    merged = (part_out * cache_weight[..., None] + tree_accum * tree_weight[..., None]) / (
        cache_weight + tree_total * tree_weight
    )[..., None]
    attended = (
        jnp.transpose(merged, (0, 3, 1, 2, 4))
        .reshape(2 * tree_len, kv_local * GROUP * HEAD_DIM)
        .astype(jnp.bfloat16)
    )
    partial_proj = jnp.dot(attended, w_out, preferred_element_type=jnp.float32)
    projected = partial_proj + lax.ppermute(partial_proj, "mlp", [(0, 1), (1, 0)])
    mixed = (resid.astype(jnp.float32) + projected).astype(jnp.bfloat16)
    normed = rms_scale(mixed, gain_mid)
    column = lax.axis_index("mlp")
    half_count = normed.shape[0] // lax.axis_size("mlp")
    ring = lax.axis_size("y")
    shifted = [normed]
    for shift in range(1, ring):
        perm = [(i, (i + shift) % ring) for i in range(ring)]
        shifted.append(lax.ppermute(normed, "y", perm))
    group_rows = jnp.concatenate(shifted, axis=0)
    dims = (((1,), (2,)), ((), ()))
    gate = lax.dot_general(group_rows, all_w[:, 0], dims, preferred_element_type=jnp.float32)
    up_part = lax.dot_general(group_rows, all_w[:, 1], dims, preferred_element_type=jnp.float32)
    hidden = (jax.nn.silu(gate) * up_part).astype(jnp.bfloat16)
    down_dims = (((1, 2), (0, 1)), ((), ()))
    partial = lax.dot_general(
        hidden, all_w[:, 2], down_dims, preferred_element_type=jnp.float32
    )
    halves = partial.reshape(ring, 2, half_count, partial.shape[1])
    mine = lax.dynamic_index_in_dim(halves, column, 1, keepdims=False)
    theirs = lax.dynamic_index_in_dim(halves, 1 - column, 1, keepdims=False)
    mine = mine + lax.ppermute(theirs, "mlp", [(0, 1), (1, 0)])
    mlp_half = mine[0]
    for shift in range(1, ring):
        perm = [(i, (i - shift) % ring) for i in range(ring)]
        mlp_half = mlp_half + lax.ppermute(mine[shift], "y", perm)
    base_half = lax.dynamic_slice_in_dim(mixed, column * half_count, half_count, 0)
    out_half = (base_half.astype(jnp.float32) + mlp_half).astype(jnp.bfloat16)
    other_half = lax.ppermute(out_half, "mlp", [(0, 1), (1, 0)])
    pair = jnp.stack([out_half, other_half])
    hidden_out = jnp.concatenate(
        [
            lax.dynamic_index_in_dim(pair, column, 0, keepdims=False),
            lax.dynamic_index_in_dim(pair, 1 - column, 0, keepdims=False),
        ],
        axis=0,
    )
    next_normed = rms_scale(hidden_out, gain_next)
    next_qkv = jnp.dot(next_normed, w_next, preferred_element_type=jnp.float32).astype(jnp.bfloat16)
    accepted = compact_path(reach, accept_leaf, kv_in.reshape(2, tree_len, 2 * kv_width))
    accepted_kv = accepted.reshape(2 * tree_len, 2, kv_width)
    return (hidden_out, next_qkv, accepted_kv)


def solution(mesh):
    devices = mesh.devices
    owners = devices.shape[0]
    lines = round(owners ** (1 / 3))
    sub_mesh = Mesh(
        devices.reshape(owners // (lines * lines), lines, lines, devices.shape[1]),
        ("z", "x", "y", "mlp"),
    )
    R = REQ
    placed = (
        P(R, None),
        P(R, "mlp"),
        P(R, None, "mlp"),
        P(R, None),
        P(R),
        P(R),
        P(R, None, None, "mlp"),
        P(R, None),
        P(R),
        P(R),
        P("mlp", None),
        P(),
        P(None, R + ("mlp",), None),
        P(R + ("mlp",), None),
        P(),
        P(None, "mlp"),
    )
    return jax.shard_map(
        per_device,
        mesh=sub_mesh,
        in_specs=placed,
        out_specs=(P(R, None), P(R, "mlp"), P(R, None, "mlp")),
        check_vma=False,
    )
```

```python
import math

import jax
import jax.numpy as jnp
from jax import lax
from jax.sharding import Mesh, PartitionSpec as P

HEAD_DIM = 64
GROUP = 4


TAG = 128
REQ = ("z", "x", "y")

norm_eps = 1e-05
masked_score = -1e30


def route(packet, dest, mark):
    plane = lax.axis_size("x") * lax.axis_size("y")
    first = jnp.zeros((lax.axis_size("z"),) + packet.shape, packet.dtype)
    first = lax.dynamic_update_index_in_dim(first, packet, dest // plane, 0)
    middle = lax.all_to_all(first, "z", 0, 0, tiled=True)
    real = middle[:, 0, mark] > 0.5
    target = middle[:, 0, mark + 1].astype(jnp.int32) % plane
    spots = jnp.arange(plane, dtype=jnp.int32)
    pick = (target[None, :] == spots[:, None]) & real[None, :]
    second = jnp.sum(jnp.where(pick[:, :, None, None], middle[None], 0), axis=1)
    second = second.astype(packet.dtype)
    arrived = lax.all_to_all(second, ("x", "y"), 0, 0, tiled=True)
    return jnp.sum(arrived.astype(jnp.float32), axis=0).astype(packet.dtype)


def split_hi_lo(values):
    high = values.astype(jnp.bfloat16)
    low = (values - high.astype(jnp.float32)).astype(jnp.bfloat16)
    return jnp.concatenate([high, low], axis=1)


def ancestors(parents):
    count_nodes = parents.shape[-1]
    nodes = jnp.arange(count_nodes, dtype=jnp.int32)
    reach = (parents[..., :, None] == nodes).astype(jnp.float32) + jnp.eye(
        count_nodes, dtype=jnp.float32
    )
    for step in range(count_nodes.bit_length()):
        reach = jnp.minimum(
            jnp.einsum(
                "sij,sjk->sik",
                reach.astype(jnp.bfloat16),
                reach.astype(jnp.bfloat16),
                preferred_element_type=jnp.float32,
            ),
            1.0,
        )
    return reach


def rms_scale(rows, gain):
    values = rows.astype(jnp.float32)
    factor = lax.rsqrt(jnp.mean(values * values, axis=-1, keepdims=True) + norm_eps)
    return (values * factor * gain.astype(jnp.float32)).astype(jnp.bfloat16)


def swiglu_rows(rows, w_in, w_down):
    dims = (((1,), (1,)), ((), ()))
    gate = lax.dot_general(rows, w_in[0], dims, preferred_element_type=jnp.float32)
    up_part = lax.dot_general(rows, w_in[1], dims, preferred_element_type=jnp.float32)
    hidden = (jax.nn.silu(gate) * up_part).astype(jnp.bfloat16)
    return jnp.dot(hidden, w_down, preferred_element_type=jnp.float32)


def compact_path(reach, leaves, rows):
    count_nodes = reach.shape[-1]
    nodes = jnp.arange(count_nodes, dtype=jnp.int32)
    leaf_hot = (nodes[None, :] == leaves[:, None]).astype(jnp.float32)
    path = jnp.einsum(
        "si,sij->sj",
        leaf_hot.astype(jnp.bfloat16),
        reach.astype(jnp.bfloat16),
        preferred_element_type=jnp.float32,
    )
    ranks = jnp.cumsum(path, axis=1) - path
    places = nodes.astype(jnp.float32)
    select = path[:, None, :] * (ranks[:, None, :] == places[None, :, None]).astype(jnp.float32)
    return jnp.einsum(
        "spj,sjw->spw", select.astype(jnp.bfloat16), rows, preferred_element_type=jnp.float32
    ).astype(jnp.bfloat16)


def per_device(
    resid,
    q_in,
    kv_in,
    parents,
    counts,
    accept_leaf,
    cache,
    held_table,
    held_len,
    prev_owner,
    w_out,
    gain_mid,
    w_in,
    w_down,
    gain_next,
    w_next,
):
    tree_len = parents.shape[1]
    kv_width = kv_in.shape[2]
    kv_local = kv_width // HEAD_DIM
    scale = HEAD_DIM ** (-0.5)
    queries = q_in.reshape(2, tree_len, kv_local, GROUP, HEAD_DIM)
    device_id = lax.axis_index(REQ)
    q_width = q_in.shape[1]
    q_tags = jnp.zeros((tree_len, TAG), jnp.float32)
    q_tags = q_tags.at[:, 0].set(1.0).at[:, 1].set(prev_owner[0]).at[:, 2].set(device_id)
    q_packet = jnp.concatenate([q_in[tree_len:], q_tags.astype(q_in.dtype)], axis=1)
    every_query = route(q_packet, prev_owner[0], q_width)
    own_w = jnp.stack([w_in[0], w_in[1], w_down])
    all_w = lax.all_gather(own_w, ("z", "x"), axis=0, tiled=False)
    page_len = cache.shape[2]
    num_blocks = cache.shape[0]
    width = kv_local * HEAD_DIM
    entries = held_table.shape[1]
    entry_start = jnp.arange(entries, dtype=jnp.int32)[:, None] * page_len
    in_page = jnp.arange(page_len, dtype=jnp.int32)[None, :]
    head_eye = jnp.eye(kv_local, dtype=jnp.float32)
    rows = kv_local * GROUP * tree_len

    def attend(slot, slot_queries, first, last, state):
        running, total, accum = state
        table = held_table[slot]
        length = held_len[slot]
        page_ids = jnp.arange(first, last, dtype=jnp.int32)
        match = table[:, None] == page_ids[None, :]
        valid = (entry_start + in_page) < length
        visible = jnp.any(match[:, :, None] & valid[:, None, :], axis=0).reshape(-1)
        key_rows = cache[first:last, 0].reshape((last - first) * page_len, width)
        value_rows = cache[first:last, 1].reshape((last - first) * page_len, width)
        spread = jnp.einsum(
            "qghe,gf->ghqfe", slot_queries, head_eye.astype(slot_queries.dtype)
        ).reshape(rows, width)
        scores = (
            lax.dot_general(
                spread, key_rows, (((1,), (1,)), ((), ())), preferred_element_type=jnp.float32
            )
            * scale
        )
        scores = jnp.where(visible, scores, masked_score)
        old = running.reshape(rows)
        newest = jnp.maximum(old, jnp.max(scores, axis=-1))
        weights = jnp.exp(scores - newest[:, None])
        factor = jnp.exp(old - newest)
        total = total.reshape(rows) * factor + jnp.sum(weights, axis=-1)
        high = weights.astype(jnp.bfloat16)
        low = (weights - high.astype(jnp.float32)).astype(jnp.bfloat16)
        full = jnp.dot(high, value_rows, preferred_element_type=jnp.float32) + jnp.dot(
            low, value_rows, preferred_element_type=jnp.float32
        )
        blocks = full.reshape(kv_local, GROUP, tree_len, kv_local, HEAD_DIM)
        update = jnp.stack([blocks[g, :, :, g] for g in range(kv_local)])
        accum = accum * factor.reshape(kv_local, GROUP, tree_len)[..., None] + update
        return (
            newest.reshape(kv_local, GROUP, tree_len),
            total.reshape(kv_local, GROUP, tree_len),
            accum,
        )

    stat_shape = (kv_local, GROUP, tree_len)
    start_state = (
        jnp.full(stat_shape, masked_score, jnp.float32),
        jnp.zeros(stat_shape, jnp.float32),
        jnp.zeros(stat_shape + (HEAD_DIM,), jnp.float32),
    )
    own_queries = queries[0]
    own_state = start_state
    sender = every_query[0, q_width + 2].astype(jnp.int32)
    foreign = every_query[:, :q_width]
    foreign = foreign.reshape(tree_len, kv_local, GROUP, HEAD_DIM)
    f_running, f_total, f_accum = attend(1, foreign, 0, num_blocks, start_state)
    f_out = f_accum / f_total[..., None]
    sent_out = jnp.transpose(f_out, (2, 0, 1, 3)).reshape(
        tree_len, kv_local * GROUP * HEAD_DIM
    )
    sent_max = jnp.transpose(f_running, (2, 0, 1)).reshape(tree_len, kv_local * GROUP)
    sent_total = jnp.transpose(f_total, (2, 0, 1)).reshape(tree_len, kv_local * GROUP)
    stats = jnp.concatenate(
        [split_hi_lo(sent_max), split_hi_lo(sent_total)], axis=1
    )
    r_tags = jnp.zeros((tree_len, TAG - stats.shape[1]), jnp.float32)
    r_tags = r_tags.at[:, 0].set(1.0).at[:, 1].set(sender)
    r_packet = jnp.concatenate(
        [sent_out.astype(jnp.bfloat16), stats, r_tags.astype(jnp.bfloat16)], axis=1
    )
    r_packet, own_state = lax.optimization_barrier((r_packet, own_state))
    got = route(r_packet, sender, sent_out.shape[1] + stats.shape[1]).astype(jnp.float32)
    running, total, accum = attend(0, own_queries, 0, num_blocks, own_state)
    all_w, running, total, accum = lax.optimization_barrier((all_w, running, total, accum))
    cache_out = accum / total[..., None]
    heads = kv_local * GROUP
    o_w = heads * HEAD_DIM
    recv_out = got[:, :o_w].reshape(tree_len, kv_local, GROUP, HEAD_DIM)
    recv_max = (got[:, o_w : o_w + heads] + got[:, o_w + heads : o_w + 2 * heads]).reshape(
        tree_len, kv_local, GROUP
    )
    t0 = o_w + 2 * heads
    recv_total = (got[:, t0 : t0 + heads] + got[:, t0 + heads : t0 + 2 * heads]).reshape(
        tree_len, kv_local, GROUP
    )
    part_out = jnp.stack([cache_out, jnp.transpose(recv_out, (1, 2, 0, 3))])
    part_max = jnp.stack([running, jnp.transpose(recv_max, (1, 2, 0))])
    part_total = jnp.stack([total, jnp.transpose(recv_total, (1, 2, 0))])
    reach = ancestors(parents)
    live = jnp.arange(tree_len, dtype=jnp.int32)[None, :] < counts[:, None]
    allowed = ((reach > 0.5) & live[:, None, :])[:, None, None, :, :]
    draft_keys = kv_in[:, 0].reshape(2, tree_len, kv_local, HEAD_DIM)
    draft_values = kv_in[:, 1].reshape(2, tree_len, kv_local, HEAD_DIM)
    tree_scores = (
        jnp.einsum("sqghe,skge->sghqk", queries, draft_keys, preferred_element_type=jnp.float32)
        * scale
    )
    tree_scores = jnp.where(allowed, tree_scores, masked_score)
    tree_max = jnp.max(tree_scores, axis=-1)
    tree_weights = jnp.exp(tree_scores - tree_max[..., None])
    tree_total = jnp.sum(tree_weights, axis=-1)
    tree_high = tree_weights.astype(jnp.bfloat16)
    tree_low = (tree_weights - tree_high.astype(jnp.float32)).astype(jnp.bfloat16)
    tree_accum = jnp.einsum(
        "sghqk,skge->sghqe", tree_high, draft_values, preferred_element_type=jnp.float32
    ) + jnp.einsum(
        "sghqk,skge->sghqe", tree_low, draft_values, preferred_element_type=jnp.float32
    )
    overall = jnp.maximum(part_max, tree_max)
    cache_weight = part_total * jnp.exp(part_max - overall)
    tree_weight = jnp.exp(tree_max - overall)
    merged = (part_out * cache_weight[..., None] + tree_accum * tree_weight[..., None]) / (
        cache_weight + tree_total * tree_weight
    )[..., None]
    attended = (
        jnp.transpose(merged, (0, 3, 1, 2, 4))
        .reshape(2 * tree_len, kv_local * GROUP * HEAD_DIM)
        .astype(jnp.bfloat16)
    )
    partial_proj = jnp.dot(attended, w_out, preferred_element_type=jnp.float32)
    projected = partial_proj + lax.ppermute(partial_proj, "mlp", [(0, 1), (1, 0)])
    mixed = (resid.astype(jnp.float32) + projected).astype(jnp.bfloat16)
    normed = rms_scale(mixed, gain_mid)
    column = lax.axis_index("mlp")
    half_count = normed.shape[0] // lax.axis_size("mlp")
    ring = lax.axis_size("y")
    shifted = [normed]
    for shift in range(1, ring):
        perm = [(i, (i + shift) % ring) for i in range(ring)]
        shifted.append(lax.ppermute(normed, "y", perm))
    group_rows = jnp.concatenate(shifted, axis=0)
    dims = (((1,), (2,)), ((), ()))
    gate = lax.dot_general(group_rows, all_w[:, 0], dims, preferred_element_type=jnp.float32)
    up_part = lax.dot_general(group_rows, all_w[:, 1], dims, preferred_element_type=jnp.float32)
    hidden = (jax.nn.silu(gate) * up_part).astype(jnp.bfloat16)
    down_dims = (((1, 2), (0, 1)), ((), ()))
    partial = lax.dot_general(
        hidden, all_w[:, 2], down_dims, preferred_element_type=jnp.float32
    )
    halves = partial.reshape(ring, 2, half_count, partial.shape[1])
    mine = lax.dynamic_index_in_dim(halves, column, 1, keepdims=False)
    theirs = lax.dynamic_index_in_dim(halves, 1 - column, 1, keepdims=False)
    mine = mine + lax.ppermute(theirs, "mlp", [(0, 1), (1, 0)])
    mlp_half = mine[0]
    for shift in range(1, ring):
        perm = [(i, (i - shift) % ring) for i in range(ring)]
        mlp_half = mlp_half + lax.ppermute(mine[shift], "y", perm)
    base_half = lax.dynamic_slice_in_dim(mixed, column * half_count, half_count, 0)
    out_half = (base_half.astype(jnp.float32) + mlp_half).astype(jnp.bfloat16)
    other_half = lax.ppermute(out_half, "mlp", [(0, 1), (1, 0)])
    pair = jnp.stack([out_half, other_half])
    hidden_out = jnp.concatenate(
        [
            lax.dynamic_index_in_dim(pair, column, 0, keepdims=False),
            lax.dynamic_index_in_dim(pair, 1 - column, 0, keepdims=False),
        ],
        axis=0,
    )
    next_normed = rms_scale(hidden_out, gain_next)
    next_qkv = jnp.dot(next_normed, w_next, preferred_element_type=jnp.float32).astype(jnp.bfloat16)
    accepted = compact_path(reach, accept_leaf, kv_in.reshape(2, tree_len, 2 * kv_width))
    accepted_kv = accepted.reshape(2 * tree_len, 2, kv_width)
    return (hidden_out, next_qkv, accepted_kv)


def solution(mesh):
    devices = mesh.devices
    owners = devices.shape[0]
    lines = round(owners ** (1 / 3))
    sub_mesh = Mesh(
        devices.reshape(owners // (lines * lines), lines, lines, devices.shape[1]),
        ("z", "x", "y", "mlp"),
    )
    R = REQ
    placed = (
        P(R, None),
        P(R, "mlp"),
        P(R, None, "mlp"),
        P(R, None),
        P(R),
        P(R),
        P(R, None, None, "mlp"),
        P(R, None),
        P(R),
        P(R),
        P("mlp", None),
        P(),
        P(None, R + ("mlp",), None),
        P(R + ("mlp",), None),
        P(),
        P(None, "mlp"),
    )
    return jax.shard_map(
        per_device,
        mesh=sub_mesh,
        in_specs=placed,
        out_specs=(P(R, None), P(R, "mlp"), P(R, None, "mlp")),
        check_vma=False,
    )
```
